256 devices in a mesh: section: 2 (over core), ccd: 128 (over y, x, z).
Axes of the slice: x: 4, y: 4, z: 8, core: 2. Of those that a mesh axis runs over, the one named last changes fastest.
Arguments:
- raw_counts: float32 [128, 2, 64, 2048], P('ccd', 'section'), may hold values from -6 to 6
- overscan: float32 [128, 2, 64], P('ccd', 'section'), may hold values from -6 to 6
- response: float32 [128, 2, 64, 2048], P('ccd', 'section'), may hold values from 0.5 to 2
- warp_rows: int32 [16384], P('ccd'), may hold values from 0 to 16383, as said below
- kernel_poly: float32 [13, 6], replicated, may hold values from -1 to 1
- tile_owner: int32 [128, 2, 128, 1], P('ccd', 'section'), may hold values from 0 to 127; in each aligned block of 128 rows (0 to 127, 128 to 255, ..., all dimensions but the last counted through in order) at most 2 rows name the same one
- tile_weight: float32 [128, 2, 128], P('ccd', 'section'), may hold values from 0.03 to 0.3
Outputs:
- patches: float32 [2, 128, 32, 32], P('section', 'ccd')
The draws below stay inside these ranges and needn't reach their ends.
Inputs may be any that keep to these rules, and one draw needn't show every extreme that they name: `warp_rows`: row g's source lies within 64 rows of g; in every draw some row takes the row 64 below it and another the row 64 above it. `tile_owner`: among the 128 tiles of one half band at most 2 have the same owner, and in every draw some half band has exactly 2 tiles on one owner.
All inputs are finite; a program needn't handle non-finite values.
Results may differ from the reference program's by a relative error of at most 0.0052.
Values may be sent and summed in bfloat16 or wider, within the bound.
No kernel may reach another device: no remote copies, remote signals or barrier semaphores. Data moves between devices by JAX's collectives and lax.ppermute only.
A program may use at most 64 MiB of HBM per device.

```python
import math
import jax
import jax.numpy as jnp
import numpy as np
from jax import lax

COLS = 2048
ROWS = 128
TILE = 32
KW = 21
NBASIS = 13
NPOLY = 6
HALF_K = 10
RH = 64
CH = 1024
REACH = 64
TILES_HALF = 128
CAP = 2
NR = 16384
N_CCD = 128


def draw_warp_rows(key, part):
    offsets = jax.random.randint(key, (NR,), -REACH, REACH + 1, dtype=jnp.int32)
    offsets = offsets.at[ROWS].set(REACH).at[2 * ROWS - 1].set(-REACH)
    return jnp.clip(jnp.arange(NR, dtype=jnp.int32) + offsets, 0, NR - 1).astype(jnp.int32)


def level_of(rng, extent, shards, low, high):
    def one(position, shards_of):
        draws = jax.random.uniform(jax.random.fold_in(jax.random.fold_in(rng, 6), position), (shards_of,), jnp.float32, low / len(shards), high / len(shards))
        return jnp.repeat(jnp.exp(draws), extent[position] // shards_of).reshape((-1,) + (1,) * (len(extent) - position - 1))

    level = one(*shards[0])
    for cut in shards[1:]:
        level = level * one(*cut)
    return level


def routed_block(own_key, own, number, rows, amount, top, reach, skew):
    order = jax.random.permutation(own_key, amount)
    packed, usual = load_shares(amount, rows * top, reach, skew, True), load_shares(amount, rows * top, reach, skew, False)
    places = jnp.arange(amount)

    def named(lengths, rotation):
        used = int((lengths > 0).sum())
        fixed = max(1, used // 4)
        shifted = fixed + (places - fixed + rotation * (used - fixed)) % max(1, amount - fixed)
        return jnp.zeros((amount,), jnp.int32).at[order[jnp.where(places < fixed, places, shifted)]].set(jnp.asarray(lengths, jnp.int32))

    lengths = jnp.where(number % 4 == 0, named(packed, number // 4), named(usual, number - number // 4 - 1))
    mixed = jax.random.permutation(jax.random.fold_in(own, 3), amount)
    donor, sink = mixed[0:amount // 2 * 2:2], mixed[1:amount // 2 * 2:2]
    room = jnp.minimum(lengths[donor] - 1, reach - lengths[sink]) // 2
    room = jnp.where((donor == order[0]) | (sink == order[0]) | (lengths[sink] == 0), 0, jnp.maximum(room, 0))
    shifted = jax.random.randint(jax.random.fold_in(own, 4), (amount // 2,), 0, 1 << 20) % (room + 1)
    lengths = lengths.at[donor].add(-shifted).at[sink].add(shifted)
    labels = jnp.searchsorted(jnp.cumsum(lengths), jnp.arange(rows * top), side="right").astype(jnp.int32)
    grid = labels.reshape(top, rows).T
    grid = grid[jax.random.permutation(jax.random.fold_in(own, 1), rows)]
    rotation = jax.random.randint(jax.random.fold_in(own, 2), (rows, 1), 0, top)
    return jnp.take_along_axis(grid, (jnp.arange(top)[None, :] + rotation) % top, axis=1)


def load_shares(number_of, total, bound, lean, full):
    portions = [(1 << 20) // math.isqrt(rank ** lean) + 1 for rank in range(1, number_of + 1)]
    largest = bound if full else min(bound, max(-(-total // number_of), total * portions[0] // sum(portions)))
    least = 1 if total - largest >= number_of - 1 else 0
    holding, spare = [largest] + [least] * (number_of - 1), total - largest - least * (number_of - 1)
    while spare > 0:
        free = [i for i in range(1, number_of) if holding[i] < largest] or [i for i in range(1, number_of) if holding[i] < bound]
        pool, budget = sum([portions[i] for i in free]), spare
        for i in free:
            addition = min(bound - holding[i], max(1, budget * portions[i] // pool), spare)
            holding[i] = holding[i] + addition
            spare = spare - addition
    return np.array(holding)


def normal_values(rng, extent, scale, bound, shards=(), kind=jnp.bfloat16):
    values = jax.random.normal(rng, extent, jnp.float32) * scale
    if len(shards) > 0:
        values = level_of(rng, extent, shards, -0.22, 0.18) * values
    return jnp.clip(values, min=-bound, max=bound).astype(kind)


def setup_inputs(seed: int = 0) -> dict:
    key_of = jax.random.split(jax.random.key(seed), 8)
    raw_counts = normal_values(key_of[0], (N_CCD, 2, RH, COLS), 1.0, 6.0, ((0, 128), (1, 2)), jnp.float32)
    overscan = normal_values(key_of[1], (N_CCD, 2, RH), 1.0, 6.0, ((0, 128), (1, 2)), jnp.float32)
    response = jnp.clip(jnp.exp(math.log(2.0) - 1.3862944 * jax.random.uniform(key_of[2], (N_CCD, 2, RH, COLS), jnp.float32) ** level_of(key_of[2], (N_CCD, 2, RH, COLS), ((0, 128), (1, 2)), -0.2, 0.2)), 0.5, 2.0)
    warp_rows = draw_warp_rows(jax.random.fold_in(key_of[7], 71), 0)
    kernel_poly = normal_values(key_of[4], (NBASIS, NPOLY), 0.2, 1.0, (), jnp.float32)
    tile_owner_keys = jax.random.split(jax.random.fold_in(key_of[5], 1), N_CCD * 2 * TILES_HALF // TILES_HALF)
    tile_owner_turns = jax.random.permutation(jax.random.fold_in(key_of[5], 3), N_CCD * 2 * TILES_HALF // TILES_HALF)
    tile_owner = jax.vmap(lambda own, number: routed_block(jax.random.fold_in(key_of[5], 2), own, number, TILES_HALF, N_CCD, 1, CAP, 2))(tile_owner_keys, tile_owner_turns).reshape((N_CCD, 2, TILES_HALF, 1))
    tile_weight = jnp.clip(jnp.exp(math.log(0.3) - 2.3025852 * jax.random.uniform(key_of[6], (N_CCD, 2, TILES_HALF), jnp.float32) ** level_of(key_of[6], (N_CCD, 2, TILES_HALF), ((0, 128), (1, 2)), -0.2, 0.2)), 0.03, 0.3)
    return {"raw_counts": raw_counts, "overscan": overscan, "response": response, "warp_rows": warp_rows, "kernel_poly": kernel_poly, "tile_owner": tile_owner, "tile_weight": tile_weight}


basis_sigma = (0.75, 0.75, 0.75, 0.75, 0.75, 0.75, 1.5, 1.5, 1.5, 1.5, 3.0, 3.0, 3.0)
column_power = (0, 1, 0, 2, 1, 0, 0, 1, 0, 1, 0, 1, 0)
row_power = (0, 0, 1, 0, 1, 2, 0, 0, 1, 1, 0, 0, 1)

def basis_taps(powers):
    offsets = jnp.arange(KW).astype(jnp.float32) - HALF_K
    sigma_col = jnp.array(basis_sigma, dtype=jnp.float32)[:, None]
    power_col = jnp.array(powers, dtype=jnp.int32)[:, None]
    spread = offsets[None, :]
    envelope = jnp.exp(-(spread * spread) / (2.0 * sigma_col * sigma_col))
    factor = jnp.where(power_col == 0, 1.0, jnp.where(power_col == 1, spread, spread * spread))
    shaped = envelope * factor
    scale = jnp.sqrt(lax.optimization_barrier(jnp.sum(shaped * shaped, axis=1, keepdims=True)))
    return (shaped / scale).astype(jnp.bfloat16)

def coefficients(terms, row_coord, col_coord):
    return terms[0] + terms[1] * row_coord + terms[2] * col_coord + terms[3] * row_coord * row_coord + terms[4] * row_coord * col_coord + terms[5] * col_coord * col_coord

def reference(raw_counts, overscan, response, warp_rows, kernel_poly, tile_owner, tile_weight):
    calibrated = ((raw_counts - overscan[..., None]) * response).astype(jnp.bfloat16)
    image = calibrated.reshape(NR, COLS)
    warped = jnp.take(image, warp_rows, axis=0)
    padded = jnp.pad(warped, HALF_K)
    col_taps = basis_taps(column_power).astype(jnp.float32)[:, None, None, :]
    row_taps = basis_taps(row_power).astype(jnp.float32)[:, None, :, None]
    terms = tuple((kernel_poly[:, term_index][:, None, None] for term_index in range(NPOLY)))
    row_tiles = ROWS // TILE

    def one_piece(totals, piece_index):
        band_index = piece_index // 2
        half_index = piece_index % 2
        window = lax.dynamic_slice(padded, ((band_index * ROWS).astype(jnp.int32), (half_index * CH).astype(jnp.int32)), (ROWS + 2 * HALF_K, CH + 2 * HALF_K)).astype(jnp.float32)
        columns = lax.conv_general_dilated(window[None, None], col_taps, (1, 1), 'VALID', precision=lax.Precision.HIGHEST)
        columns = lax.optimization_barrier(columns.astype(jnp.bfloat16)).astype(jnp.float32)
        vertical = lax.conv_general_dilated(columns, row_taps, (1, 1), 'VALID', feature_group_count=NBASIS, precision=lax.Precision.HIGHEST)[0]
        row_pos = (band_index * ROWS + jnp.arange(ROWS)).astype(jnp.float32)
        col_pos = (half_index * CH + jnp.arange(CH)).astype(jnp.float32)
        row_coord = (2.0 * (row_pos + 0.5) / NR - 1.0)[None, :, None]
        col_coord = (2.0 * (col_pos + 0.5) / COLS - 1.0)[None, None, :]
        coefficient = coefficients(terms, row_coord, col_coord)
        matched = lax.optimization_barrier(jnp.sum(coefficient * vertical, axis=0))
        tile_stack = matched.reshape(row_tiles, TILE, CH // TILE, TILE).transpose(2, 0, 1, 3).reshape(-1, TILE * TILE)
        owners = tile_owner[band_index, half_index, :, 0]
        weights = tile_weight[band_index, half_index]
        selector = jnp.where(jnp.arange(N_CCD)[:, None] == owners[None, :], weights[None, :], 0.0)
        update = jnp.dot(selector, tile_stack, precision=lax.Precision.HIGHEST, preferred_element_type=jnp.float32)
        totals = totals.at[half_index].add(update)
        return (totals, None)
    start_totals = jnp.zeros((2, N_CCD, TILE * TILE), jnp.float32)
    totals, unused = lax.scan(one_piece, start_totals, jnp.arange(2 * N_CCD).astype(jnp.int32))
    return totals.reshape(2, N_CCD, TILE, TILE)
```

```python
import jax
import jax.numpy as jnp
from jax import lax
from jax.sharding import PartitionSpec as P

ROWS = 128
TILE = 32
STRIP = 128
KW = 21
NBASIS = 13
NPOLY = 6
HALF_K = 10
CH = 1024
REACH = 64


basis_sigma = (0.75, 0.75, 0.75, 0.75, 0.75, 0.75, 1.5, 1.5, 1.5, 1.5, 3.0, 3.0, 3.0)
column_power = (0, 1, 0, 2, 1, 0, 0, 1, 0, 1, 0, 1, 0)
row_power = (0, 0, 1, 0, 1, 2, 0, 0, 1, 1, 0, 0, 1)


def with_halo(array, sides, width):
    for axis, dim in sides:
        devices, length = (lax.axis_size(axis), array.shape[dim])
        up = [(i, (i + 1) % devices) for i in range(devices - 1)]
        down = [(j, i) for i, j in up]
        last = lax.slice_in_dim(array, length - width, length, axis=dim)
        leading = lax.slice_in_dim(array, 0, width, axis=dim)
        before = lax.ppermute(last, axis, up)
        after = lax.ppermute(leading, axis, down)
        array = jnp.concatenate([before, array, after], axis=dim)
    return array


def basis_taps(powers):
    offsets = jnp.arange(KW).astype(jnp.float32) - HALF_K
    sigma_col = jnp.array(basis_sigma, dtype=jnp.float32)[:, None]
    power_col = jnp.array(powers, dtype=jnp.int32)[:, None]
    spread = offsets[None, :]
    envelope = jnp.exp(-(spread * spread) / (2.0 * sigma_col * sigma_col))
    factor = jnp.where(power_col == 0, 1.0, jnp.where(power_col == 1, spread, spread * spread))
    shaped = envelope * factor
    scale = jnp.sqrt(jnp.sum(shaped * shaped, axis=1, keepdims=True))
    return (shaped / scale).astype(jnp.bfloat16)


def coefficients(terms, row_coord, col_coord):
    return (
        terms[0]
        + terms[1] * row_coord
        + terms[2] * col_coord
        + terms[3] * row_coord * row_coord
        + terms[4] * row_coord * col_coord
        + terms[5] * col_coord * col_coord
    )


def band_matrix(tap_table, inner_len):
    lead_idx = jnp.arange(inner_len + 2 * HALF_K)[:, None]
    trail_idx = jnp.arange(inner_len)[None, :]
    offset = lead_idx - trail_idx
    onehot = (offset[None] == jnp.arange(KW)[:, None, None]).astype(tap_table.dtype)
    band = jnp.einsum("kt,tai->kai", tap_table, onehot, preferred_element_type=jnp.float32)
    return band.astype(tap_table.dtype)


def shards(raw_counts, overscan, response, warp_rows, kernel_poly, tile_owner, tile_weight):
    band_count = lax.axis_size("ccd")
    halves = lax.axis_size("section")
    total_rows = ROWS * band_count
    total_cols = CH * halves
    top_row = lax.axis_index("ccd") * ROWS
    left_col = lax.axis_index("section") * CH
    band = lax.axis_index("ccd")
    half = lax.axis_index("section")
    calibrated = ((raw_counts - overscan[..., None]) * response).astype(jnp.bfloat16)[0, 0]
    wide = jnp.pad(calibrated, ((0, 0), (HALF_K, HALF_K)))
    width = CH + 2 * HALF_K
    own = lax.dynamic_slice_in_dim(wide, half * CH, width, 1)
    other = lax.dynamic_slice_in_dim(wide, (1 - half) * CH, width, 1)
    received = lax.ppermute(other, "section", [(0, 1), (1, 0)])
    band_rows = jnp.where(
        half == 0,
        jnp.concatenate([own, received], axis=0),
        jnp.concatenate([received, own], axis=0),
    )
    reach = REACH + HALF_K
    up = [(i, i + 1) for i in range(band_count - 1)]
    down = [(i + 1, i) for i in range(band_count - 1)]
    before = lax.ppermute(band_rows[ROWS - reach :], "ccd", up)
    after = lax.ppermute(band_rows[:reach], "ccd", down)
    window = jnp.concatenate([before, band_rows, after], axis=0)
    rows_before = lax.ppermute(warp_rows[ROWS - HALF_K :], "ccd", up)
    rows_after = lax.ppermute(warp_rows[:HALF_K], "ccd", down)
    sources = jnp.concatenate([rows_before, warp_rows, rows_after])
    out_rows = top_row - HALF_K + jnp.arange(ROWS + 2 * HALF_K)
    inside = (out_rows >= 0) & (out_rows < total_rows)
    warped = jnp.take(window, sources - (top_row - reach), axis=0, mode="clip")
    padded = jnp.where(inside[:, None], warped, jnp.zeros((), warped.dtype))
    col_matrix = (
        band_matrix(basis_taps(column_power), STRIP)
        .transpose(1, 0, 2)
        .reshape(STRIP + 2 * HALF_K, NBASIS * STRIP)
    )
    row_matrix = band_matrix(basis_taps(row_power), STRIP).transpose(0, 2, 1)
    row_strips = ROWS // STRIP
    terms = tuple((kernel_poly[:, term_index][None, :, None, None] for term_index in range(NPOLY)))
    row_pos = (top_row + jnp.arange(ROWS)).astype(jnp.float32)
    row_coord = (2.0 * (row_pos + 0.5) / total_rows - 1.0).reshape(row_strips, 1, STRIP, 1)

    def one_column(column_index):
        col_start = column_index * STRIP
        strip = lax.dynamic_slice_in_dim(padded, col_start, STRIP + 2 * HALF_K, 1)
        across = jnp.dot(strip, col_matrix, preferred_element_type=jnp.float32).astype(jnp.bfloat16)
        across = across.reshape(ROWS + 2 * HALF_K, NBASIS, STRIP)
        stacked = jnp.stack([across])
        vertical = jnp.einsum(
            "kra,bakc->bkrc", row_matrix, stacked, preferred_element_type=jnp.float32
        )
        col_pos = (left_col + col_start + jnp.arange(STRIP)).astype(jnp.float32)
        col_coord = (2.0 * (col_pos + 0.5) / total_cols - 1.0)[None, None, None, :]
        coefficient = coefficients(terms, row_coord, col_coord)
        return jnp.sum(coefficient * vertical, axis=1)

    matched = lax.map(one_column, jnp.arange(CH // STRIP))
    matched = matched.transpose(1, 2, 0, 3).reshape(ROWS, CH)
    tile_stack = (
        matched.reshape(ROWS // TILE, TILE, CH // TILE, TILE)
        .transpose(2, 0, 1, 3)
        .reshape(-1, TILE * TILE)
    )
    owners = tile_owner.reshape(-1)
    weights = tile_weight.reshape(-1)
    selector = jnp.where(
        jnp.arange(band_count)[:, None] == owners[None, :], weights[None, :], 0.0
    )
    outgoing = jnp.dot(
        selector, tile_stack, precision=lax.Precision.HIGHEST, preferred_element_type=jnp.float32
    )
    incoming = lax.all_to_all(outgoing, "ccd", split_axis=0, concat_axis=0, tiled=True)
    patch_sum = jnp.sum(incoming, axis=0, keepdims=True)
    return patch_sum.reshape(1, 1, TILE, TILE)


def solution(mesh):
    in_specs = (
        P("ccd", "section", None, None),
        P("ccd", "section", None),
        P("ccd", "section", None, None),
        P("ccd"),
        P(),
        P("ccd", "section", None, None),
        P("ccd", "section", None),
    )
    out_specs = P("section", "ccd", None, None)
    return jax.shard_map(shards, mesh=mesh, in_specs=in_specs, out_specs=out_specs, check_vma=False)
```

```python
import jax
import jax.numpy as jnp
from jax import lax
from jax.sharding import PartitionSpec as P
from jax.experimental import pallas as pl

ROWS = 128
TILE = 32
STRIP = 128
KW = 21
NBASIS = 13
NPOLY = 6
HALF_K = 10
CH = 1024
REACH = 64


basis_sigma = (0.75, 0.75, 0.75, 0.75, 0.75, 0.75, 1.5, 1.5, 1.5, 1.5, 3.0, 3.0, 3.0)
column_power = (0, 1, 0, 2, 1, 0, 0, 1, 0, 1, 0, 1, 0)
row_power = (0, 0, 1, 0, 1, 2, 0, 0, 1, 1, 0, 0, 1)


def with_halo(array, sides, width):
    for axis, dim in sides:
        devices, length = (lax.axis_size(axis), array.shape[dim])
        up = [(i, (i + 1) % devices) for i in range(devices - 1)]
        down = [(j, i) for i, j in up]
        last = lax.slice_in_dim(array, length - width, length, axis=dim)
        leading = lax.slice_in_dim(array, 0, width, axis=dim)
        before = lax.ppermute(last, axis, up)
        after = lax.ppermute(leading, axis, down)
        array = jnp.concatenate([before, array, after], axis=dim)
    return array


def basis_taps(powers):
    offsets = jnp.arange(KW).astype(jnp.float32) - HALF_K
    sigma_col = jnp.array(basis_sigma, dtype=jnp.float32)[:, None]
    power_col = jnp.array(powers, dtype=jnp.int32)[:, None]
    spread = offsets[None, :]
    envelope = jnp.exp(-(spread * spread) / (2.0 * sigma_col * sigma_col))
    factor = jnp.where(power_col == 0, 1.0, jnp.where(power_col == 1, spread, spread * spread))
    shaped = envelope * factor
    scale = jnp.sqrt(jnp.sum(shaped * shaped, axis=1, keepdims=True))
    return (shaped / scale).astype(jnp.bfloat16)


def coefficients(terms, row_coord, col_coord):
    return (
        terms[0]
        + terms[1] * row_coord
        + terms[2] * col_coord
        + terms[3] * row_coord * row_coord
        + terms[4] * row_coord * col_coord
        + terms[5] * col_coord * col_coord
    )


def band_matrix(tap_table, inner_len):
    lead_idx = jnp.arange(inner_len + 2 * HALF_K)[:, None]
    trail_idx = jnp.arange(inner_len)[None, :]
    offset = lead_idx - trail_idx
    onehot = (offset[None] == jnp.arange(KW)[:, None, None]).astype(tap_table.dtype)
    band = jnp.einsum("kt,tai->kai", tap_table, onehot, preferred_element_type=jnp.float32)
    return band.astype(tap_table.dtype)


def shards(raw_counts, overscan, response, warp_rows, kernel_poly, tile_owner, tile_weight):
    band_count = lax.axis_size("ccd")
    halves = lax.axis_size("section")
    total_rows = ROWS * band_count
    total_cols = CH * halves
    top_row = lax.axis_index("ccd") * ROWS
    left_col = lax.axis_index("section") * CH
    half = lax.axis_index("section")
    calibrated = ((raw_counts - overscan[..., None]) * response).astype(jnp.bfloat16)[0, 0]
    wide = jnp.pad(calibrated, ((0, 0), (HALF_K, HALF_K)))
    width = CH + 2 * HALF_K
    own = lax.dynamic_slice_in_dim(wide, half * CH, width, 1)
    other = lax.dynamic_slice_in_dim(wide, (1 - half) * CH, width, 1)
    received = lax.ppermute(other, "section", [(0, 1), (1, 0)])
    band_rows = jnp.where(
        half == 0,
        jnp.concatenate([own, received], axis=0),
        jnp.concatenate([received, own], axis=0),
    )
    reach = REACH + HALF_K
    up = [(i, i + 1) for i in range(band_count - 1)]
    down = [(i + 1, i) for i in range(band_count - 1)]
    before = lax.ppermute(band_rows[ROWS - reach :], "ccd", up)
    after = lax.ppermute(band_rows[:reach], "ccd", down)
    window = jnp.concatenate([before, band_rows, after], axis=0)
    rows_before = lax.ppermute(warp_rows[ROWS - HALF_K :], "ccd", up)
    rows_after = lax.ppermute(warp_rows[:HALF_K], "ccd", down)
    sources = jnp.concatenate([rows_before, warp_rows, rows_after])
    out_rows = top_row - HALF_K + jnp.arange(ROWS + 2 * HALF_K)
    inside = (out_rows >= 0) & (out_rows < total_rows)
    warped = jnp.take(window, sources - (top_row - reach), axis=0, mode="clip")
    padded = jnp.where(inside[:, None], warped, jnp.zeros((), warped.dtype))
    strips = CH // STRIP
    span = 2 * STRIP
    lead = ROWS + 2 * HALF_K
    lead_pad = -(-lead // 16) * 16
    image = jnp.pad(padded, ((0, lead_pad - lead), (0, strips * STRIP + STRIP - padded.shape[1])))
    col_band = band_matrix(basis_taps(column_power), STRIP)
    col_band = jnp.pad(col_band, ((0, 0), (0, span - col_band.shape[1]), (0, 0)))
    col_matrix = col_band.transpose(1, 0, 2).reshape(span, NBASIS * STRIP)
    row_matrix = band_matrix(basis_taps(row_power), ROWS).transpose(0, 2, 1)
    row_matrix = jnp.pad(row_matrix, ((0, 0), (0, 0), (0, lead_pad - lead)))
    row_pos = (top_row + jnp.arange(ROWS)).astype(jnp.float32)
    row_coord = (2.0 * (row_pos + 0.5) / total_rows - 1.0)[None, :, None]
    col_pos = (left_col + jnp.arange(CH)).astype(jnp.float32)
    col_coord = (2.0 * (col_pos + 0.5) / total_cols - 1.0).reshape(strips, 1, STRIP)
    poly = kernel_poly[:, :, None, None]
    row_part = poly[:, 0] + poly[:, 1] * row_coord + poly[:, 3] * row_coord * row_coord
    slope_part = poly[:, 2] + poly[:, 4] * row_coord
    square_part = poly[:, 5]

    def match_kernel(img_ref, colm_ref, rowm_ref, a_ref, b_ref, c_ref, v_ref, out_ref):
        i = pl.program_id(0)
        offset = pl.multiple_of(i * STRIP, STRIP)
        strip = img_ref[:, pl.ds(offset, span)]
        across = jnp.dot(strip, colm_ref[...], preferred_element_type=jnp.float32)
        across = across.astype(jnp.bfloat16)
        v = v_ref[0]
        acc = jnp.zeros((ROWS, STRIP), jnp.float32)
        for k in range(NBASIS):
            vert = jnp.dot(
                rowm_ref[k], across[:, k * STRIP : (k + 1) * STRIP],
                preferred_element_type=jnp.float32,
            )
            coef = a_ref[k] + v * (b_ref[k] + c_ref[k] * v)
            acc = acc + coef * vert
        out_ref[...] = acc

    full = lambda shape: pl.BlockSpec(shape, lambda i: (0,) * len(shape))
    matched = pl.pallas_call(
        match_kernel,
        grid=(strips,),
        in_specs=[
            full(image.shape),
            full(col_matrix.shape),
            full(row_matrix.shape),
            full(row_part.shape),
            full(slope_part.shape),
            full(square_part.shape),
            pl.BlockSpec((1, 1, STRIP), lambda i: (i, 0, 0)),
        ],
        out_specs=pl.BlockSpec((ROWS, STRIP), lambda i: (0, i)),
        out_shape=jax.ShapeDtypeStruct((ROWS, CH), jnp.float32),
    )(image, col_matrix, row_matrix, row_part, slope_part, square_part, col_coord)
    tile_stack = (
        matched.reshape(ROWS // TILE, TILE, CH // TILE, TILE)
        .transpose(2, 0, 1, 3)
        .reshape(-1, TILE * TILE)
    )
    owners = tile_owner.reshape(-1)
    weights = tile_weight.reshape(-1)
    selector = jnp.where(
        jnp.arange(band_count)[:, None] == owners[None, :], weights[None, :], 0.0
    )
    outgoing = jnp.dot(
        selector, tile_stack, precision=lax.Precision.HIGHEST, preferred_element_type=jnp.float32
    )
    incoming = lax.all_to_all(outgoing, "ccd", split_axis=0, concat_axis=0, tiled=True)
    patch_sum = jnp.sum(incoming, axis=0, keepdims=True)
    return patch_sum.reshape(1, 1, TILE, TILE)


def solution(mesh):
    in_specs = (
        P("ccd", "section", None, None),
        P("ccd", "section", None),
        P("ccd", "section", None, None),
        P("ccd"),
        P(),
        P("ccd", "section", None, None),
        P("ccd", "section", None),
    )
    out_specs = P("section", "ccd", None, None)
    return jax.shard_map(shards, mesh=mesh, in_specs=in_specs, out_specs=out_specs, check_vma=False)
```

```python
import jax
import jax.numpy as jnp
from jax import lax
from jax.sharding import PartitionSpec as P
from jax.experimental import pallas as pl
from jax.experimental.pallas import tpu as pltpu

ROWS = 128
TILE = 32
STRIP = 128
KW = 21
NBASIS = 13
NPOLY = 6
HALF_K = 10
CH = 1024
REACH = 64


basis_sigma = (0.75, 0.75, 0.75, 0.75, 0.75, 0.75, 1.5, 1.5, 1.5, 1.5, 3.0, 3.0, 3.0)
column_power = (0, 1, 0, 2, 1, 0, 0, 1, 0, 1, 0, 1, 0)
row_power = (0, 0, 1, 0, 1, 2, 0, 0, 1, 1, 0, 0, 1)


def with_halo(array, sides, width):
    for axis, dim in sides:
        devices, length = (lax.axis_size(axis), array.shape[dim])
        up = [(i, (i + 1) % devices) for i in range(devices - 1)]
        down = [(j, i) for i, j in up]
        last = lax.slice_in_dim(array, length - width, length, axis=dim)
        leading = lax.slice_in_dim(array, 0, width, axis=dim)
        before = lax.ppermute(last, axis, up)
        after = lax.ppermute(leading, axis, down)
        array = jnp.concatenate([before, array, after], axis=dim)
    return array


def basis_taps(powers):
    offsets = jnp.arange(KW).astype(jnp.float32) - HALF_K
    sigma_col = jnp.array(basis_sigma, dtype=jnp.float32)[:, None]
    power_col = jnp.array(powers, dtype=jnp.int32)[:, None]
    spread = offsets[None, :]
    envelope = jnp.exp(-(spread * spread) / (2.0 * sigma_col * sigma_col))
    factor = jnp.where(power_col == 0, 1.0, jnp.where(power_col == 1, spread, spread * spread))
    shaped = envelope * factor
    scale = jnp.sqrt(jnp.sum(shaped * shaped, axis=1, keepdims=True))
    return (shaped / scale).astype(jnp.bfloat16)


def coefficients(terms, row_coord, col_coord):
    return (
        terms[0]
        + terms[1] * row_coord
        + terms[2] * col_coord
        + terms[3] * row_coord * row_coord
        + terms[4] * row_coord * col_coord
        + terms[5] * col_coord * col_coord
    )


def band_matrix(tap_table, inner_len):
    lead_idx = jnp.arange(inner_len + 2 * HALF_K)[:, None]
    trail_idx = jnp.arange(inner_len)[None, :]
    offset = lead_idx - trail_idx
    onehot = (offset[None] == jnp.arange(KW)[:, None, None]).astype(tap_table.dtype)
    band = jnp.einsum("kt,tai->kai", tap_table, onehot, preferred_element_type=jnp.float32)
    return band.astype(tap_table.dtype)


def shards(raw_counts, overscan, response, warp_rows, kernel_poly, tile_owner, tile_weight):
    band_count = lax.axis_size("ccd")
    halves = lax.axis_size("section")
    total_rows = ROWS * band_count
    total_cols = CH * halves
    top_row = lax.axis_index("ccd") * ROWS
    left_col = lax.axis_index("section") * CH
    half = lax.axis_index("section")
    calibrated = ((raw_counts - overscan[..., None]) * response).astype(jnp.bfloat16)[0, 0]
    wide = jnp.pad(calibrated, ((0, 0), (HALF_K, HALF_K)))
    width = CH + 2 * HALF_K
    own = lax.dynamic_slice_in_dim(wide, half * CH, width, 1)
    other = lax.dynamic_slice_in_dim(wide, (1 - half) * CH, width, 1)
    received = lax.ppermute(other, "section", [(0, 1), (1, 0)])
    band_rows = jnp.where(
        half == 0,
        jnp.concatenate([own, received], axis=0),
        jnp.concatenate([received, own], axis=0),
    )
    reach = REACH + HALF_K
    up = [(i, i + 1) for i in range(band_count - 1)]
    down = [(i + 1, i) for i in range(band_count - 1)]
    before = lax.ppermute(band_rows[ROWS - reach :], "ccd", up)
    after = lax.ppermute(band_rows[:reach], "ccd", down)
    window = jnp.concatenate([before, band_rows, after], axis=0)
    rows_before = lax.ppermute(warp_rows[ROWS - HALF_K :], "ccd", up)
    rows_after = lax.ppermute(warp_rows[:HALF_K], "ccd", down)
    sources = jnp.concatenate([rows_before, warp_rows, rows_after])
    out_rows = top_row - HALF_K + jnp.arange(ROWS + 2 * HALF_K)
    inside = (out_rows >= 0) & (out_rows < total_rows)
    warped = jnp.take(window, sources - (top_row - reach), axis=0, mode="clip")
    padded = jnp.where(inside[:, None], warped, jnp.zeros((), warped.dtype))
    strips = CH // STRIP
    span = 2 * STRIP
    lead = ROWS + 2 * HALF_K
    lead_pad = -(-lead // 16) * 16
    image = jnp.pad(padded, ((0, lead_pad - lead), (0, strips * STRIP + STRIP - padded.shape[1])))
    col_band = band_matrix(basis_taps(column_power), STRIP)
    col_band = jnp.pad(col_band, ((0, 0), (0, span - col_band.shape[1]), (0, 0)))
    col_matrix = col_band.transpose(1, 0, 2).reshape(span, NBASIS * STRIP)
    row_matrix = band_matrix(basis_taps(row_power), ROWS).transpose(0, 2, 1)
    row_matrix = jnp.pad(row_matrix, ((0, 0), (0, 0), (0, lead_pad - lead)))
    row_pos = (top_row + jnp.arange(ROWS)).astype(jnp.float32)
    row_coord = (2.0 * (row_pos + 0.5) / total_rows - 1.0)[None, :, None]
    col_pos = (left_col + jnp.arange(CH)).astype(jnp.float32)
    col_coord = (2.0 * (col_pos + 0.5) / total_cols - 1.0).reshape(strips, 1, STRIP)
    poly = kernel_poly[:, :, None, None]
    row_part = poly[:, 0] + poly[:, 1] * row_coord + poly[:, 3] * row_coord * row_coord
    slope_part = poly[:, 2] + poly[:, 4] * row_coord
    square_part = poly[:, 5]

    owners = tile_owner.reshape(-1)
    weights = tile_weight.reshape(-1)
    selector = jnp.where(
        jnp.arange(band_count)[:, None] == owners[None, :], weights[None, :], 0.0
    )
    groups = TILE * TILE // STRIP
    tiles = selector.shape[1]
    row_tiles = ROWS // TILE
    per_lane = STRIP // TILE

    def match_kernel(img_ref, colm_ref, rowm_ref, a_ref, b_ref, c_ref, v_ref, s_ref,
                     out_ref, acc_ref, pack_ref):
        i = pl.program_id(0)
        offset = pl.multiple_of(i * STRIP, STRIP)
        strip = img_ref[:, pl.ds(offset, span)]
        across = jnp.dot(strip, colm_ref[...], preferred_element_type=jnp.float32)
        across = across.astype(jnp.bfloat16)
        v = v_ref[0]
        acc = jnp.zeros((ROWS, STRIP), jnp.float32)
        for k in range(NBASIS):
            vert = jnp.dot(
                rowm_ref[k], across[:, k * STRIP : (k + 1) * STRIP],
                preferred_element_type=jnp.float32,
            )
            coef = a_ref[k] + v * (b_ref[k] + c_ref[k] * v)
            acc = acc + coef * vert
        acc_ref[...] = acc
        lane_group = lax.broadcasted_iota(jnp.int32, (groups, STRIP), 1) // TILE
        for rb in range(row_tiles):
            picked = [
                acc_ref[pl.ds(rb * TILE + g, groups, stride=per_lane), :] for g in range(per_lane)
            ]
            for cbl in range(per_lane):
                packed = jnp.zeros((groups, STRIP), jnp.float32)
                for g in range(per_lane):
                    shift = ((g - cbl) % per_lane) * TILE
                    rolled = pltpu.roll(picked[g], shift, 1) if shift else picked[g]
                    packed = jnp.where(lane_group == g, rolled, packed)
                j = (i * per_lane + cbl) * row_tiles + rb
                pack_ref[pl.ds(pl.multiple_of(j * groups, groups), groups), :] = packed

        @pl.when(i == strips - 1)
        def _():
            sel = s_ref[...]
            for q in range(groups):
                part = pack_ref[pl.ds(q, tiles, stride=groups), :]
                out_ref[pl.ds(q, band_count, stride=groups), :] = jnp.dot(
                    sel, part, precision=lax.Precision.HIGHEST,
                    preferred_element_type=jnp.float32,
                )

    full = lambda shape: pl.BlockSpec(shape, lambda i: (0,) * len(shape))
    outgoing = pl.pallas_call(
        match_kernel,
        grid=(strips,),
        in_specs=[
            full(image.shape),
            full(col_matrix.shape),
            full(row_matrix.shape),
            full(row_part.shape),
            full(slope_part.shape),
            full(square_part.shape),
            pl.BlockSpec((1, 1, STRIP), lambda i: (i, 0, 0)),
            full(selector.shape),
        ],
        out_specs=full((band_count * groups, STRIP)),
        out_shape=jax.ShapeDtypeStruct((band_count * groups, STRIP), jnp.float32),
        scratch_shapes=[
            pltpu.VMEM((ROWS, STRIP), jnp.float32),
            pltpu.VMEM((tiles * groups, STRIP), jnp.float32),
        ],
    )(image, col_matrix, row_matrix, row_part, slope_part, square_part, col_coord, selector)
    outgoing = outgoing.reshape(band_count, groups, STRIP)
    incoming = lax.all_to_all(outgoing, "ccd", split_axis=0, concat_axis=0, tiled=True)
    patch_sum = jnp.sum(incoming, axis=0, keepdims=True)
    return patch_sum.reshape(1, 1, TILE, TILE)


def solution(mesh):
    in_specs = (
        P("ccd", "section", None, None),
        P("ccd", "section", None),
        P("ccd", "section", None, None),
        P("ccd"),
        P(),
        P("ccd", "section", None, None),
        P("ccd", "section", None),
    )
    out_specs = P("section", "ccd", None, None)
    return jax.shard_map(shards, mesh=mesh, in_specs=in_specs, out_specs=out_specs, check_vma=False)
```

```python
import jax
import jax.numpy as jnp
from jax import lax
from jax.sharding import PartitionSpec as P
from jax.experimental import pallas as pl
from jax.experimental.pallas import tpu as pltpu

ROWS = 128
TILE = 32
STRIP = 128
KW = 21
NBASIS = 13
NPOLY = 6
HALF_K = 10
CH = 1024
REACH = 64


basis_sigma = (0.75, 0.75, 0.75, 0.75, 0.75, 0.75, 1.5, 1.5, 1.5, 1.5, 3.0, 3.0, 3.0)
column_power = (0, 1, 0, 2, 1, 0, 0, 1, 0, 1, 0, 1, 0)
row_power = (0, 0, 1, 0, 1, 2, 0, 0, 1, 1, 0, 0, 1)


def with_halo(array, sides, width):
    for axis, dim in sides:
        devices, length = (lax.axis_size(axis), array.shape[dim])
        up = [(i, (i + 1) % devices) for i in range(devices - 1)]
        down = [(j, i) for i, j in up]
        last = lax.slice_in_dim(array, length - width, length, axis=dim)
        leading = lax.slice_in_dim(array, 0, width, axis=dim)
        before = lax.ppermute(last, axis, up)
        after = lax.ppermute(leading, axis, down)
        array = jnp.concatenate([before, array, after], axis=dim)
    return array


def basis_taps(powers):
    offsets = jnp.arange(KW).astype(jnp.float32) - HALF_K
    sigma_col = jnp.array(basis_sigma, dtype=jnp.float32)[:, None]
    power_col = jnp.array(powers, dtype=jnp.int32)[:, None]
    spread = offsets[None, :]
    envelope = jnp.exp(-(spread * spread) / (2.0 * sigma_col * sigma_col))
    factor = jnp.where(power_col == 0, 1.0, jnp.where(power_col == 1, spread, spread * spread))
    shaped = envelope * factor
    scale = jnp.sqrt(jnp.sum(shaped * shaped, axis=1, keepdims=True))
    return (shaped / scale).astype(jnp.bfloat16)


def coefficients(terms, row_coord, col_coord):
    return (
        terms[0]
        + terms[1] * row_coord
        + terms[2] * col_coord
        + terms[3] * row_coord * row_coord
        + terms[4] * row_coord * col_coord
        + terms[5] * col_coord * col_coord
    )


def band_matrix(tap_table, inner_len):
    lead_idx = jnp.arange(inner_len + 2 * HALF_K)[:, None]
    trail_idx = jnp.arange(inner_len)[None, :]
    offset = lead_idx - trail_idx
    onehot = (offset[None] == jnp.arange(KW)[:, None, None]).astype(tap_table.dtype)
    band = jnp.einsum("kt,tai->kai", tap_table, onehot, preferred_element_type=jnp.float32)
    return band.astype(tap_table.dtype)


def shards(raw_counts, overscan, response, warp_rows, kernel_poly, tile_owner, tile_weight):
    band_count = lax.axis_size("ccd")
    halves = lax.axis_size("section")
    total_rows = ROWS * band_count
    total_cols = CH * halves
    top_row = lax.axis_index("ccd") * ROWS
    left_col = lax.axis_index("section") * CH
    half = lax.axis_index("section")
    strips = CH // STRIP
    wide_cols = strips * STRIP + STRIP
    rh = raw_counts.shape[2]
    calibrated = ((raw_counts - overscan[..., None]) * response).astype(jnp.bfloat16)[0, 0]
    shifts = (warp_rows - (top_row + jnp.arange(ROWS))).astype(jnp.bfloat16)
    my_shifts = lax.dynamic_slice_in_dim(shifts, half * rh, rh)[:, None]
    wide = jnp.pad(calibrated, ((0, 0), (HALF_K, HALF_K)))
    width = CH + 2 * HALF_K
    filler = jnp.zeros((rh, wide_cols - width - 1), jnp.bfloat16)

    def slab(col_start):
        cols = lax.dynamic_slice_in_dim(wide, col_start, width, 1)
        return jnp.concatenate([cols, my_shifts, filler], axis=1)

    own = slab(half * CH)
    other = slab((1 - half) * CH)
    nb = band_count
    dev = lambda s, b: s * nb + b
    axes = ("section", "ccd")
    swap = [(dev(s, b), dev(1 - s, b)) for s in range(2) for b in range(nb)]
    cross = [(dev(1, b), dev(0, b + 1)) for b in range(nb - 1)] + [
        (dev(0, b), dev(1, b - 1)) for b in range(1, nb)
    ]
    straight = [(dev(1, b), dev(1, b + 1)) for b in range(nb - 1)] + [
        (dev(0, b), dev(0, b - 1)) for b in range(1, nb)
    ]
    straight_down = [(dev(0, b), dev(0, b + 1)) for b in range(nb - 1)] + [
        (dev(1, b), dev(1, b - 1)) for b in range(1, nb)
    ]
    cross_down = [(dev(0, b), dev(1, b + 1)) for b in range(nb - 1)] + [
        (dev(1, b), dev(0, b - 1)) for b in range(1, nb)
    ]
    edge = lambda x: jnp.where(half == 0, x[rh - HALF_K :], x[:HALF_K])
    got_swap = lax.ppermute(other, axes, swap)
    got_cross = lax.ppermute(other, axes, cross)
    got_straight = lax.ppermute(own, axes, straight)
    got_edge = lax.ppermute(edge(own), axes, straight_down)
    got_edge_cross = lax.ppermute(edge(other), axes, cross_down)
    window = jnp.where(
        half == 0,
        jnp.concatenate([got_edge, got_cross, own, got_swap, got_straight, got_edge_cross], axis=0),
        jnp.concatenate([got_edge_cross, got_straight, got_swap, own, got_cross, got_edge], axis=0),
    )
    reach = REACH + HALF_K
    lead = ROWS + 2 * HALF_K
    steps = window[REACH : REACH + lead, width].astype(jnp.int32)
    picks = jnp.arange(lead) + REACH + steps
    out_rows = top_row - HALF_K + jnp.arange(lead)
    inside = (out_rows >= 0) & (out_rows < total_rows)
    warped = jnp.take(window, picks, axis=0, mode="clip")
    padded = jnp.where(inside[:, None], warped, jnp.zeros((), warped.dtype))
    span = 2 * STRIP
    lead_pad = -(-lead // 16) * 16
    image = jnp.pad(padded, ((0, lead_pad - lead), (0, 0)))
    col_band = band_matrix(basis_taps(column_power), STRIP)
    col_band = jnp.pad(col_band, ((0, 0), (0, span - col_band.shape[1]), (0, 0)))
    col_matrix = col_band.transpose(1, 0, 2).reshape(span, NBASIS * STRIP)
    row_matrix = band_matrix(basis_taps(row_power), ROWS).transpose(0, 2, 1)
    row_matrix = jnp.pad(row_matrix, ((0, 0), (0, 0), (0, lead_pad - lead)))
    row_pos = (top_row + jnp.arange(ROWS)).astype(jnp.float32)
    row_coord = (2.0 * (row_pos + 0.5) / total_rows - 1.0)[None, :, None]
    col_pos = (left_col + jnp.arange(CH)).astype(jnp.float32)
    col_coord = (2.0 * (col_pos + 0.5) / total_cols - 1.0).reshape(strips, 1, STRIP)
    poly = kernel_poly[:, :, None, None]
    row_part = poly[:, 0] + poly[:, 1] * row_coord + poly[:, 3] * row_coord * row_coord
    slope_part = poly[:, 2] + poly[:, 4] * row_coord
    square_part = poly[:, 5]

    owners = tile_owner.reshape(-1)
    weights = tile_weight.reshape(-1)
    selector = jnp.where(
        jnp.arange(band_count)[:, None] == owners[None, :], weights[None, :], 0.0
    )
    groups = TILE * TILE // STRIP
    tiles = selector.shape[1]
    row_tiles = ROWS // TILE
    per_lane = STRIP // TILE

    def match_kernel(img_ref, colm_ref, rowm_ref, a_ref, b_ref, c_ref, v_ref, s_ref,
                     out_ref, acc_ref, pack_ref):
        i = pl.program_id(0)
        offset = pl.multiple_of(i * STRIP, STRIP)
        strip = img_ref[:, pl.ds(offset, span)]
        across = jnp.dot(strip, colm_ref[...], preferred_element_type=jnp.float32)
        across = across.astype(jnp.bfloat16)
        v = v_ref[0]
        acc = jnp.zeros((ROWS, STRIP), jnp.float32)
        for k in range(NBASIS):
            vert = jnp.dot(
                rowm_ref[k], across[:, k * STRIP : (k + 1) * STRIP],
                preferred_element_type=jnp.float32,
            )
            coef = a_ref[k] + v * (b_ref[k] + c_ref[k] * v)
            acc = acc + coef * vert
        acc_ref[...] = acc
        lane_group = lax.broadcasted_iota(jnp.int32, (groups, STRIP), 1) // TILE
        for rb in range(row_tiles):
            picked = [
                acc_ref[pl.ds(rb * TILE + g, groups, stride=per_lane), :] for g in range(per_lane)
            ]
            for cbl in range(per_lane):
                packed = jnp.zeros((groups, STRIP), jnp.float32)
                for g in range(per_lane):
                    shift = ((g - cbl) % per_lane) * TILE
                    rolled = pltpu.roll(picked[g], shift, 1) if shift else picked[g]
                    packed = jnp.where(lane_group == g, rolled, packed)
                j = (i * per_lane + cbl) * row_tiles + rb
                pack_ref[pl.ds(pl.multiple_of(j * groups, groups), groups), :] = packed

        @pl.when(i == strips - 1)
        def _():
            sel = s_ref[...]
            for q in range(groups):
                part = pack_ref[pl.ds(q, tiles, stride=groups), :]
                out_ref[pl.ds(q, band_count, stride=groups), :] = jnp.dot(
                    sel, part, precision=lax.Precision.HIGHEST,
                    preferred_element_type=jnp.float32,
                )

    full = lambda shape: pl.BlockSpec(shape, lambda i: (0,) * len(shape))
    outgoing = pl.pallas_call(
        match_kernel,
        grid=(strips,),
        in_specs=[
            full(image.shape),
            full(col_matrix.shape),
            full(row_matrix.shape),
            full(row_part.shape),
            full(slope_part.shape),
            full(square_part.shape),
            pl.BlockSpec((1, 1, STRIP), lambda i: (i, 0, 0)),
            full(selector.shape),
        ],
        out_specs=full((band_count * groups, STRIP)),
        out_shape=jax.ShapeDtypeStruct((band_count * groups, STRIP), jnp.float32),
        scratch_shapes=[
            pltpu.VMEM((ROWS, STRIP), jnp.float32),
            pltpu.VMEM((tiles * groups, STRIP), jnp.float32),
        ],
    )(image, col_matrix, row_matrix, row_part, slope_part, square_part, col_coord, selector)
    outgoing = outgoing.reshape(band_count, groups, STRIP)
    incoming = lax.all_to_all(outgoing, "ccd", split_axis=0, concat_axis=0, tiled=True)
    patch_sum = jnp.sum(incoming, axis=0, keepdims=True)
    return patch_sum.reshape(1, 1, TILE, TILE)


def solution(mesh):
    in_specs = (
        P("ccd", "section", None, None),
        P("ccd", "section", None),
        P("ccd", "section", None, None),
        P("ccd"),
        P(),
        P("ccd", "section", None, None),
        P("ccd", "section", None),
    )
    out_specs = P("section", "ccd", None, None)
    return jax.shard_map(shards, mesh=mesh, in_specs=in_specs, out_specs=out_specs, check_vma=False)
```

```python
import jax
import jax.numpy as jnp
from jax import lax
from jax.sharding import PartitionSpec as P
from jax.experimental import pallas as pl
from jax.experimental.pallas import tpu as pltpu

ROWS = 128
TILE = 32
STRIP = 128
KW = 21
NBASIS = 13
NPOLY = 6
HALF_K = 10
CH = 1024
REACH = 64


basis_sigma = (0.75, 0.75, 0.75, 0.75, 0.75, 0.75, 1.5, 1.5, 1.5, 1.5, 3.0, 3.0, 3.0)
column_power = (0, 1, 0, 2, 1, 0, 0, 1, 0, 1, 0, 1, 0)
row_power = (0, 0, 1, 0, 1, 2, 0, 0, 1, 1, 0, 0, 1)


def with_halo(array, sides, width):
    for axis, dim in sides:
        devices, length = (lax.axis_size(axis), array.shape[dim])
        up = [(i, (i + 1) % devices) for i in range(devices - 1)]
        down = [(j, i) for i, j in up]
        last = lax.slice_in_dim(array, length - width, length, axis=dim)
        leading = lax.slice_in_dim(array, 0, width, axis=dim)
        before = lax.ppermute(last, axis, up)
        after = lax.ppermute(leading, axis, down)
        array = jnp.concatenate([before, array, after], axis=dim)
    return array


def basis_taps(powers):
    offsets = jnp.arange(KW).astype(jnp.float32) - HALF_K
    sigma_col = jnp.array(basis_sigma, dtype=jnp.float32)[:, None]
    power_col = jnp.array(powers, dtype=jnp.int32)[:, None]
    spread = offsets[None, :]
    envelope = jnp.exp(-(spread * spread) / (2.0 * sigma_col * sigma_col))
    factor = jnp.where(power_col == 0, 1.0, jnp.where(power_col == 1, spread, spread * spread))
    shaped = envelope * factor
    scale = jnp.sqrt(jnp.sum(shaped * shaped, axis=1, keepdims=True))
    return (shaped / scale).astype(jnp.bfloat16)


def coefficients(terms, row_coord, col_coord):
    return (
        terms[0]
        + terms[1] * row_coord
        + terms[2] * col_coord
        + terms[3] * row_coord * row_coord
        + terms[4] * row_coord * col_coord
        + terms[5] * col_coord * col_coord
    )


def band_matrix(tap_table, inner_len):
    lead_idx = jnp.arange(inner_len + 2 * HALF_K)[:, None]
    trail_idx = jnp.arange(inner_len)[None, :]
    offset = lead_idx - trail_idx
    onehot = (offset[None] == jnp.arange(KW)[:, None, None]).astype(tap_table.dtype)
    band = jnp.einsum("kt,tai->kai", tap_table, onehot, preferred_element_type=jnp.float32)
    return band.astype(tap_table.dtype)


def shards(raw_counts, overscan, response, warp_rows, kernel_poly, tile_owner, tile_weight):
    band_count = lax.axis_size("ccd")
    halves = lax.axis_size("section")
    total_rows = ROWS * band_count
    total_cols = CH * halves
    top_row = lax.axis_index("ccd") * ROWS
    left_col = lax.axis_index("section") * CH
    half = lax.axis_index("section")
    strips = CH // STRIP
    wide_cols = strips * STRIP + STRIP
    rh = raw_counts.shape[2]
    calibrated = ((raw_counts - overscan[..., None]) * response).astype(jnp.bfloat16)[0, 0]
    shifts = (warp_rows - (top_row + jnp.arange(ROWS))).astype(jnp.bfloat16)
    my_shifts = lax.dynamic_slice_in_dim(shifts, half * rh, rh)[:, None]
    wide = jnp.pad(calibrated, ((0, 0), (HALF_K, HALF_K)))
    width = CH + 2 * HALF_K
    filler = jnp.zeros((rh, wide_cols - width - 1), jnp.bfloat16)

    def slab(col_start):
        cols = lax.dynamic_slice_in_dim(wide, col_start, width, 1)
        return jnp.concatenate([cols, my_shifts, filler], axis=1)

    own = slab(half * CH)
    other = slab((1 - half) * CH)
    nb = band_count
    dev = lambda s, b: s * nb + b
    axes = ("section", "ccd")
    swap = [(dev(s, b), dev(1 - s, b)) for s in range(2) for b in range(nb)]
    cross = [(dev(1, b), dev(0, b + 1)) for b in range(nb - 1)] + [
        (dev(0, b), dev(1, b - 1)) for b in range(1, nb)
    ]
    straight = [(dev(1, b), dev(1, b + 1)) for b in range(nb - 1)] + [
        (dev(0, b), dev(0, b - 1)) for b in range(1, nb)
    ]
    straight_down = [(dev(0, b), dev(0, b + 1)) for b in range(nb - 1)] + [
        (dev(1, b), dev(1, b - 1)) for b in range(1, nb)
    ]
    cross_down = [(dev(0, b), dev(1, b + 1)) for b in range(nb - 1)] + [
        (dev(1, b), dev(0, b - 1)) for b in range(1, nb)
    ]
    edge = lambda x: jnp.where(half == 0, x[rh - HALF_K :], x[:HALF_K])
    got_swap = lax.ppermute(other, axes, swap)
    got_cross = lax.ppermute(other, axes, cross)
    got_straight = lax.ppermute(own, axes, straight)
    got_edge = lax.ppermute(edge(own), axes, straight_down)
    got_edge_cross = lax.ppermute(edge(other), axes, cross_down)
    pick = lambda a, b: jnp.where(half == 0, a, b)
    window = jnp.concatenate(
        [
            pick(got_edge, got_edge_cross),
            pick(got_cross, got_straight),
            pick(own, got_swap),
            pick(got_swap, own),
            pick(got_straight, got_cross),
            pick(got_edge_cross, got_edge),
        ],
        axis=0,
    )
    lead = ROWS + 2 * HALF_K
    lead_pad = -(-lead // 16) * 16
    steps = window[REACH : REACH + lead, width].astype(jnp.int32)
    picks = jnp.pad(jnp.arange(lead) + REACH + steps, (0, lead_pad - lead))
    out_rows = top_row - HALF_K + jnp.arange(lead_pad)
    inside = (out_rows >= 0) & (out_rows < total_rows) & (jnp.arange(lead_pad) < lead)
    warped = jnp.take(window, picks, axis=0, mode="clip")
    image = jnp.where(inside[:, None], warped, jnp.zeros((), warped.dtype))
    span = 2 * STRIP
    col_band = band_matrix(basis_taps(column_power), STRIP)
    col_band = jnp.pad(col_band, ((0, 0), (0, span - col_band.shape[1]), (0, 0)))
    col_matrix = col_band.transpose(1, 0, 2).reshape(span, NBASIS * STRIP)
    row_matrix = band_matrix(basis_taps(row_power), ROWS).transpose(0, 2, 1)
    row_matrix = jnp.pad(row_matrix, ((0, 0), (0, 0), (0, lead_pad - lead)))
    positions = jnp.stack([top_row, left_col]).astype(jnp.int32)
    owners = tile_owner.reshape(1, -1)
    weights = tile_weight.reshape(1, -1)
    groups = TILE * TILE // STRIP
    tiles = owners.shape[1]
    row_tiles = ROWS // TILE
    per_lane = STRIP // TILE

    def match_kernel(kp_ref, pos_ref, img_ref, colm_ref, rowm_ref, own_ref, w_ref,
                     out_ref, acc_ref, pack_ref, a_ref, b_ref):
        i = pl.program_id(0)

        @pl.when(i == 0)
        def _():
            rows = lax.broadcasted_iota(jnp.int32, (ROWS, STRIP), 0) + pos_ref[0]
            u = 2.0 * (rows.astype(jnp.float32) + 0.5) / total_rows - 1.0
            for k in range(NBASIS):
                a_ref[k] = kp_ref[k, 0] + kp_ref[k, 1] * u + kp_ref[k, 3] * u * u
                b_ref[k] = kp_ref[k, 2] + kp_ref[k, 4] * u

        offset = pl.multiple_of(i * STRIP, STRIP)
        strip = img_ref[:, pl.ds(offset, span)]
        across = jnp.dot(strip, colm_ref[...], preferred_element_type=jnp.float32)
        across = across.astype(jnp.bfloat16)
        cols = lax.broadcasted_iota(jnp.int32, (1, STRIP), 1) + (pos_ref[1] + i * STRIP)
        v = 2.0 * (cols.astype(jnp.float32) + 0.5) / total_cols - 1.0
        acc = jnp.zeros((ROWS, STRIP), jnp.float32)
        for k in range(NBASIS):
            vert = jnp.dot(
                rowm_ref[k], across[:, k * STRIP : (k + 1) * STRIP],
                preferred_element_type=jnp.float32,
            )
            coef = a_ref[k] + v * (b_ref[k] + kp_ref[k, 5] * v)
            acc = acc + coef * vert
        acc_ref[...] = acc
        lane_group = lax.broadcasted_iota(jnp.int32, (groups, STRIP), 1) // TILE
        for rb in range(row_tiles):
            picked = [
                acc_ref[pl.ds(rb * TILE + g, groups, stride=per_lane), :] for g in range(per_lane)
            ]
            for cbl in range(per_lane):
                packed = jnp.zeros((groups, STRIP), jnp.float32)
                for g in range(per_lane):
                    shift = ((g - cbl) % per_lane) * TILE
                    rolled = pltpu.roll(picked[g], shift, 1) if shift else picked[g]
                    packed = jnp.where(lane_group == g, rolled, packed)
                j = (i * per_lane + cbl) * row_tiles + rb
                pack_ref[pl.ds(pl.multiple_of(j * groups, groups), groups), :] = packed

        @pl.when(i == strips - 1)
        def _():
            owner_ids = lax.broadcasted_iota(jnp.int32, (band_count, tiles), 0)
            sel = jnp.where(owner_ids == own_ref[...], w_ref[...], 0.0)
            for q in range(groups):
                part = pack_ref[pl.ds(q, tiles, stride=groups), :]
                out_ref[pl.ds(q, band_count, stride=groups), :] = jnp.dot(
                    sel, part, precision=lax.Precision.HIGHEST,
                    preferred_element_type=jnp.float32,
                )

    full = lambda shape: pl.BlockSpec(shape, lambda i: (0,) * len(shape))
    outgoing = pl.pallas_call(
        match_kernel,
        grid=(strips,),
        in_specs=[
            pl.BlockSpec(memory_space=pltpu.SMEM),
            pl.BlockSpec(memory_space=pltpu.SMEM),
            full(image.shape),
            full(col_matrix.shape),
            full(row_matrix.shape),
            full(owners.shape),
            full(weights.shape),
        ],
        out_specs=full((band_count * groups, STRIP)),
        out_shape=jax.ShapeDtypeStruct((band_count * groups, STRIP), jnp.float32),
        scratch_shapes=[
            pltpu.VMEM((ROWS, STRIP), jnp.float32),
            pltpu.VMEM((tiles * groups, STRIP), jnp.float32),
            pltpu.VMEM((NBASIS, ROWS, STRIP), jnp.float32),
            pltpu.VMEM((NBASIS, ROWS, STRIP), jnp.float32),
        ],
    )(kernel_poly, positions, image, col_matrix, row_matrix, owners, weights)
    outgoing = outgoing.reshape(band_count, groups, STRIP)
    incoming = lax.all_to_all(outgoing, "ccd", split_axis=0, concat_axis=0, tiled=True)
    patch_sum = jnp.sum(incoming, axis=0, keepdims=True)
    return patch_sum.reshape(1, 1, TILE, TILE)


def solution(mesh):
    in_specs = (
        P("ccd", "section", None, None),
        P("ccd", "section", None),
        P("ccd", "section", None, None),
        P("ccd"),
        P(),
        P("ccd", "section", None, None),
        P("ccd", "section", None),
    )
    out_specs = P("section", "ccd", None, None)
    return jax.shard_map(shards, mesh=mesh, in_specs=in_specs, out_specs=out_specs, check_vma=False)
```

```python
import jax
import jax.numpy as jnp
from jax import lax
from jax.sharding import PartitionSpec as P
from jax.experimental import pallas as pl
from jax.experimental.pallas import tpu as pltpu

ROWS = 128
TILE = 32
STRIP = 128
KW = 21
NBASIS = 13
NPOLY = 6
HALF_K = 10
CH = 1024
REACH = 64


basis_sigma = (0.75, 0.75, 0.75, 0.75, 0.75, 0.75, 1.5, 1.5, 1.5, 1.5, 3.0, 3.0, 3.0)
column_power = (0, 1, 0, 2, 1, 0, 0, 1, 0, 1, 0, 1, 0)
row_power = (0, 0, 1, 0, 1, 2, 0, 0, 1, 1, 0, 0, 1)


def with_halo(array, sides, width):
    for axis, dim in sides:
        devices, length = (lax.axis_size(axis), array.shape[dim])
        up = [(i, (i + 1) % devices) for i in range(devices - 1)]
        down = [(j, i) for i, j in up]
        last = lax.slice_in_dim(array, length - width, length, axis=dim)
        leading = lax.slice_in_dim(array, 0, width, axis=dim)
        before = lax.ppermute(last, axis, up)
        after = lax.ppermute(leading, axis, down)
        array = jnp.concatenate([before, array, after], axis=dim)
    return array


def basis_taps(powers):
    offsets = jnp.arange(KW).astype(jnp.float32) - HALF_K
    sigma_col = jnp.array(basis_sigma, dtype=jnp.float32)[:, None]
    power_col = jnp.array(powers, dtype=jnp.int32)[:, None]
    spread = offsets[None, :]
    envelope = jnp.exp(-(spread * spread) / (2.0 * sigma_col * sigma_col))
    factor = jnp.where(power_col == 0, 1.0, jnp.where(power_col == 1, spread, spread * spread))
    shaped = envelope * factor
    scale = jnp.sqrt(jnp.sum(shaped * shaped, axis=1, keepdims=True))
    return (shaped / scale).astype(jnp.bfloat16)


def coefficients(terms, row_coord, col_coord):
    return (
        terms[0]
        + terms[1] * row_coord
        + terms[2] * col_coord
        + terms[3] * row_coord * row_coord
        + terms[4] * row_coord * col_coord
        + terms[5] * col_coord * col_coord
    )


def band_matrix(tap_table, inner_len):
    lead_idx = jnp.arange(inner_len + 2 * HALF_K)[:, None]
    trail_idx = jnp.arange(inner_len)[None, :]
    offset = lead_idx - trail_idx
    onehot = (offset[None] == jnp.arange(KW)[:, None, None]).astype(tap_table.dtype)
    band = jnp.einsum("kt,tai->kai", tap_table, onehot, preferred_element_type=jnp.float32)
    return band.astype(tap_table.dtype)


def shards(raw_counts, overscan, response, warp_rows, kernel_poly, tile_owner, tile_weight):
    band_count = lax.axis_size("ccd")
    halves = lax.axis_size("section")
    total_rows = ROWS * band_count
    total_cols = CH * halves
    top_row = lax.axis_index("ccd") * ROWS
    left_col = lax.axis_index("section") * CH
    half = lax.axis_index("section")
    strips = CH // STRIP
    wide_cols = strips * STRIP + STRIP
    rh = raw_counts.shape[2]
    calibrated = ((raw_counts - overscan[..., None]) * response).astype(jnp.bfloat16)[0, 0]
    shifts = (warp_rows - (top_row + jnp.arange(ROWS))).astype(jnp.bfloat16)
    my_shifts = lax.dynamic_slice_in_dim(shifts, half * rh, rh)[:, None]
    wide = jnp.pad(calibrated, ((0, 0), (HALF_K, HALF_K)))
    width = CH + 2 * HALF_K
    filler = jnp.zeros((rh, wide_cols - width - 1), jnp.bfloat16)

    def slab(col_start):
        cols = lax.dynamic_slice_in_dim(wide, col_start, width, 1)
        return jnp.concatenate([cols, my_shifts, filler], axis=1)

    own = slab(half * CH)
    other = slab((1 - half) * CH)
    nb = band_count
    dev = lambda s, b: s * nb + b
    axes = ("section", "ccd")
    swap = [(dev(s, b), dev(1 - s, b)) for s in range(2) for b in range(nb)]
    cross = [(dev(1, b), dev(0, b + 1)) for b in range(nb - 1)] + [
        (dev(0, b), dev(1, b - 1)) for b in range(1, nb)
    ]
    straight = [(dev(1, b), dev(1, b + 1)) for b in range(nb - 1)] + [
        (dev(0, b), dev(0, b - 1)) for b in range(1, nb)
    ]
    straight_down = [(dev(0, b), dev(0, b + 1)) for b in range(nb - 1)] + [
        (dev(1, b), dev(1, b - 1)) for b in range(1, nb)
    ]
    cross_down = [(dev(0, b), dev(1, b + 1)) for b in range(nb - 1)] + [
        (dev(1, b), dev(0, b - 1)) for b in range(1, nb)
    ]
    edge = lambda x: jnp.where(half == 0, x[rh - HALF_K :], x[:HALF_K])
    got_swap = lax.ppermute(other, axes, swap)
    got_cross = lax.ppermute(other, axes, cross)
    got_straight = lax.ppermute(own, axes, straight)
    got_edge = lax.ppermute(edge(own), axes, straight_down)
    got_edge_cross = lax.ppermute(edge(other), axes, cross_down)
    pick = lambda a, b: jnp.where(half == 0, a, b)
    window = jnp.concatenate(
        [
            pick(got_edge, got_edge_cross),
            pick(got_cross, got_straight),
            pick(own, got_swap),
            pick(got_swap, own),
            pick(got_straight, got_cross),
            pick(got_edge_cross, got_edge),
        ],
        axis=0,
    )
    lead = ROWS + 2 * HALF_K
    lead_pad = -(-lead // 16) * 16
    steps = window[REACH : REACH + lead, width].astype(jnp.int32)
    picks = jnp.pad(jnp.arange(lead) + REACH + steps, (0, lead_pad - lead))
    out_rows = top_row - HALF_K + jnp.arange(lead_pad)
    inside = (out_rows >= 0) & (out_rows < total_rows) & (jnp.arange(lead_pad) < lead)
    warped = jnp.take(window, picks, axis=0, mode="clip")
    image = jnp.where(inside[:, None], warped, jnp.zeros((), warped.dtype))
    span = 2 * STRIP
    col_band = band_matrix(basis_taps(column_power), STRIP)
    col_band = jnp.pad(col_band, ((0, 0), (0, span - col_band.shape[1]), (0, 0)))
    col_matrix = col_band.transpose(1, 0, 2).reshape(span, NBASIS * STRIP)
    row_matrix = band_matrix(basis_taps(row_power), ROWS).transpose(0, 2, 1)
    row_matrix = jnp.pad(row_matrix, ((0, 0), (0, 0), (0, lead_pad - lead)))
    positions = jnp.stack([top_row, left_col]).astype(jnp.int32)
    owners = tile_owner.reshape(1, -1)
    weights = tile_weight.reshape(1, -1)
    groups = TILE * TILE // STRIP
    tiles = owners.shape[1]
    row_tiles = ROWS // TILE
    per_lane = STRIP // TILE

    def match_kernel(kp_ref, pos_ref, img_ref, colm_ref, rowm_ref, own_ref, w_ref,
                     out_ref, acc_ref, pack_ref, a_ref, b_ref):
        i = pl.program_id(0)

        @pl.when(i == 0)
        def _():
            rows = lax.broadcasted_iota(jnp.int32, (ROWS, STRIP), 0) + pos_ref[0]
            u = 2.0 * (rows.astype(jnp.float32) + 0.5) / total_rows - 1.0
            for k in range(NBASIS):
                a_ref[k] = kp_ref[k, 0] + kp_ref[k, 1] * u + kp_ref[k, 3] * u * u
                b_ref[k] = kp_ref[k, 2] + kp_ref[k, 4] * u

        offset = pl.multiple_of(i * STRIP, STRIP)
        strip = img_ref[:, pl.ds(offset, span)]
        across = jnp.dot(strip, colm_ref[...], preferred_element_type=jnp.float32)
        across = across.astype(jnp.bfloat16)
        cols = lax.broadcasted_iota(jnp.int32, (1, STRIP), 1) + (pos_ref[1] + i * STRIP)
        v = 2.0 * (cols.astype(jnp.float32) + 0.5) / total_cols - 1.0
        acc = jnp.zeros((ROWS, STRIP), jnp.float32)
        for k in range(NBASIS):
            vert = jnp.dot(
                rowm_ref[k], across[:, k * STRIP : (k + 1) * STRIP],
                preferred_element_type=jnp.float32,
            )
            coef = a_ref[k] + v * (b_ref[k] + kp_ref[k, 5] * v)
            acc = acc + coef * vert
        acc_ref[...] = acc
        lane_group = lax.broadcasted_iota(jnp.int32, (groups, STRIP), 1) // TILE
        for rb in range(row_tiles):
            picked = [
                acc_ref[pl.ds(rb * TILE + g, groups, stride=per_lane), :] for g in range(per_lane)
            ]
            for cbl in range(per_lane):
                packed = jnp.zeros((groups, STRIP), jnp.float32)
                for g in range(per_lane):
                    shift = ((g - cbl) % per_lane) * TILE
                    rolled = pltpu.roll(picked[g], shift, 1) if shift else picked[g]
                    packed = jnp.where(lane_group == g, rolled, packed)
                j = (i * per_lane + cbl) * row_tiles + rb
                pack_ref[pl.ds(pl.multiple_of(j * groups, groups), groups), :] = packed

        @pl.when(i == strips - 1)
        def _():
            owner_ids = lax.broadcasted_iota(jnp.int32, (band_count, tiles), 0)
            sel = jnp.where(owner_ids == own_ref[...], w_ref[...], 0.0)
            for q in range(groups):
                part = pack_ref[pl.ds(q, tiles, stride=groups), :]
                out_ref[pl.ds(q, band_count, stride=groups), :] = jnp.dot(
                    sel, part, precision=lax.Precision.HIGHEST,
                    preferred_element_type=jnp.float32,
                )

    full = lambda shape: pl.BlockSpec(shape, lambda i: (0,) * len(shape))
    outgoing = pl.pallas_call(
        match_kernel,
        grid=(strips,),
        in_specs=[
            pl.BlockSpec(memory_space=pltpu.SMEM),
            pl.BlockSpec(memory_space=pltpu.SMEM),
            full(image.shape),
            full(col_matrix.shape),
            full(row_matrix.shape),
            full(owners.shape),
            full(weights.shape),
        ],
        out_specs=full((band_count * groups, STRIP)),
        out_shape=jax.ShapeDtypeStruct((band_count * groups, STRIP), jnp.float32),
        scratch_shapes=[
            pltpu.VMEM((ROWS, STRIP), jnp.float32),
            pltpu.VMEM((tiles * groups, STRIP), jnp.float32),
            pltpu.VMEM((NBASIS, ROWS, STRIP), jnp.float32),
            pltpu.VMEM((NBASIS, ROWS, STRIP), jnp.float32),
        ],
    )(kernel_poly, positions, image, col_matrix, row_matrix, owners, weights)
    outgoing = outgoing.reshape(band_count, groups, STRIP)
    outgoing = outgoing.astype(jnp.bfloat16)
    incoming = lax.all_to_all(outgoing, "ccd", split_axis=0, concat_axis=0, tiled=True)
    patch_sum = jnp.sum(incoming.astype(jnp.float32), axis=0, keepdims=True)
    return patch_sum.reshape(1, 1, TILE, TILE)


def solution(mesh):
    in_specs = (
        P("ccd", "section", None, None),
        P("ccd", "section", None),
        P("ccd", "section", None, None),
        P("ccd"),
        P(),
        P("ccd", "section", None, None),
        P("ccd", "section", None),
    )
    out_specs = P("section", "ccd", None, None)
    return jax.shard_map(shards, mesh=mesh, in_specs=in_specs, out_specs=out_specs, check_vma=False)
```

```python
import jax
import jax.numpy as jnp
from jax import lax
from jax.sharding import PartitionSpec as P
from jax.experimental import pallas as pl
from jax.experimental.pallas import tpu as pltpu

ROWS = 128
TILE = 32
STRIP = 128
KW = 21
NBASIS = 13
NPOLY = 6
HALF_K = 10
CH = 1024
REACH = 64


basis_sigma = (0.75, 0.75, 0.75, 0.75, 0.75, 0.75, 1.5, 1.5, 1.5, 1.5, 3.0, 3.0, 3.0)
column_power = (0, 1, 0, 2, 1, 0, 0, 1, 0, 1, 0, 1, 0)
row_power = (0, 0, 1, 0, 1, 2, 0, 0, 1, 1, 0, 0, 1)


def with_halo(array, sides, width):
    for axis, dim in sides:
        devices, length = (lax.axis_size(axis), array.shape[dim])
        up = [(i, (i + 1) % devices) for i in range(devices - 1)]
        down = [(j, i) for i, j in up]
        last = lax.slice_in_dim(array, length - width, length, axis=dim)
        leading = lax.slice_in_dim(array, 0, width, axis=dim)
        before = lax.ppermute(last, axis, up)
        after = lax.ppermute(leading, axis, down)
        array = jnp.concatenate([before, array, after], axis=dim)
    return array


def basis_taps(powers):
    offsets = jnp.arange(KW).astype(jnp.float32) - HALF_K
    sigma_col = jnp.array(basis_sigma, dtype=jnp.float32)[:, None]
    power_col = jnp.array(powers, dtype=jnp.int32)[:, None]
    spread = offsets[None, :]
    envelope = jnp.exp(-(spread * spread) / (2.0 * sigma_col * sigma_col))
    factor = jnp.where(power_col == 0, 1.0, jnp.where(power_col == 1, spread, spread * spread))
    shaped = envelope * factor
    scale = jnp.sqrt(jnp.sum(shaped * shaped, axis=1, keepdims=True))
    return (shaped / scale).astype(jnp.bfloat16)


def coefficients(terms, row_coord, col_coord):
    return (
        terms[0]
        + terms[1] * row_coord
        + terms[2] * col_coord
        + terms[3] * row_coord * row_coord
        + terms[4] * row_coord * col_coord
        + terms[5] * col_coord * col_coord
    )


def band_matrix(tap_table, inner_len):
    lead_idx = jnp.arange(inner_len + 2 * HALF_K)[:, None]
    trail_idx = jnp.arange(inner_len)[None, :]
    offset = lead_idx - trail_idx
    onehot = (offset[None] == jnp.arange(KW)[:, None, None]).astype(tap_table.dtype)
    band = jnp.einsum("kt,tai->kai", tap_table, onehot, preferred_element_type=jnp.float32)
    return band.astype(tap_table.dtype)


def shards(raw_counts, overscan, response, warp_rows, kernel_poly, tile_owner, tile_weight):
    band_count = lax.axis_size("ccd")
    halves = lax.axis_size("section")
    total_rows = ROWS * band_count
    total_cols = CH * halves
    top_row = lax.axis_index("ccd") * ROWS
    left_col = lax.axis_index("section") * CH
    half = lax.axis_index("section")
    strips = CH // STRIP
    wide_cols = strips * STRIP + STRIP
    rh = raw_counts.shape[2]
    calibrated = ((raw_counts - overscan[..., None]) * response).astype(jnp.bfloat16)[0, 0]
    shifts = (warp_rows - (top_row + jnp.arange(ROWS))).astype(jnp.bfloat16)
    my_shifts = lax.dynamic_slice_in_dim(shifts, half * rh, rh)[:, None]
    wide = jnp.pad(calibrated, ((0, 0), (HALF_K, HALF_K)))
    width = CH + 2 * HALF_K
    filler = jnp.zeros((rh, wide_cols - width - 1), jnp.bfloat16)

    def slab(col_start):
        cols = lax.dynamic_slice_in_dim(wide, col_start, width, 1)
        return jnp.concatenate([cols, my_shifts, filler], axis=1)

    own = slab(half * CH)
    other = slab((1 - half) * CH)
    nb = band_count
    dev = lambda s, b: s * nb + b
    axes = ("section", "ccd")
    swap = [(dev(s, b), dev(1 - s, b)) for s in range(2) for b in range(nb)]
    cross = [(dev(1, b), dev(0, b + 1)) for b in range(nb - 1)] + [
        (dev(0, b), dev(1, b - 1)) for b in range(1, nb)
    ]
    straight = [(dev(1, b), dev(1, b + 1)) for b in range(nb - 1)] + [
        (dev(0, b), dev(0, b - 1)) for b in range(1, nb)
    ]
    straight_down = [(dev(0, b), dev(0, b + 1)) for b in range(nb - 1)] + [
        (dev(1, b), dev(1, b - 1)) for b in range(1, nb)
    ]
    cross_down = [(dev(0, b), dev(1, b + 1)) for b in range(nb - 1)] + [
        (dev(1, b), dev(0, b - 1)) for b in range(1, nb)
    ]
    edge = lambda x: jnp.where(half == 0, x[rh - HALF_K :], x[:HALF_K])
    got_swap = lax.ppermute(other, axes, swap)
    got_cross = lax.ppermute(other, axes, cross)
    got_straight = lax.ppermute(own, axes, straight)
    got_edge = lax.ppermute(edge(own), axes, straight_down)
    got_edge_cross = lax.ppermute(edge(other), axes, cross_down)
    pick = lambda a, b: jnp.where(half == 0, a, b)
    window = jnp.concatenate(
        [
            pick(got_edge, got_edge_cross),
            pick(got_cross, got_straight),
            pick(own, got_swap),
            pick(got_swap, own),
            pick(got_straight, got_cross),
            pick(got_edge_cross, got_edge),
        ],
        axis=0,
    )
    lead = ROWS + 2 * HALF_K
    lead_pad = -(-lead // 16) * 16
    steps = window[REACH : REACH + lead, width].astype(jnp.int32)
    picks = jnp.pad(jnp.arange(lead) + REACH + steps, (0, lead_pad - lead))
    out_rows = top_row - HALF_K + jnp.arange(lead_pad)
    inside = (out_rows >= 0) & (out_rows < total_rows) & (jnp.arange(lead_pad) < lead)
    warped = jnp.take(window, picks, axis=0, mode="clip")
    image = jnp.where(inside[:, None], warped, jnp.zeros((), warped.dtype))
    span = 2 * STRIP
    tap_lanes = lambda powers: jnp.pad(
        basis_taps(powers).astype(jnp.float32), ((0, 0), (0, span - KW))
    )
    col_taps = tap_lanes(column_power)
    row_taps = tap_lanes(row_power)
    positions = jnp.stack([top_row, left_col]).astype(jnp.int32)
    owners = tile_owner.reshape(1, -1)
    weights = tile_weight.reshape(1, -1)
    groups = TILE * TILE // STRIP
    tiles = owners.shape[1]
    row_tiles = ROWS // TILE
    per_lane = STRIP // TILE

    def match_kernel(kp_ref, pos_ref, img_ref, ctap_ref, rtap_ref, own_ref, w_ref,
                     out_ref, acc_ref, pack_ref, a_ref, b_ref, colm_ref, rowm_ref):
        i = pl.program_id(0)

        @pl.when(i == 0)
        def _():
            for k in range(NBASIS):
                spread = jnp.broadcast_to(ctap_ref[pl.ds(k, 1), :], (STRIP, span))
                band_t = pltpu.roll(spread, 0, 1, stride=1, stride_axis=0)
                colm_ref[:, k * STRIP : (k + 1) * STRIP] = band_t.T.astype(jnp.bfloat16)
                spread = jnp.broadcast_to(rtap_ref[pl.ds(k, 1), :], (ROWS, span))
                band = pltpu.roll(spread, 0, 1, stride=1, stride_axis=0)
                rowm_ref[k] = band.astype(jnp.bfloat16)
            rows = lax.broadcasted_iota(jnp.int32, (ROWS, STRIP), 0) + pos_ref[0]
            u = 2.0 * (rows.astype(jnp.float32) + 0.5) / total_rows - 1.0
            for k in range(NBASIS):
                a_ref[k] = kp_ref[k, 0] + kp_ref[k, 1] * u + kp_ref[k, 3] * u * u
                b_ref[k] = kp_ref[k, 2] + kp_ref[k, 4] * u

        offset = pl.multiple_of(i * STRIP, STRIP)
        strip = img_ref[:, pl.ds(offset, span)]
        across = jnp.dot(strip, colm_ref[...], preferred_element_type=jnp.float32)
        across = across.astype(jnp.bfloat16)
        cols = lax.broadcasted_iota(jnp.int32, (1, STRIP), 1) + (pos_ref[1] + i * STRIP)
        v = 2.0 * (cols.astype(jnp.float32) + 0.5) / total_cols - 1.0
        acc = jnp.zeros((ROWS, STRIP), jnp.float32)
        for k in range(NBASIS):
            vert = jnp.dot(
                rowm_ref[k, :, pl.ds(0, lead_pad)], across[:, k * STRIP : (k + 1) * STRIP],
                preferred_element_type=jnp.float32,
            )
            coef = a_ref[k] + v * (b_ref[k] + kp_ref[k, 5] * v)
            acc = acc + coef * vert
        acc_ref[...] = acc
        lane_group = lax.broadcasted_iota(jnp.int32, (groups, STRIP), 1) // TILE
        for rb in range(row_tiles):
            picked = [
                acc_ref[pl.ds(rb * TILE + g, groups, stride=per_lane), :] for g in range(per_lane)
            ]
            for cbl in range(per_lane):
                packed = jnp.zeros((groups, STRIP), jnp.float32)
                for g in range(per_lane):
                    shift = ((g - cbl) % per_lane) * TILE
                    rolled = pltpu.roll(picked[g], shift, 1) if shift else picked[g]
                    packed = jnp.where(lane_group == g, rolled, packed)
                j = (i * per_lane + cbl) * row_tiles + rb
                pack_ref[pl.ds(pl.multiple_of(j * groups, groups), groups), :] = packed

        @pl.when(i == strips - 1)
        def _():
            owner_ids = lax.broadcasted_iota(jnp.int32, (band_count, tiles), 0)
            sel = jnp.where(owner_ids == own_ref[...], w_ref[...], 0.0)
            for q in range(groups):
                part = pack_ref[pl.ds(q, tiles, stride=groups), :]
                out_ref[pl.ds(q, band_count, stride=groups), :] = jnp.dot(
                    sel, part, precision=lax.Precision.HIGHEST,
                    preferred_element_type=jnp.float32,
                )

    full = lambda shape: pl.BlockSpec(shape, lambda i: (0,) * len(shape))
    outgoing = pl.pallas_call(
        match_kernel,
        grid=(strips,),
        in_specs=[
            pl.BlockSpec(memory_space=pltpu.SMEM),
            pl.BlockSpec(memory_space=pltpu.SMEM),
            full(image.shape),
            full(col_taps.shape),
            full(row_taps.shape),
            full(owners.shape),
            full(weights.shape),
        ],
        out_specs=full((band_count * groups, STRIP)),
        out_shape=jax.ShapeDtypeStruct((band_count * groups, STRIP), jnp.float32),
        scratch_shapes=[
            pltpu.VMEM((ROWS, STRIP), jnp.float32),
            pltpu.VMEM((tiles * groups, STRIP), jnp.float32),
            pltpu.VMEM((NBASIS, ROWS, STRIP), jnp.float32),
            pltpu.VMEM((NBASIS, ROWS, STRIP), jnp.float32),
            pltpu.VMEM((span, NBASIS * STRIP), jnp.bfloat16),
            pltpu.VMEM((NBASIS, ROWS, span), jnp.bfloat16),
        ],
    )(kernel_poly, positions, image, col_taps, row_taps, owners, weights)
    outgoing = outgoing.reshape(band_count, groups, STRIP)
    outgoing = outgoing.astype(jnp.bfloat16)
    incoming = lax.all_to_all(outgoing, "ccd", split_axis=0, concat_axis=0, tiled=True)
    patch_sum = jnp.sum(incoming.astype(jnp.float32), axis=0, keepdims=True)
    return patch_sum.reshape(1, 1, TILE, TILE)


def solution(mesh):
    in_specs = (
        P("ccd", "section", None, None),
        P("ccd", "section", None),
        P("ccd", "section", None, None),
        P("ccd"),
        P(),
        P("ccd", "section", None, None),
        P("ccd", "section", None),
    )
    out_specs = P("section", "ccd", None, None)
    return jax.shard_map(shards, mesh=mesh, in_specs=in_specs, out_specs=out_specs, check_vma=False)
```

```python
import jax
import jax.numpy as jnp
from jax import lax
from jax.sharding import PartitionSpec as P
from jax.experimental import pallas as pl
from jax.experimental.pallas import tpu as pltpu

ROWS = 128
TILE = 32
STRIP = 128
KW = 21
NBASIS = 13
NPOLY = 6
HALF_K = 10
CH = 1024
REACH = 64


basis_sigma = (0.75, 0.75, 0.75, 0.75, 0.75, 0.75, 1.5, 1.5, 1.5, 1.5, 3.0, 3.0, 3.0)
column_power = (0, 1, 0, 2, 1, 0, 0, 1, 0, 1, 0, 1, 0)
row_power = (0, 0, 1, 0, 1, 2, 0, 0, 1, 1, 0, 0, 1)


def with_halo(array, sides, width):
    for axis, dim in sides:
        devices, length = (lax.axis_size(axis), array.shape[dim])
        up = [(i, (i + 1) % devices) for i in range(devices - 1)]
        down = [(j, i) for i, j in up]
        last = lax.slice_in_dim(array, length - width, length, axis=dim)
        leading = lax.slice_in_dim(array, 0, width, axis=dim)
        before = lax.ppermute(last, axis, up)
        after = lax.ppermute(leading, axis, down)
        array = jnp.concatenate([before, array, after], axis=dim)
    return array


def basis_taps(powers, sigmas=basis_sigma):
    offsets = jnp.arange(KW).astype(jnp.float32) - HALF_K
    sigma_col = jnp.array(sigmas, dtype=jnp.float32)[:, None]
    power_col = jnp.array(powers, dtype=jnp.int32)[:, None]
    spread = offsets[None, :]
    envelope = jnp.exp(-(spread * spread) / (2.0 * sigma_col * sigma_col))
    factor = jnp.where(power_col == 0, 1.0, jnp.where(power_col == 1, spread, spread * spread))
    shaped = envelope * factor
    scale = jnp.sqrt(jnp.sum(shaped * shaped, axis=1, keepdims=True))
    return (shaped / scale).astype(jnp.bfloat16)


def coefficients(terms, row_coord, col_coord):
    return (
        terms[0]
        + terms[1] * row_coord
        + terms[2] * col_coord
        + terms[3] * row_coord * row_coord
        + terms[4] * row_coord * col_coord
        + terms[5] * col_coord * col_coord
    )


def band_matrix(tap_table, inner_len):
    lead_idx = jnp.arange(inner_len + 2 * HALF_K)[:, None]
    trail_idx = jnp.arange(inner_len)[None, :]
    offset = lead_idx - trail_idx
    onehot = (offset[None] == jnp.arange(KW)[:, None, None]).astype(tap_table.dtype)
    band = jnp.einsum("kt,tai->kai", tap_table, onehot, preferred_element_type=jnp.float32)
    return band.astype(tap_table.dtype)


def shards(raw_counts, overscan, response, warp_rows, kernel_poly, tile_owner, tile_weight):
    band_count = lax.axis_size("ccd")
    halves = lax.axis_size("section")
    total_rows = ROWS * band_count
    total_cols = CH * halves
    top_row = lax.axis_index("ccd") * ROWS
    left_col = lax.axis_index("section") * CH
    half = lax.axis_index("section")
    strips = CH // STRIP
    wide_cols = strips * STRIP + STRIP
    rh = raw_counts.shape[2]
    calibrated = ((raw_counts - overscan[..., None]) * response).astype(jnp.bfloat16)[0, 0]
    shifts = (warp_rows - (top_row + jnp.arange(ROWS))).astype(jnp.bfloat16)
    my_shifts = lax.dynamic_slice_in_dim(shifts, half * rh, rh)[:, None]
    wide = jnp.pad(calibrated, ((0, 0), (HALF_K, HALF_K)))
    width = CH + 2 * HALF_K
    filler = jnp.zeros((rh, wide_cols - width - 1), jnp.bfloat16)

    def slab(col_start):
        cols = lax.dynamic_slice_in_dim(wide, col_start, width, 1)
        return jnp.concatenate([cols, my_shifts, filler], axis=1)

    own = slab(half * CH)
    other = slab((1 - half) * CH)
    nb = band_count
    dev = lambda s, b: s * nb + b
    axes = ("section", "ccd")
    swap = [(dev(s, b), dev(1 - s, b)) for s in range(2) for b in range(nb)]
    cross = [(dev(1, b), dev(0, b + 1)) for b in range(nb - 1)] + [
        (dev(0, b), dev(1, b - 1)) for b in range(1, nb)
    ]
    straight = [(dev(1, b), dev(1, b + 1)) for b in range(nb - 1)] + [
        (dev(0, b), dev(0, b - 1)) for b in range(1, nb)
    ]
    straight_down = [(dev(0, b), dev(0, b + 1)) for b in range(nb - 1)] + [
        (dev(1, b), dev(1, b - 1)) for b in range(1, nb)
    ]
    cross_down = [(dev(0, b), dev(1, b + 1)) for b in range(nb - 1)] + [
        (dev(1, b), dev(0, b - 1)) for b in range(1, nb)
    ]
    edge = lambda x: jnp.where(half == 0, x[rh - HALF_K :], x[:HALF_K])
    got_swap = lax.ppermute(other, axes, swap)
    got_cross = lax.ppermute(other, axes, cross)
    got_straight = lax.ppermute(own, axes, straight)
    got_edge = lax.ppermute(edge(own), axes, straight_down)
    got_edge_cross = lax.ppermute(edge(other), axes, cross_down)
    pick = lambda a, b: jnp.where(half == 0, a, b)
    window = jnp.concatenate(
        [
            pick(got_edge, got_edge_cross),
            pick(got_cross, got_straight),
            pick(own, got_swap),
            pick(got_swap, own),
            pick(got_straight, got_cross),
            pick(got_edge_cross, got_edge),
        ],
        axis=0,
    )
    lead = ROWS + 2 * HALF_K
    lead_pad = -(-lead // 16) * 16
    steps = window[REACH : REACH + lead, width].astype(jnp.int32)
    picks = jnp.pad(jnp.arange(lead) + REACH + steps, (0, lead_pad - lead))
    out_rows = top_row - HALF_K + jnp.arange(lead_pad)
    inside = (out_rows >= 0) & (out_rows < total_rows) & (jnp.arange(lead_pad) < lead)
    warped = jnp.take(window, picks, axis=0, mode="clip")
    image = jnp.where(inside[:, None], warped, jnp.zeros((), warped.dtype))
    span = 2 * STRIP
    both_taps = basis_taps(column_power + row_power, basis_sigma + basis_sigma)
    taps = jnp.pad(both_taps.astype(jnp.float32), ((0, 0), (0, span - KW)))
    params = jnp.concatenate(
        [kernel_poly.reshape(-1), jnp.stack([top_row, left_col]).astype(jnp.float32)]
    )
    at = NBASIS * NPOLY
    owners = tile_owner.reshape(1, -1)
    weights = tile_weight.reshape(1, -1)
    groups = TILE * TILE // STRIP
    tiles = owners.shape[1]
    row_tiles = ROWS // TILE
    per_lane = STRIP // TILE

    def match_kernel(kp_ref, img_ref, tap_ref, own_ref, w_ref,
                     out_ref, acc_ref, pack_ref, a_ref, b_ref, colm_ref, rowm_ref):
        i = pl.program_id(0)

        @pl.when(i == 0)
        def _():
            for k in range(NBASIS):
                spread = jnp.broadcast_to(tap_ref[pl.ds(k, 1), :], (STRIP, span))
                band_t = pltpu.roll(spread, 0, 1, stride=1, stride_axis=0)
                colm_ref[:, k * STRIP : (k + 1) * STRIP] = band_t.T.astype(jnp.bfloat16)
                spread = jnp.broadcast_to(tap_ref[pl.ds(NBASIS + k, 1), :], (ROWS, span))
                band = pltpu.roll(spread, 0, 1, stride=1, stride_axis=0)
                rowm_ref[k] = band.astype(jnp.bfloat16)
            rows = lax.broadcasted_iota(jnp.int32, (ROWS, STRIP), 0).astype(jnp.float32)
            u = 2.0 * (rows + kp_ref[at] + 0.5) / total_rows - 1.0
            for k in range(NBASIS):
                p = lambda m: kp_ref[k * NPOLY + m]
                a_ref[k] = p(0) + p(1) * u + p(3) * u * u
                b_ref[k] = p(2) + p(4) * u

        offset = pl.multiple_of(i * STRIP, STRIP)
        strip = img_ref[:, pl.ds(offset, span)]
        across = jnp.dot(strip, colm_ref[...], preferred_element_type=jnp.float32)
        across = across.astype(jnp.bfloat16)
        cols = lax.broadcasted_iota(jnp.int32, (1, STRIP), 1) + i * STRIP
        v = 2.0 * (cols.astype(jnp.float32) + kp_ref[at + 1] + 0.5) / total_cols - 1.0
        acc = jnp.zeros((ROWS, STRIP), jnp.float32)
        for k in range(NBASIS):
            vert = jnp.dot(
                rowm_ref[k, :, pl.ds(0, lead_pad)], across[:, k * STRIP : (k + 1) * STRIP],
                preferred_element_type=jnp.float32,
            )
            coef = a_ref[k] + v * (b_ref[k] + kp_ref[k * NPOLY + 5] * v)
            acc = acc + coef * vert
        acc_ref[...] = acc
        lane_group = lax.broadcasted_iota(jnp.int32, (groups, STRIP), 1) // TILE
        for rb in range(row_tiles):
            picked = [
                acc_ref[pl.ds(rb * TILE + g, groups, stride=per_lane), :] for g in range(per_lane)
            ]
            for cbl in range(per_lane):
                packed = jnp.zeros((groups, STRIP), jnp.float32)
                for g in range(per_lane):
                    shift = ((g - cbl) % per_lane) * TILE
                    rolled = pltpu.roll(picked[g], shift, 1) if shift else picked[g]
                    packed = jnp.where(lane_group == g, rolled, packed)
                j = (i * per_lane + cbl) * row_tiles + rb
                pack_ref[pl.ds(pl.multiple_of(j * groups, groups), groups), :] = packed

        @pl.when(i == strips - 1)
        def _():
            owner_ids = lax.broadcasted_iota(jnp.int32, (band_count, tiles), 0)
            sel = jnp.where(owner_ids == own_ref[...], w_ref[...], 0.0)
            for q in range(groups):
                part = pack_ref[pl.ds(q, tiles, stride=groups), :]
                out_ref[pl.ds(q, band_count, stride=groups), :] = jnp.dot(
                    sel, part, precision=lax.Precision.HIGHEST,
                    preferred_element_type=jnp.float32,
                )

    full = lambda shape: pl.BlockSpec(shape, lambda i: (0,) * len(shape))
    outgoing = pl.pallas_call(
        match_kernel,
        grid=(strips,),
        in_specs=[
            pl.BlockSpec(memory_space=pltpu.SMEM),
            full(image.shape),
            full(taps.shape),
            full(owners.shape),
            full(weights.shape),
        ],
        out_specs=full((band_count * groups, STRIP)),
        out_shape=jax.ShapeDtypeStruct((band_count * groups, STRIP), jnp.float32),
        scratch_shapes=[
            pltpu.VMEM((ROWS, STRIP), jnp.float32),
            pltpu.VMEM((tiles * groups, STRIP), jnp.float32),
            pltpu.VMEM((NBASIS, ROWS, STRIP), jnp.float32),
            pltpu.VMEM((NBASIS, ROWS, STRIP), jnp.float32),
            pltpu.VMEM((span, NBASIS * STRIP), jnp.bfloat16),
            pltpu.VMEM((NBASIS, ROWS, span), jnp.bfloat16),
        ],
    )(params, image, taps, owners, weights)
    outgoing = outgoing.reshape(band_count, groups, STRIP).astype(jnp.bfloat16)
    incoming = lax.all_to_all(outgoing, "ccd", split_axis=0, concat_axis=0, tiled=True)
    patch_sum = jnp.sum(incoming.astype(jnp.float32), axis=0, keepdims=True)
    return patch_sum.reshape(1, 1, TILE, TILE)


def solution(mesh):
    in_specs = (
        P("ccd", "section", None, None),
        P("ccd", "section", None),
        P("ccd", "section", None, None),
        P("ccd"),
        P(),
        P("ccd", "section", None, None),
        P("ccd", "section", None),
    )
    out_specs = P("section", "ccd", None, None)
    return jax.shard_map(shards, mesh=mesh, in_specs=in_specs, out_specs=out_specs, check_vma=False)
```

```python
import jax
import jax.numpy as jnp
from jax import lax
from jax.sharding import PartitionSpec as P
from jax.experimental import pallas as pl
from jax.experimental.pallas import tpu as pltpu

ROWS = 128
TILE = 32
STRIP = 128
KW = 21
NBASIS = 13
NPOLY = 6
HALF_K = 10
CH = 1024
REACH = 64


basis_sigma = (0.75, 0.75, 0.75, 0.75, 0.75, 0.75, 1.5, 1.5, 1.5, 1.5, 3.0, 3.0, 3.0)
column_power = (0, 1, 0, 2, 1, 0, 0, 1, 0, 1, 0, 1, 0)
row_power = (0, 0, 1, 0, 1, 2, 0, 0, 1, 1, 0, 0, 1)


def with_halo(array, sides, width):
    for axis, dim in sides:
        devices, length = (lax.axis_size(axis), array.shape[dim])
        up = [(i, (i + 1) % devices) for i in range(devices - 1)]
        down = [(j, i) for i, j in up]
        last = lax.slice_in_dim(array, length - width, length, axis=dim)
        leading = lax.slice_in_dim(array, 0, width, axis=dim)
        before = lax.ppermute(last, axis, up)
        after = lax.ppermute(leading, axis, down)
        array = jnp.concatenate([before, array, after], axis=dim)
    return array


def basis_taps(powers, sigmas=basis_sigma):
    offsets = jnp.arange(KW).astype(jnp.float32) - HALF_K
    sigma_col = jnp.array(sigmas, dtype=jnp.float32)[:, None]
    power_col = jnp.array(powers, dtype=jnp.int32)[:, None]
    spread = offsets[None, :]
    envelope = jnp.exp(-(spread * spread) / (2.0 * sigma_col * sigma_col))
    factor = jnp.where(power_col == 0, 1.0, jnp.where(power_col == 1, spread, spread * spread))
    shaped = envelope * factor
    scale = jnp.sqrt(jnp.sum(shaped * shaped, axis=1, keepdims=True))
    return (shaped / scale).astype(jnp.bfloat16)


def coefficients(terms, row_coord, col_coord):
    return (
        terms[0]
        + terms[1] * row_coord
        + terms[2] * col_coord
        + terms[3] * row_coord * row_coord
        + terms[4] * row_coord * col_coord
        + terms[5] * col_coord * col_coord
    )


def band_matrix(tap_table, inner_len):
    lead_idx = jnp.arange(inner_len + 2 * HALF_K)[:, None]
    trail_idx = jnp.arange(inner_len)[None, :]
    offset = lead_idx - trail_idx
    onehot = (offset[None] == jnp.arange(KW)[:, None, None]).astype(tap_table.dtype)
    band = jnp.einsum("kt,tai->kai", tap_table, onehot, preferred_element_type=jnp.float32)
    return band.astype(tap_table.dtype)


def shards(raw_counts, overscan, response, warp_rows, kernel_poly, tile_owner, tile_weight):
    band_count = lax.axis_size("ccd")
    halves = lax.axis_size("section")
    total_rows = ROWS * band_count
    total_cols = CH * halves
    top_row = lax.axis_index("ccd") * ROWS
    left_col = lax.axis_index("section") * CH
    half = lax.axis_index("section")
    strips = CH // STRIP
    wide_cols = strips * STRIP + STRIP
    rh = raw_counts.shape[2]
    calibrated = ((raw_counts - overscan[..., None]) * response).astype(jnp.bfloat16)[0, 0]
    shifts = (warp_rows - (top_row + jnp.arange(ROWS))).astype(jnp.bfloat16)
    my_shifts = lax.dynamic_slice_in_dim(shifts, half * rh, rh)[:, None]
    wide = jnp.pad(calibrated, ((0, 0), (HALF_K, HALF_K)))
    width = CH + 2 * HALF_K

    def slab(col_start):
        cols = lax.dynamic_slice_in_dim(wide, col_start, width, 1)
        return jnp.concatenate([cols, my_shifts], axis=1)

    own = slab(half * CH)
    other = slab((1 - half) * CH)
    nb = band_count
    dev = lambda s, b: s * nb + b
    axes = ("section", "ccd")
    swap = [(dev(s, b), dev(1 - s, b)) for s in range(2) for b in range(nb)]
    cross = [(dev(1, b), dev(0, b + 1)) for b in range(nb - 1)] + [
        (dev(0, b), dev(1, b - 1)) for b in range(1, nb)
    ]
    straight = [(dev(1, b), dev(1, b + 1)) for b in range(nb - 1)] + [
        (dev(0, b), dev(0, b - 1)) for b in range(1, nb)
    ]
    straight_down = [(dev(0, b), dev(0, b + 1)) for b in range(nb - 1)] + [
        (dev(1, b), dev(1, b - 1)) for b in range(1, nb)
    ]
    cross_down = [(dev(0, b), dev(1, b + 1)) for b in range(nb - 1)] + [
        (dev(1, b), dev(0, b - 1)) for b in range(1, nb)
    ]
    edge = lambda x: jnp.where(half == 0, x[rh - HALF_K :], x[:HALF_K])
    got_swap = lax.ppermute(other, axes, swap)
    got_cross = lax.ppermute(other, axes, cross)
    got_straight = lax.ppermute(own, axes, straight)
    got_edge = lax.ppermute(edge(own), axes, straight_down)
    got_edge_cross = lax.ppermute(edge(other), axes, cross_down)
    pick = lambda a, b: jnp.where(half == 0, a, b)
    window = jnp.concatenate(
        [
            pick(got_edge, got_edge_cross),
            pick(got_cross, got_straight),
            pick(own, got_swap),
            pick(got_swap, own),
            pick(got_straight, got_cross),
            pick(got_edge_cross, got_edge),
        ],
        axis=0,
    )
    window = jnp.pad(window, ((0, 0), (0, wide_cols - width - 1)))
    lead = ROWS + 2 * HALF_K
    lead_pad = -(-lead // 16) * 16
    steps = window[REACH : REACH + lead, width].astype(jnp.int32)
    picks = jnp.pad(jnp.arange(lead) + REACH + steps, (0, lead_pad - lead))
    out_rows = top_row - HALF_K + jnp.arange(lead_pad)
    inside = (out_rows >= 0) & (out_rows < total_rows) & (jnp.arange(lead_pad) < lead)
    warped = jnp.take(window, picks, axis=0, mode="clip")
    image = jnp.where(inside[:, None], warped, jnp.zeros((), warped.dtype))
    span = 2 * STRIP
    both_taps = basis_taps(column_power + row_power, basis_sigma + basis_sigma)
    taps = jnp.pad(both_taps.astype(jnp.float32), ((0, 0), (0, span - KW)))
    params = jnp.concatenate(
        [kernel_poly.reshape(-1), jnp.stack([top_row, left_col]).astype(jnp.float32)]
    )
    at = NBASIS * NPOLY
    owners = tile_owner.reshape(1, -1)
    weights = tile_weight.reshape(1, -1)
    groups = TILE * TILE // STRIP
    tiles = owners.shape[1]
    row_tiles = ROWS // TILE
    per_lane = STRIP // TILE

    def match_kernel(kp_ref, img_ref, tap_ref, own_ref, w_ref,
                     out_ref, acc_ref, pack_ref, a_ref, b_ref, colm_ref, rowm_ref):
        i = pl.program_id(0)

        @pl.when(i == 0)
        def _():
            for k in range(NBASIS):
                spread = jnp.broadcast_to(tap_ref[pl.ds(k, 1), :], (STRIP, span))
                band_t = pltpu.roll(spread, 0, 1, stride=1, stride_axis=0)
                colm_ref[:, k * STRIP : (k + 1) * STRIP] = band_t.T.astype(jnp.bfloat16)
                spread = jnp.broadcast_to(tap_ref[pl.ds(NBASIS + k, 1), :], (ROWS, span))
                band = pltpu.roll(spread, 0, 1, stride=1, stride_axis=0)
                rowm_ref[k] = band.astype(jnp.bfloat16)
            rows = lax.broadcasted_iota(jnp.int32, (ROWS, STRIP), 0).astype(jnp.float32)
            u = 2.0 * (rows + kp_ref[at] + 0.5) / total_rows - 1.0
            for k in range(NBASIS):
                p = lambda m: kp_ref[k * NPOLY + m]
                a_ref[k] = p(0) + p(1) * u + p(3) * u * u
                b_ref[k] = p(2) + p(4) * u

        offset = pl.multiple_of(i * STRIP, STRIP)
        strip = img_ref[:, pl.ds(offset, span)]
        across = jnp.dot(strip, colm_ref[...], preferred_element_type=jnp.float32)
        across = across.astype(jnp.bfloat16)
        cols = lax.broadcasted_iota(jnp.int32, (1, STRIP), 1) + i * STRIP
        v = 2.0 * (cols.astype(jnp.float32) + kp_ref[at + 1] + 0.5) / total_cols - 1.0
        acc = jnp.zeros((ROWS, STRIP), jnp.float32)
        for k in range(NBASIS):
            vert = jnp.dot(
                rowm_ref[k, :, pl.ds(0, lead_pad)], across[:, k * STRIP : (k + 1) * STRIP],
                preferred_element_type=jnp.float32,
            )
            coef = a_ref[k] + v * (b_ref[k] + kp_ref[k * NPOLY + 5] * v)
            acc = acc + coef * vert
        acc_ref[...] = acc
        lane_group = lax.broadcasted_iota(jnp.int32, (groups, STRIP), 1) // TILE
        for rb in range(row_tiles):
            picked = [
                acc_ref[pl.ds(rb * TILE + g, groups, stride=per_lane), :] for g in range(per_lane)
            ]
            for cbl in range(per_lane):
                packed = jnp.zeros((groups, STRIP), jnp.float32)
                for g in range(per_lane):
                    shift = ((g - cbl) % per_lane) * TILE
                    rolled = pltpu.roll(picked[g], shift, 1) if shift else picked[g]
                    packed = jnp.where(lane_group == g, rolled, packed)
                j = (i * per_lane + cbl) * row_tiles + rb
                pack_ref[pl.ds(pl.multiple_of(j * groups, groups), groups), :] = packed

        @pl.when(i == strips - 1)
        def _():
            owner_ids = lax.broadcasted_iota(jnp.int32, (band_count, tiles), 0)
            sel = jnp.where(owner_ids == own_ref[...], w_ref[...], 0.0)
            for q in range(groups):
                part = pack_ref[pl.ds(q, tiles, stride=groups), :]
                out_ref[pl.ds(q, band_count, stride=groups), :] = jnp.dot(
                    sel, part, precision=lax.Precision.HIGHEST,
                    preferred_element_type=jnp.float32,
                )

    full = lambda shape: pl.BlockSpec(shape, lambda i: (0,) * len(shape))
    outgoing = pl.pallas_call(
        match_kernel,
        grid=(strips,),
        in_specs=[
            pl.BlockSpec(memory_space=pltpu.SMEM),
            full(image.shape),
            full(taps.shape),
            full(owners.shape),
            full(weights.shape),
        ],
        out_specs=full((band_count * groups, STRIP)),
        out_shape=jax.ShapeDtypeStruct((band_count * groups, STRIP), jnp.float32),
        scratch_shapes=[
            pltpu.VMEM((ROWS, STRIP), jnp.float32),
            pltpu.VMEM((tiles * groups, STRIP), jnp.float32),
            pltpu.VMEM((NBASIS, ROWS, STRIP), jnp.float32),
            pltpu.VMEM((NBASIS, ROWS, STRIP), jnp.float32),
            pltpu.VMEM((span, NBASIS * STRIP), jnp.bfloat16),
            pltpu.VMEM((NBASIS, ROWS, span), jnp.bfloat16),
        ],
    )(params, image, taps, owners, weights)
    outgoing = outgoing.reshape(band_count, groups, STRIP).astype(jnp.bfloat16)
    incoming = lax.all_to_all(outgoing, "ccd", split_axis=0, concat_axis=0, tiled=True)
    patch_sum = jnp.sum(incoming.astype(jnp.float32), axis=0, keepdims=True)
    return patch_sum.reshape(1, 1, TILE, TILE)


def solution(mesh):
    in_specs = (
        P("ccd", "section", None, None),
        P("ccd", "section", None),
        P("ccd", "section", None, None),
        P("ccd"),
        P(),
        P("ccd", "section", None, None),
        P("ccd", "section", None),
    )
    out_specs = P("section", "ccd", None, None)
    return jax.shard_map(shards, mesh=mesh, in_specs=in_specs, out_specs=out_specs, check_vma=False)
```

```python
import jax
import jax.numpy as jnp
from jax import lax
from jax.sharding import PartitionSpec as P
from jax.experimental import pallas as pl
from jax.experimental.pallas import tpu as pltpu

ROWS = 128
TILE = 32
STRIP = 128
KW = 21
NBASIS = 13
NPOLY = 6
HALF_K = 10
CH = 1024
REACH = 64


basis_sigma = (0.75, 0.75, 0.75, 0.75, 0.75, 0.75, 1.5, 1.5, 1.5, 1.5, 3.0, 3.0, 3.0)
column_power = (0, 1, 0, 2, 1, 0, 0, 1, 0, 1, 0, 1, 0)
row_power = (0, 0, 1, 0, 1, 2, 0, 0, 1, 1, 0, 0, 1)


def with_halo(array, sides, width):
    for axis, dim in sides:
        devices, length = (lax.axis_size(axis), array.shape[dim])
        up = [(i, (i + 1) % devices) for i in range(devices - 1)]
        down = [(j, i) for i, j in up]
        last = lax.slice_in_dim(array, length - width, length, axis=dim)
        leading = lax.slice_in_dim(array, 0, width, axis=dim)
        before = lax.ppermute(last, axis, up)
        after = lax.ppermute(leading, axis, down)
        array = jnp.concatenate([before, array, after], axis=dim)
    return array


def basis_taps(powers, sigmas=basis_sigma):
    offsets = jnp.arange(KW).astype(jnp.float32) - HALF_K
    sigma_col = jnp.array(sigmas, dtype=jnp.float32)[:, None]
    power_col = jnp.array(powers, dtype=jnp.int32)[:, None]
    spread = offsets[None, :]
    envelope = jnp.exp(-(spread * spread) / (2.0 * sigma_col * sigma_col))
    factor = jnp.where(power_col == 0, 1.0, jnp.where(power_col == 1, spread, spread * spread))
    shaped = envelope * factor
    scale = jnp.sqrt(jnp.sum(shaped * shaped, axis=1, keepdims=True))
    return (shaped / scale).astype(jnp.bfloat16)


def coefficients(terms, row_coord, col_coord):
    return (
        terms[0]
        + terms[1] * row_coord
        + terms[2] * col_coord
        + terms[3] * row_coord * row_coord
        + terms[4] * row_coord * col_coord
        + terms[5] * col_coord * col_coord
    )


def band_matrix(tap_table, inner_len):
    lead_idx = jnp.arange(inner_len + 2 * HALF_K)[:, None]
    trail_idx = jnp.arange(inner_len)[None, :]
    offset = lead_idx - trail_idx
    onehot = (offset[None] == jnp.arange(KW)[:, None, None]).astype(tap_table.dtype)
    band = jnp.einsum("kt,tai->kai", tap_table, onehot, preferred_element_type=jnp.float32)
    return band.astype(tap_table.dtype)


def shards(raw_counts, overscan, response, warp_rows, kernel_poly, tile_owner, tile_weight):
    band_count = lax.axis_size("ccd")
    halves = lax.axis_size("section")
    total_rows = ROWS * band_count
    total_cols = CH * halves
    top_row = lax.axis_index("ccd") * ROWS
    left_col = lax.axis_index("section") * CH
    half = lax.axis_index("section")
    strips = CH // STRIP
    wide_cols = strips * STRIP + STRIP
    rh = raw_counts.shape[2]
    calibrated = ((raw_counts - overscan[..., None]) * response).astype(jnp.bfloat16)[0, 0]
    shifts = (warp_rows - (top_row + jnp.arange(ROWS))).astype(jnp.bfloat16)
    my_shifts = lax.dynamic_slice_in_dim(shifts, half * rh, rh)[:, None]
    wide = jnp.pad(calibrated, ((0, 0), (HALF_K, HALF_K)))
    width = CH + 2 * HALF_K
    filler = jnp.zeros((rh, wide_cols - width - 1), jnp.bfloat16)

    def slab(col_start):
        cols = lax.dynamic_slice_in_dim(wide, col_start, width, 1)
        return jnp.concatenate([cols, my_shifts, filler], axis=1)

    own = slab(half * CH)
    other = slab((1 - half) * CH)
    nb = band_count
    dev = lambda s, b: s * nb + b
    axes = ("section", "ccd")
    swap = [(dev(s, b), dev(1 - s, b)) for s in range(2) for b in range(nb)]
    cross = [(dev(1, b), dev(0, b + 1)) for b in range(nb - 1)] + [
        (dev(0, b), dev(1, b - 1)) for b in range(1, nb)
    ]
    straight = [(dev(1, b), dev(1, b + 1)) for b in range(nb - 1)] + [
        (dev(0, b), dev(0, b - 1)) for b in range(1, nb)
    ]
    straight_down = [(dev(0, b), dev(0, b + 1)) for b in range(nb - 1)] + [
        (dev(1, b), dev(1, b - 1)) for b in range(1, nb)
    ]
    cross_down = [(dev(0, b), dev(1, b + 1)) for b in range(nb - 1)] + [
        (dev(1, b), dev(0, b - 1)) for b in range(1, nb)
    ]
    rim = 16
    edge = lambda x: jnp.where(half == 0, x[rh - rim :], x[:rim])
    got_swap = lax.ppermute(other, axes, swap)
    got_cross = lax.ppermute(other, axes, cross)
    got_straight = lax.ppermute(own, axes, straight)
    got_edge = lax.ppermute(edge(own), axes, straight_down)
    got_edge_cross = lax.ppermute(edge(other), axes, cross_down)
    pick = lambda a, b: jnp.where(half == 0, a, b)
    lead = ROWS + 2 * HALF_K
    lead_pad = -(-lead // 16) * 16
    near = REACH - HALF_K
    steps = jnp.concatenate(
        [
            pick(got_cross, got_straight)[near:, width],
            pick(own, got_swap)[:, width],
            pick(got_swap, own)[:, width],
            pick(got_straight, got_cross)[: 2 * HALF_K - (REACH - near), width],
        ]
    ).astype(jnp.int32)
    origin = rim + REACH
    out_rows = top_row - HALF_K + jnp.arange(lead)
    inside = (out_rows >= 0) & (out_rows < total_rows)
    picks = jnp.where(inside, jnp.arange(lead) + origin - HALF_K + steps, -1)
    picks = jnp.pad(picks, (0, lead_pad - lead), constant_values=-1)[:, None]
    pieces = (got_edge, got_edge_cross, got_cross, got_straight, own, got_swap)
    slot = (0, rim, rim + rh, rim + 2 * rh, rim + 3 * rh, rim + 4 * rh)
    bases = ((slot[0], slot[5]), (slot[5], slot[0]), (slot[1], slot[4]),
             (slot[4], slot[1]), (slot[2], slot[3]), (slot[3], slot[2]))
    span = 2 * STRIP
    both_taps = basis_taps(column_power + row_power, basis_sigma + basis_sigma)
    taps = jnp.pad(both_taps.astype(jnp.float32), ((0, 0), (0, span - KW)))
    params = jnp.concatenate(
        [kernel_poly.reshape(-1), jnp.stack([top_row, left_col]).astype(jnp.float32)]
    )
    at = NBASIS * NPOLY
    owners = tile_owner.reshape(1, -1)
    weights = tile_weight.reshape(1, -1)
    groups = TILE * TILE // STRIP
    tiles = owners.shape[1]
    row_tiles = ROWS // TILE
    per_lane = STRIP // TILE

    def match_kernel(kp_ref, picks_ref, e0_ref, e1_ref, p0_ref, p1_ref, p2_ref, p3_ref,
                     tap_ref, own_ref, w_ref,
                     out_ref, acc_ref, pack_ref, a_ref, b_ref, colm_ref, rowm_ref, img_ref):
        i = pl.program_id(0)

        @pl.when(i == 0)
        def _():
            first = kp_ref[at + 1] == 0.0
            gathered = jnp.zeros((lead_pad, wide_cols), jnp.float32)
            piece_refs = (e0_ref, e1_ref, p0_ref, p1_ref, p2_ref, p3_ref)
            for ref, (b0, b1) in zip(piece_refs, bases):
                n = ref.shape[0]
                base = jnp.where(first, b0, b1)
                hit = lax.broadcasted_iota(jnp.int32, (lead_pad, n), 1) + base == picks_ref[...]
                gathered = gathered + jnp.dot(
                    hit.astype(jnp.bfloat16), ref[...], preferred_element_type=jnp.float32
                )
            img_ref[...] = gathered.astype(jnp.bfloat16)
            for k in range(NBASIS):
                spread = jnp.broadcast_to(tap_ref[pl.ds(k, 1), :], (STRIP, span))
                band_t = pltpu.roll(spread, 0, 1, stride=1, stride_axis=0)
                colm_ref[:, k * STRIP : (k + 1) * STRIP] = band_t.T.astype(jnp.bfloat16)
                spread = jnp.broadcast_to(tap_ref[pl.ds(NBASIS + k, 1), :], (ROWS, span))
                band = pltpu.roll(spread, 0, 1, stride=1, stride_axis=0)
                rowm_ref[k] = band.astype(jnp.bfloat16)
            rows = lax.broadcasted_iota(jnp.int32, (ROWS, STRIP), 0).astype(jnp.float32)
            u = 2.0 * (rows + kp_ref[at] + 0.5) / total_rows - 1.0
            for k in range(NBASIS):
                p = lambda m: kp_ref[k * NPOLY + m]
                a_ref[k] = p(0) + p(1) * u + p(3) * u * u
                b_ref[k] = p(2) + p(4) * u

        offset = pl.multiple_of(i * STRIP, STRIP)
        strip = img_ref[:, pl.ds(offset, span)]
        across = jnp.dot(strip, colm_ref[...], preferred_element_type=jnp.float32)
        across = across.astype(jnp.bfloat16)
        cols = lax.broadcasted_iota(jnp.int32, (1, STRIP), 1) + i * STRIP
        v = 2.0 * (cols.astype(jnp.float32) + kp_ref[at + 1] + 0.5) / total_cols - 1.0
        acc = jnp.zeros((ROWS, STRIP), jnp.float32)
        for k in range(NBASIS):
            vert = jnp.dot(
                rowm_ref[k, :, pl.ds(0, lead_pad)], across[:, k * STRIP : (k + 1) * STRIP],
                preferred_element_type=jnp.float32,
            )
            coef = a_ref[k] + v * (b_ref[k] + kp_ref[k * NPOLY + 5] * v)
            acc = acc + coef * vert
        acc_ref[...] = acc
        lane_group = lax.broadcasted_iota(jnp.int32, (groups, STRIP), 1) // TILE
        for rb in range(row_tiles):
            picked = [
                acc_ref[pl.ds(rb * TILE + g, groups, stride=per_lane), :] for g in range(per_lane)
            ]
            for cbl in range(per_lane):
                packed = jnp.zeros((groups, STRIP), jnp.float32)
                for g in range(per_lane):
                    shift = ((g - cbl) % per_lane) * TILE
                    rolled = pltpu.roll(picked[g], shift, 1) if shift else picked[g]
                    packed = jnp.where(lane_group == g, rolled, packed)
                j = (i * per_lane + cbl) * row_tiles + rb
                pack_ref[pl.ds(pl.multiple_of(j * groups, groups), groups), :] = packed

        @pl.when(i == strips - 1)
        def _():
            owner_ids = lax.broadcasted_iota(jnp.int32, (band_count, tiles), 0)
            sel = jnp.where(owner_ids == own_ref[...], w_ref[...], 0.0)
            for q in range(groups):
                part = pack_ref[pl.ds(q, tiles, stride=groups), :]
                out_ref[pl.ds(q, band_count, stride=groups), :] = jnp.dot(
                    sel, part, precision=lax.Precision.HIGHEST,
                    preferred_element_type=jnp.float32,
                )

    full = lambda shape: pl.BlockSpec(shape, lambda i: (0,) * len(shape))
    outgoing = pl.pallas_call(
        match_kernel,
        grid=(strips,),
        in_specs=[pl.BlockSpec(memory_space=pltpu.SMEM), full(picks.shape)]
        + [full(x.shape) for x in pieces]
        + [full(taps.shape), full(owners.shape), full(weights.shape)],
        out_specs=full((band_count * groups, STRIP)),
        out_shape=jax.ShapeDtypeStruct((band_count * groups, STRIP), jnp.float32),
        scratch_shapes=[
            pltpu.VMEM((ROWS, STRIP), jnp.float32),
            pltpu.VMEM((tiles * groups, STRIP), jnp.float32),
            pltpu.VMEM((NBASIS, ROWS, STRIP), jnp.float32),
            pltpu.VMEM((NBASIS, ROWS, STRIP), jnp.float32),
            pltpu.VMEM((span, NBASIS * STRIP), jnp.bfloat16),
            pltpu.VMEM((NBASIS, ROWS, span), jnp.bfloat16),
            pltpu.VMEM((lead_pad, wide_cols), jnp.bfloat16),
        ],
    )(params, picks, *pieces, taps, owners, weights)
    outgoing = outgoing.reshape(band_count, groups, STRIP).astype(jnp.bfloat16)
    incoming = lax.all_to_all(outgoing, "ccd", split_axis=0, concat_axis=0, tiled=True)
    patch_sum = jnp.sum(incoming.astype(jnp.float32), axis=0, keepdims=True)
    return patch_sum.reshape(1, 1, TILE, TILE)


def solution(mesh):
    in_specs = (
        P("ccd", "section", None, None),
        P("ccd", "section", None),
        P("ccd", "section", None, None),
        P("ccd"),
        P(),
        P("ccd", "section", None, None),
        P("ccd", "section", None),
    )
    out_specs = P("section", "ccd", None, None)
    return jax.shard_map(shards, mesh=mesh, in_specs=in_specs, out_specs=out_specs, check_vma=False)
```

```python
import jax
import jax.numpy as jnp
from jax import lax
from jax.sharding import PartitionSpec as P
from jax.experimental import pallas as pl
from jax.experimental.pallas import tpu as pltpu

ROWS = 128
TILE = 32
STRIP = 128
KW = 21
NBASIS = 13
NPOLY = 6
HALF_K = 10
CH = 1024
REACH = 64


basis_sigma = (0.75, 0.75, 0.75, 0.75, 0.75, 0.75, 1.5, 1.5, 1.5, 1.5, 3.0, 3.0, 3.0)
column_power = (0, 1, 0, 2, 1, 0, 0, 1, 0, 1, 0, 1, 0)
row_power = (0, 0, 1, 0, 1, 2, 0, 0, 1, 1, 0, 0, 1)


def with_halo(array, sides, width):
    for axis, dim in sides:
        devices, length = (lax.axis_size(axis), array.shape[dim])
        up = [(i, (i + 1) % devices) for i in range(devices - 1)]
        down = [(j, i) for i, j in up]
        last = lax.slice_in_dim(array, length - width, length, axis=dim)
        leading = lax.slice_in_dim(array, 0, width, axis=dim)
        before = lax.ppermute(last, axis, up)
        after = lax.ppermute(leading, axis, down)
        array = jnp.concatenate([before, array, after], axis=dim)
    return array


def basis_taps(powers, sigmas=basis_sigma):
    offsets = jnp.arange(KW).astype(jnp.float32) - HALF_K
    sigma_col = jnp.array(sigmas, dtype=jnp.float32)[:, None]
    power_col = jnp.array(powers, dtype=jnp.int32)[:, None]
    spread = offsets[None, :]
    envelope = jnp.exp(-(spread * spread) / (2.0 * sigma_col * sigma_col))
    factor = jnp.where(power_col == 0, 1.0, jnp.where(power_col == 1, spread, spread * spread))
    shaped = envelope * factor
    scale = jnp.sqrt(jnp.sum(shaped * shaped, axis=1, keepdims=True))
    return (shaped / scale).astype(jnp.bfloat16)


def coefficients(terms, row_coord, col_coord):
    return (
        terms[0]
        + terms[1] * row_coord
        + terms[2] * col_coord
        + terms[3] * row_coord * row_coord
        + terms[4] * row_coord * col_coord
        + terms[5] * col_coord * col_coord
    )


def band_matrix(tap_table, inner_len):
    lead_idx = jnp.arange(inner_len + 2 * HALF_K)[:, None]
    trail_idx = jnp.arange(inner_len)[None, :]
    offset = lead_idx - trail_idx
    onehot = (offset[None] == jnp.arange(KW)[:, None, None]).astype(tap_table.dtype)
    band = jnp.einsum("kt,tai->kai", tap_table, onehot, preferred_element_type=jnp.float32)
    return band.astype(tap_table.dtype)


def shards(raw_counts, overscan, response, warp_rows, kernel_poly, tile_owner, tile_weight):
    band_count = lax.axis_size("ccd")
    halves = lax.axis_size("section")
    total_rows = ROWS * band_count
    total_cols = CH * halves
    top_row = lax.axis_index("ccd") * ROWS
    left_col = lax.axis_index("section") * CH
    half = lax.axis_index("section")
    strips = CH // STRIP
    wide_cols = strips * STRIP + STRIP
    rh = raw_counts.shape[2]
    calibrated = ((raw_counts - overscan[..., None]) * response).astype(jnp.bfloat16)[0, 0]
    shifts = (warp_rows - (top_row + jnp.arange(ROWS))).astype(jnp.bfloat16)
    my_shifts = lax.dynamic_slice_in_dim(shifts, half * rh, rh)[:, None]
    wide = jnp.pad(calibrated, ((0, 0), (HALF_K, HALF_K)))
    width = CH + 2 * HALF_K
    filler = jnp.zeros((rh, wide_cols - width - 1), jnp.bfloat16)

    def slab(col_start):
        cols = lax.dynamic_slice_in_dim(wide, col_start, width, 1)
        return jnp.concatenate([cols, my_shifts, filler], axis=1)

    own = slab(half * CH)
    other = slab((1 - half) * CH)
    nb = band_count
    dev = lambda s, b: s * nb + b
    axes = ("section", "ccd")
    swap = [(dev(s, b), dev(1 - s, b)) for s in range(2) for b in range(nb)]
    cross = [(dev(1, b), dev(0, b + 1)) for b in range(nb - 1)] + [
        (dev(0, b), dev(1, b - 1)) for b in range(1, nb)
    ]
    straight = [(dev(1, b), dev(1, b + 1)) for b in range(nb - 1)] + [
        (dev(0, b), dev(0, b - 1)) for b in range(1, nb)
    ]
    straight_down = [(dev(0, b), dev(0, b + 1)) for b in range(nb - 1)] + [
        (dev(1, b), dev(1, b - 1)) for b in range(1, nb)
    ]
    cross_down = [(dev(0, b), dev(1, b + 1)) for b in range(nb - 1)] + [
        (dev(1, b), dev(0, b - 1)) for b in range(1, nb)
    ]
    rim = 16
    edge = lambda x: jnp.where(half == 0, x[rh - rim :], x[:rim])
    got_swap = lax.ppermute(other, axes, swap)
    got_cross = lax.ppermute(other, axes, cross)
    got_straight = lax.ppermute(own, axes, straight)
    got_edge = lax.ppermute(edge(own), axes, straight_down)
    got_edge_cross = lax.ppermute(edge(other), axes, cross_down)
    pick = lambda a, b: jnp.where(half == 0, a, b)
    lead = ROWS + 2 * HALF_K
    lead_pad = -(-lead // 16) * 16
    near = REACH - HALF_K
    steps = jnp.concatenate(
        [
            pick(got_cross, got_straight)[near:, width],
            pick(own, got_swap)[:, width],
            pick(got_swap, own)[:, width],
            pick(got_straight, got_cross)[: 2 * HALF_K - (REACH - near), width],
        ]
    ).astype(jnp.int32)
    origin = rim + REACH
    out_rows = top_row - HALF_K + jnp.arange(lead)
    inside = (out_rows >= 0) & (out_rows < total_rows)
    picks = jnp.where(inside, jnp.arange(lead) + origin - HALF_K + steps, -1)
    picks = jnp.pad(picks, (0, lead_pad - lead), constant_values=-1)[:, None]
    pieces = (got_edge, got_edge_cross, got_cross, got_straight, own, got_swap)
    slot = (0, rim, rim + rh, rim + 2 * rh, rim + 3 * rh, rim + 4 * rh)
    bases = ((slot[0], slot[5]), (slot[5], slot[0]), (slot[1], slot[4]),
             (slot[4], slot[1]), (slot[2], slot[3]), (slot[3], slot[2]))
    span = 2 * STRIP
    both_taps = basis_taps(column_power + row_power, basis_sigma + basis_sigma)
    taps = jnp.pad(both_taps.astype(jnp.float32), ((0, 0), (0, span - KW)))
    params = jnp.concatenate(
        [kernel_poly.reshape(-1), jnp.stack([top_row, left_col]).astype(jnp.float32)]
    )
    at = NBASIS * NPOLY
    owners = tile_owner.reshape(1, -1)
    weights = tile_weight.reshape(1, -1)
    groups = TILE * TILE // STRIP
    tiles = owners.shape[1]
    row_tiles = ROWS // TILE
    per_lane = STRIP // TILE

    def match_kernel(kp_ref, picks_ref, e0_ref, e1_ref, p0_ref, p1_ref, p2_ref, p3_ref,
                     tap_ref, own_ref, w_ref,
                     out_ref, acc_ref, pack_ref, a_ref, b_ref, colm_ref, rowm_ref, img_ref):
        i = pl.program_id(0)

        @pl.when(i == 0)
        def _():
            first = kp_ref[at + 1] == 0.0
            gathered = jnp.zeros((lead_pad, wide_cols), jnp.float32)
            piece_refs = (e0_ref, e1_ref, p0_ref, p1_ref, p2_ref, p3_ref)
            for ref, (b0, b1) in zip(piece_refs, bases):
                n = ref.shape[0]
                base = jnp.where(first, b0, b1)
                hit = lax.broadcasted_iota(jnp.int32, (lead_pad, n), 1) + base == picks_ref[...]
                gathered = gathered + jnp.dot(
                    hit.astype(jnp.bfloat16), ref[...], preferred_element_type=jnp.float32
                )
            img_ref[...] = gathered.astype(jnp.bfloat16)
            for k in range(NBASIS):
                spread = jnp.broadcast_to(tap_ref[pl.ds(k, 1), :], (STRIP, span))
                band_t = pltpu.roll(spread, 0, 1, stride=1, stride_axis=0)
                colm_ref[:, k * STRIP : (k + 1) * STRIP] = band_t.T.astype(jnp.bfloat16)
                spread = jnp.broadcast_to(tap_ref[pl.ds(NBASIS + k, 1), :], (ROWS, span))
                band = pltpu.roll(spread, 0, 1, stride=1, stride_axis=0)
                rowm_ref[k] = band.astype(jnp.bfloat16)
            rows = lax.broadcasted_iota(jnp.int32, (ROWS, STRIP), 0).astype(jnp.float32)
            u = 2.0 * (rows + kp_ref[at] + 0.5) / total_rows - 1.0
            for k in range(NBASIS):
                p = lambda m: kp_ref[k * NPOLY + m]
                a_ref[k] = p(0) + p(1) * u + p(3) * u * u
                b_ref[k] = p(2) + p(4) * u

        offset = pl.multiple_of(i * STRIP, STRIP)
        strip = img_ref[:, pl.ds(offset, span)]
        across = jnp.dot(strip, colm_ref[...], preferred_element_type=jnp.float32)
        across = across.astype(jnp.bfloat16)
        cols = lax.broadcasted_iota(jnp.int32, (1, STRIP), 1) + i * STRIP
        v = 2.0 * (cols.astype(jnp.float32) + kp_ref[at + 1] + 0.5) / total_cols - 1.0
        acc = jnp.zeros((ROWS, STRIP), jnp.float32)
        for k in range(NBASIS):
            vert = jnp.dot(
                rowm_ref[k, :, pl.ds(0, lead_pad)], across[:, k * STRIP : (k + 1) * STRIP],
                preferred_element_type=jnp.float32,
            )
            coef = a_ref[k] + v * (b_ref[k] + kp_ref[k * NPOLY + 5] * v)
            acc = acc + coef * vert
        acc_ref[...] = acc
        lane_group = lax.broadcasted_iota(jnp.int32, (groups, STRIP), 1) // TILE
        for rb in range(row_tiles):
            picked = [
                acc_ref[pl.ds(rb * TILE + g, groups, stride=per_lane), :] for g in range(per_lane)
            ]
            for cbl in range(per_lane):
                packed = jnp.zeros((groups, STRIP), jnp.float32)
                for g in range(per_lane):
                    shift = ((g - cbl) % per_lane) * TILE
                    rolled = pltpu.roll(picked[g], shift, 1) if shift else picked[g]
                    packed = jnp.where(lane_group == g, rolled, packed)
                j = (i * per_lane + cbl) * row_tiles + rb
                pack_ref[pl.ds(pl.multiple_of(j * groups, groups), groups), :] = packed

        @pl.when(i == strips - 1)
        def _():
            owner_ids = lax.broadcasted_iota(jnp.int32, (band_count, tiles), 0)
            sel = jnp.where(owner_ids == own_ref[...], w_ref[...], 0.0)
            for q in range(groups):
                part = pack_ref[pl.ds(q, tiles, stride=groups), :]
                out_ref[:, q, :] = jnp.dot(
                    sel, part, precision=lax.Precision.HIGHEST,
                    preferred_element_type=jnp.float32,
                ).astype(out_ref.dtype)

    full = lambda shape: pl.BlockSpec(shape, lambda i: (0,) * len(shape))
    outgoing = pl.pallas_call(
        match_kernel,
        grid=(strips,),
        in_specs=[pl.BlockSpec(memory_space=pltpu.SMEM), full(picks.shape)]
        + [full(x.shape) for x in pieces]
        + [full(taps.shape), full(owners.shape), full(weights.shape)],
        out_specs=full((band_count, groups, STRIP)),
        out_shape=jax.ShapeDtypeStruct((band_count, groups, STRIP), jnp.bfloat16),
        scratch_shapes=[
            pltpu.VMEM((ROWS, STRIP), jnp.float32),
            pltpu.VMEM((tiles * groups, STRIP), jnp.float32),
            pltpu.VMEM((NBASIS, ROWS, STRIP), jnp.float32),
            pltpu.VMEM((NBASIS, ROWS, STRIP), jnp.float32),
            pltpu.VMEM((span, NBASIS * STRIP), jnp.bfloat16),
            pltpu.VMEM((NBASIS, ROWS, span), jnp.bfloat16),
            pltpu.VMEM((lead_pad, wide_cols), jnp.bfloat16),
        ],
    )(params, picks, *pieces, taps, owners, weights)
    incoming = lax.all_to_all(outgoing, "ccd", split_axis=0, concat_axis=0, tiled=True)
    patch_sum = jnp.sum(incoming.astype(jnp.float32), axis=0, keepdims=True)
    return patch_sum.reshape(1, 1, TILE, TILE)


def solution(mesh):
    in_specs = (
        P("ccd", "section", None, None),
        P("ccd", "section", None),
        P("ccd", "section", None, None),
        P("ccd"),
        P(),
        P("ccd", "section", None, None),
        P("ccd", "section", None),
    )
    out_specs = P("section", "ccd", None, None)
    return jax.shard_map(shards, mesh=mesh, in_specs=in_specs, out_specs=out_specs, check_vma=False)
```

```python
import jax
import jax.numpy as jnp
from jax import lax
from jax.sharding import PartitionSpec as P
from jax.experimental import pallas as pl
from jax.experimental.pallas import tpu as pltpu

ROWS = 128
TILE = 32
STRIP = 128
KW = 21
NBASIS = 13
NPOLY = 6
HALF_K = 10
CH = 1024
REACH = 64


basis_sigma = (0.75, 0.75, 0.75, 0.75, 0.75, 0.75, 1.5, 1.5, 1.5, 1.5, 3.0, 3.0, 3.0)
column_power = (0, 1, 0, 2, 1, 0, 0, 1, 0, 1, 0, 1, 0)
row_power = (0, 0, 1, 0, 1, 2, 0, 0, 1, 1, 0, 0, 1)


def with_halo(array, sides, width):
    for axis, dim in sides:
        devices, length = (lax.axis_size(axis), array.shape[dim])
        up = [(i, (i + 1) % devices) for i in range(devices - 1)]
        down = [(j, i) for i, j in up]
        last = lax.slice_in_dim(array, length - width, length, axis=dim)
        leading = lax.slice_in_dim(array, 0, width, axis=dim)
        before = lax.ppermute(last, axis, up)
        after = lax.ppermute(leading, axis, down)
        array = jnp.concatenate([before, array, after], axis=dim)
    return array


def basis_taps(powers, sigmas=basis_sigma):
    offsets = jnp.arange(KW).astype(jnp.float32) - HALF_K
    sigma_col = jnp.array(sigmas, dtype=jnp.float32)[:, None]
    power_col = jnp.array(powers, dtype=jnp.int32)[:, None]
    spread = offsets[None, :]
    envelope = jnp.exp(-(spread * spread) / (2.0 * sigma_col * sigma_col))
    factor = jnp.where(power_col == 0, 1.0, jnp.where(power_col == 1, spread, spread * spread))
    shaped = envelope * factor
    scale = jnp.sqrt(jnp.sum(shaped * shaped, axis=1, keepdims=True))
    return (shaped / scale).astype(jnp.bfloat16)


def coefficients(terms, row_coord, col_coord):
    return (
        terms[0]
        + terms[1] * row_coord
        + terms[2] * col_coord
        + terms[3] * row_coord * row_coord
        + terms[4] * row_coord * col_coord
        + terms[5] * col_coord * col_coord
    )


def band_matrix(tap_table, inner_len):
    lead_idx = jnp.arange(inner_len + 2 * HALF_K)[:, None]
    trail_idx = jnp.arange(inner_len)[None, :]
    offset = lead_idx - trail_idx
    onehot = (offset[None] == jnp.arange(KW)[:, None, None]).astype(tap_table.dtype)
    band = jnp.einsum("kt,tai->kai", tap_table, onehot, preferred_element_type=jnp.float32)
    return band.astype(tap_table.dtype)


def shards(raw_counts, overscan, response, warp_rows, kernel_poly, tile_owner, tile_weight):
    band_count = lax.axis_size("ccd")
    halves = lax.axis_size("section")
    total_rows = ROWS * band_count
    total_cols = CH * halves
    top_row = lax.axis_index("ccd") * ROWS
    left_col = lax.axis_index("section") * CH
    half = lax.axis_index("section")
    strips = CH // STRIP
    wide_cols = strips * STRIP + STRIP
    rh = raw_counts.shape[2]
    calibrated = ((raw_counts - overscan[..., None]) * response).astype(jnp.bfloat16)[0, 0]
    shifts = (warp_rows - (top_row + jnp.arange(ROWS))).astype(jnp.bfloat16)
    my_shifts = lax.dynamic_slice_in_dim(shifts, half * rh, rh)[:, None]
    wide = jnp.pad(calibrated, ((0, 0), (HALF_K, HALF_K)))
    width = CH + 2 * HALF_K
    filler = jnp.zeros((rh, wide_cols - width - 1), jnp.bfloat16)

    def slab(col_start):
        cols = lax.dynamic_slice_in_dim(wide, col_start, width, 1)
        return jnp.concatenate([cols, my_shifts, filler], axis=1)

    own = slab(half * CH)
    other = slab((1 - half) * CH)
    nb = band_count
    axes = ("section", "ccd")
    swap = [(s * nb + b, (1 - s) * nb + b) for s in range(2) for b in range(nb)]
    got_swap = lax.ppermute(other, axes, swap)
    pick = lambda a, b: jnp.where(half == 0, a, b)
    first_rows = pick(own, got_swap)
    second_rows = pick(got_swap, own)
    rim = 16
    sent_up = jnp.concatenate([first_rows, second_rows[:rim]], axis=0)
    sent_down = jnp.concatenate([first_rows[rh - rim :], second_rows], axis=0)
    from_below = lax.ppermute(sent_up, "ccd", [(b, b - 1) for b in range(1, nb)])
    from_above = lax.ppermute(sent_down, "ccd", [(b, b + 1) for b in range(nb - 1)])
    lead = ROWS + 2 * HALF_K
    lead_pad = -(-lead // 16) * 16
    above = rh + rim
    steps = jnp.concatenate(
        [
            from_above[above - HALF_K :, width],
            first_rows[:, width],
            second_rows[:, width],
            from_below[:HALF_K, width],
        ]
    ).astype(jnp.int32)
    origin = rim + REACH
    out_rows = top_row - HALF_K + jnp.arange(lead)
    inside = (out_rows >= 0) & (out_rows < total_rows)
    picks = jnp.where(inside, jnp.arange(lead) + origin - HALF_K + steps, -1)
    picks = jnp.pad(picks, (0, lead_pad - lead), constant_values=-1)[:, None]
    pieces = (from_above, own, got_swap, from_below)
    bases = ((0, 0), (above, above + rh), (above + rh, above), (above + 2 * rh, above + 2 * rh))
    span = 2 * STRIP
    both_taps = basis_taps(column_power + row_power, basis_sigma + basis_sigma)
    taps = jnp.pad(both_taps.astype(jnp.float32), ((0, 0), (0, span - KW)))
    params = jnp.concatenate(
        [kernel_poly.reshape(-1), jnp.stack([top_row, left_col]).astype(jnp.float32)]
    )
    at = NBASIS * NPOLY
    owners = tile_owner.reshape(1, -1)
    weights = tile_weight.reshape(1, -1)
    groups = TILE * TILE // STRIP
    tiles = owners.shape[1]
    row_tiles = ROWS // TILE
    per_lane = STRIP // TILE

    def match_kernel(kp_ref, picks_ref, p0_ref, p1_ref, p2_ref, p3_ref,
                     tap_ref, own_ref, w_ref,
                     out_ref, acc_ref, pack_ref, a_ref, b_ref, colm_ref, rowm_ref, img_ref):
        i = pl.program_id(0)

        @pl.when(i == 0)
        def _():
            first = kp_ref[at + 1] == 0.0
            gathered = jnp.zeros((lead_pad, wide_cols), jnp.float32)
            piece_refs = (p0_ref, p1_ref, p2_ref, p3_ref)
            for ref, (b0, b1) in zip(piece_refs, bases):
                n = ref.shape[0]
                base = jnp.where(first, b0, b1)
                hit = lax.broadcasted_iota(jnp.int32, (lead_pad, n), 1) + base == picks_ref[...]
                gathered = gathered + jnp.dot(
                    hit.astype(jnp.bfloat16), ref[...], preferred_element_type=jnp.float32
                )
            img_ref[...] = gathered.astype(jnp.bfloat16)
            for k in range(NBASIS):
                spread = jnp.broadcast_to(tap_ref[pl.ds(k, 1), :], (STRIP, span))
                band_t = pltpu.roll(spread, 0, 1, stride=1, stride_axis=0)
                colm_ref[:, k * STRIP : (k + 1) * STRIP] = band_t.T.astype(jnp.bfloat16)
                spread = jnp.broadcast_to(tap_ref[pl.ds(NBASIS + k, 1), :], (ROWS, span))
                band = pltpu.roll(spread, 0, 1, stride=1, stride_axis=0)
                rowm_ref[k] = band.astype(jnp.bfloat16)
            rows = lax.broadcasted_iota(jnp.int32, (ROWS, STRIP), 0).astype(jnp.float32)
            u = 2.0 * (rows + kp_ref[at] + 0.5) / total_rows - 1.0
            for k in range(NBASIS):
                p = lambda m: kp_ref[k * NPOLY + m]
                a_ref[k] = p(0) + p(1) * u + p(3) * u * u
                b_ref[k] = p(2) + p(4) * u

        offset = pl.multiple_of(i * STRIP, STRIP)
        strip = img_ref[:, pl.ds(offset, span)]
        across = jnp.dot(strip, colm_ref[...], preferred_element_type=jnp.float32)
        across = across.astype(jnp.bfloat16)
        cols = lax.broadcasted_iota(jnp.int32, (1, STRIP), 1) + i * STRIP
        v = 2.0 * (cols.astype(jnp.float32) + kp_ref[at + 1] + 0.5) / total_cols - 1.0
        acc = jnp.zeros((ROWS, STRIP), jnp.float32)
        for k in range(NBASIS):
            vert = jnp.dot(
                rowm_ref[k, :, pl.ds(0, lead_pad)], across[:, k * STRIP : (k + 1) * STRIP],
                preferred_element_type=jnp.float32,
            )
            coef = a_ref[k] + v * (b_ref[k] + kp_ref[k * NPOLY + 5] * v)
            acc = acc + coef * vert
        acc_ref[...] = acc
        lane_group = lax.broadcasted_iota(jnp.int32, (groups, STRIP), 1) // TILE
        for rb in range(row_tiles):
            picked = [
                acc_ref[pl.ds(rb * TILE + g, groups, stride=per_lane), :] for g in range(per_lane)
            ]
            for cbl in range(per_lane):
                packed = jnp.zeros((groups, STRIP), jnp.float32)
                for g in range(per_lane):
                    shift = ((g - cbl) % per_lane) * TILE
                    rolled = pltpu.roll(picked[g], shift, 1) if shift else picked[g]
                    packed = jnp.where(lane_group == g, rolled, packed)
                j = (i * per_lane + cbl) * row_tiles + rb
                pack_ref[pl.ds(pl.multiple_of(j * groups, groups), groups), :] = packed

        @pl.when(i == strips - 1)
        def _():
            owner_ids = lax.broadcasted_iota(jnp.int32, (band_count, tiles), 0)
            sel = jnp.where(owner_ids == own_ref[...], w_ref[...], 0.0)
            for q in range(groups):
                part = pack_ref[pl.ds(q, tiles, stride=groups), :]
                out_ref[:, q, :] = jnp.dot(
                    sel, part, precision=lax.Precision.HIGHEST,
                    preferred_element_type=jnp.float32,
                ).astype(out_ref.dtype)

    full = lambda shape: pl.BlockSpec(shape, lambda i: (0,) * len(shape))
    outgoing = pl.pallas_call(
        match_kernel,
        grid=(strips,),
        in_specs=[pl.BlockSpec(memory_space=pltpu.SMEM), full(picks.shape)]
        + [full(x.shape) for x in pieces]
        + [full(taps.shape), full(owners.shape), full(weights.shape)],
        out_specs=full((band_count, groups, STRIP)),
        out_shape=jax.ShapeDtypeStruct((band_count, groups, STRIP), jnp.bfloat16),
        scratch_shapes=[
            pltpu.VMEM((ROWS, STRIP), jnp.float32),
            pltpu.VMEM((tiles * groups, STRIP), jnp.float32),
            pltpu.VMEM((NBASIS, ROWS, STRIP), jnp.float32),
            pltpu.VMEM((NBASIS, ROWS, STRIP), jnp.float32),
            pltpu.VMEM((span, NBASIS * STRIP), jnp.bfloat16),
            pltpu.VMEM((NBASIS, ROWS, span), jnp.bfloat16),
            pltpu.VMEM((lead_pad, wide_cols), jnp.bfloat16),
        ],
    )(params, picks, *pieces, taps, owners, weights)
    incoming = lax.all_to_all(outgoing, "ccd", split_axis=0, concat_axis=0, tiled=True)
    patch_sum = jnp.sum(incoming.astype(jnp.float32), axis=0, keepdims=True)
    return patch_sum.reshape(1, 1, TILE, TILE)


def solution(mesh):
    in_specs = (
        P("ccd", "section", None, None),
        P("ccd", "section", None),
        P("ccd", "section", None, None),
        P("ccd"),
        P(),
        P("ccd", "section", None, None),
        P("ccd", "section", None),
    )
    out_specs = P("section", "ccd", None, None)
    return jax.shard_map(shards, mesh=mesh, in_specs=in_specs, out_specs=out_specs, check_vma=False)
```

```python
import jax
import jax.numpy as jnp
from jax import lax
from jax.sharding import PartitionSpec as P
from jax.experimental import pallas as pl
from jax.experimental.pallas import tpu as pltpu

ROWS = 128
TILE = 32
STRIP = 128
KW = 21
NBASIS = 13
NPOLY = 6
HALF_K = 10
CH = 1024
REACH = 64


basis_sigma = (0.75, 0.75, 0.75, 0.75, 0.75, 0.75, 1.5, 1.5, 1.5, 1.5, 3.0, 3.0, 3.0)
column_power = (0, 1, 0, 2, 1, 0, 0, 1, 0, 1, 0, 1, 0)
row_power = (0, 0, 1, 0, 1, 2, 0, 0, 1, 1, 0, 0, 1)


def with_halo(array, sides, width):
    for axis, dim in sides:
        devices, length = (lax.axis_size(axis), array.shape[dim])
        up = [(i, (i + 1) % devices) for i in range(devices - 1)]
        down = [(j, i) for i, j in up]
        last = lax.slice_in_dim(array, length - width, length, axis=dim)
        leading = lax.slice_in_dim(array, 0, width, axis=dim)
        before = lax.ppermute(last, axis, up)
        after = lax.ppermute(leading, axis, down)
        array = jnp.concatenate([before, array, after], axis=dim)
    return array


def basis_taps(powers, sigmas=basis_sigma):
    offsets = jnp.arange(KW).astype(jnp.float32) - HALF_K
    sigma_col = jnp.array(sigmas, dtype=jnp.float32)[:, None]
    power_col = jnp.array(powers, dtype=jnp.int32)[:, None]
    spread = offsets[None, :]
    envelope = jnp.exp(-(spread * spread) / (2.0 * sigma_col * sigma_col))
    factor = jnp.where(power_col == 0, 1.0, jnp.where(power_col == 1, spread, spread * spread))
    shaped = envelope * factor
    scale = jnp.sqrt(jnp.sum(shaped * shaped, axis=1, keepdims=True))
    return (shaped / scale).astype(jnp.bfloat16)


def coefficients(terms, row_coord, col_coord):
    return (
        terms[0]
        + terms[1] * row_coord
        + terms[2] * col_coord
        + terms[3] * row_coord * row_coord
        + terms[4] * row_coord * col_coord
        + terms[5] * col_coord * col_coord
    )


def band_matrix(tap_table, inner_len):
    lead_idx = jnp.arange(inner_len + 2 * HALF_K)[:, None]
    trail_idx = jnp.arange(inner_len)[None, :]
    offset = lead_idx - trail_idx
    onehot = (offset[None] == jnp.arange(KW)[:, None, None]).astype(tap_table.dtype)
    band = jnp.einsum("kt,tai->kai", tap_table, onehot, preferred_element_type=jnp.float32)
    return band.astype(tap_table.dtype)


def shards(raw_counts, overscan, response, warp_rows, kernel_poly, tile_owner, tile_weight):
    band_count = lax.axis_size("ccd")
    halves = lax.axis_size("section")
    total_rows = ROWS * band_count
    total_cols = CH * halves
    top_row = lax.axis_index("ccd") * ROWS
    left_col = lax.axis_index("section") * CH
    half = lax.axis_index("section")
    strips = CH // STRIP
    wide_cols = strips * STRIP + STRIP
    rh = raw_counts.shape[2]
    calibrated = ((raw_counts - overscan[..., None]) * response).astype(jnp.bfloat16)[0, 0]
    shifts = (warp_rows - (top_row + jnp.arange(ROWS))).astype(jnp.bfloat16)
    my_shifts = lax.dynamic_slice_in_dim(shifts, half * rh, rh)[:, None]
    wide = jnp.pad(calibrated, ((0, 0), (HALF_K, HALF_K)))
    width = CH + 2 * HALF_K
    filler = jnp.zeros((rh, wide_cols - width - 1), jnp.bfloat16)

    def slab(col_start):
        cols = lax.dynamic_slice_in_dim(wide, col_start, width, 1)
        return jnp.concatenate([cols, my_shifts, filler], axis=1)

    own = slab(half * CH)
    other = slab((1 - half) * CH)
    nb = band_count
    axes = ("section", "ccd")
    swap = [(s * nb + b, (1 - s) * nb + b) for s in range(2) for b in range(nb)]
    got_swap = lax.ppermute(other, axes, swap)
    pick = lambda a, b: jnp.where(half == 0, a, b)
    first_rows = pick(own, got_swap)
    second_rows = pick(got_swap, own)
    rim = 16
    sent_up = jnp.concatenate([first_rows, second_rows[:rim]], axis=0)
    sent_down = jnp.concatenate([first_rows[rh - rim :], second_rows], axis=0)
    upward = [(b, b - 1) for b in range(1, nb)]
    downward = [(b, b + 1) for b in range(nb - 1)]
    mixed = [(x, y) for x, y in upward] + [(nb + x, nb + y) for x, y in downward]
    mirrored = [(x, y) for x, y in downward] + [(nb + x, nb + y) for x, y in upward]
    got_mixed = lax.ppermute(pick(sent_up, sent_down), axes, mixed)
    got_mirrored = lax.ppermute(pick(sent_down, sent_up), axes, mirrored)
    from_below = pick(got_mixed, got_mirrored)
    from_above = pick(got_mirrored, got_mixed)
    lead = ROWS + 2 * HALF_K
    lead_pad = -(-lead // 16) * 16
    above = rh + rim
    steps = jnp.concatenate(
        [
            from_above[above - HALF_K :, width],
            first_rows[:, width],
            second_rows[:, width],
            from_below[:HALF_K, width],
        ]
    ).astype(jnp.int32)
    origin = rim + REACH
    out_rows = top_row - HALF_K + jnp.arange(lead)
    inside = (out_rows >= 0) & (out_rows < total_rows)
    picks = jnp.where(inside, jnp.arange(lead) + origin - HALF_K + steps, -1)
    picks = jnp.pad(picks, (0, lead_pad - lead), constant_values=-1)[:, None]
    pieces = (got_mirrored, own, got_swap, got_mixed)
    bases = ((0, above + 2 * rh), (above, above + rh), (above + rh, above), (above + 2 * rh, 0))
    span = 2 * STRIP
    both_taps = basis_taps(column_power + row_power, basis_sigma + basis_sigma)
    taps = jnp.pad(both_taps.astype(jnp.float32), ((0, 0), (0, span - KW)))
    params = jnp.concatenate(
        [kernel_poly.reshape(-1), jnp.stack([top_row, left_col]).astype(jnp.float32)]
    )
    at = NBASIS * NPOLY
    owners = tile_owner.reshape(1, -1)
    weights = tile_weight.reshape(1, -1)
    groups = TILE * TILE // STRIP
    tiles = owners.shape[1]
    row_tiles = ROWS // TILE
    per_lane = STRIP // TILE

    def match_kernel(kp_ref, picks_ref, p0_ref, p1_ref, p2_ref, p3_ref,
                     tap_ref, own_ref, w_ref,
                     out_ref, acc_ref, pack_ref, a_ref, b_ref, colm_ref, rowm_ref, img_ref):
        i = pl.program_id(0)

        @pl.when(i == 0)
        def _():
            first = kp_ref[at + 1] == 0.0
            gathered = jnp.zeros((lead_pad, wide_cols), jnp.float32)
            piece_refs = (p0_ref, p1_ref, p2_ref, p3_ref)
            for ref, (b0, b1) in zip(piece_refs, bases):
                n = ref.shape[0]
                base = jnp.where(first, b0, b1)
                hit = lax.broadcasted_iota(jnp.int32, (lead_pad, n), 1) + base == picks_ref[...]
                gathered = gathered + jnp.dot(
                    hit.astype(jnp.bfloat16), ref[...], preferred_element_type=jnp.float32
                )
            img_ref[...] = gathered.astype(jnp.bfloat16)
            for k in range(NBASIS):
                spread = jnp.broadcast_to(tap_ref[pl.ds(k, 1), :], (STRIP, span))
                band_t = pltpu.roll(spread, 0, 1, stride=1, stride_axis=0)
                colm_ref[:, k * STRIP : (k + 1) * STRIP] = band_t.T.astype(jnp.bfloat16)
                spread = jnp.broadcast_to(tap_ref[pl.ds(NBASIS + k, 1), :], (ROWS, span))
                band = pltpu.roll(spread, 0, 1, stride=1, stride_axis=0)
                rowm_ref[k] = band.astype(jnp.bfloat16)
            rows = lax.broadcasted_iota(jnp.int32, (ROWS, STRIP), 0).astype(jnp.float32)
            u = 2.0 * (rows + kp_ref[at] + 0.5) / total_rows - 1.0
            for k in range(NBASIS):
                p = lambda m: kp_ref[k * NPOLY + m]
                a_ref[k] = p(0) + p(1) * u + p(3) * u * u
                b_ref[k] = p(2) + p(4) * u

        offset = pl.multiple_of(i * STRIP, STRIP)
        strip = img_ref[:, pl.ds(offset, span)]
        across = jnp.dot(strip, colm_ref[...], preferred_element_type=jnp.float32)
        across = across.astype(jnp.bfloat16)
        cols = lax.broadcasted_iota(jnp.int32, (1, STRIP), 1) + i * STRIP
        v = 2.0 * (cols.astype(jnp.float32) + kp_ref[at + 1] + 0.5) / total_cols - 1.0
        acc = jnp.zeros((ROWS, STRIP), jnp.float32)
        for k in range(NBASIS):
            vert = jnp.dot(
                rowm_ref[k, :, pl.ds(0, lead_pad)], across[:, k * STRIP : (k + 1) * STRIP],
                preferred_element_type=jnp.float32,
            )
            coef = a_ref[k] + v * (b_ref[k] + kp_ref[k * NPOLY + 5] * v)
            acc = acc + coef * vert
        acc_ref[...] = acc
        lane_group = lax.broadcasted_iota(jnp.int32, (groups, STRIP), 1) // TILE
        for rb in range(row_tiles):
            picked = [
                acc_ref[pl.ds(rb * TILE + g, groups, stride=per_lane), :] for g in range(per_lane)
            ]
            for cbl in range(per_lane):
                packed = jnp.zeros((groups, STRIP), jnp.float32)
                for g in range(per_lane):
                    shift = ((g - cbl) % per_lane) * TILE
                    rolled = pltpu.roll(picked[g], shift, 1) if shift else picked[g]
                    packed = jnp.where(lane_group == g, rolled, packed)
                j = (i * per_lane + cbl) * row_tiles + rb
                pack_ref[pl.ds(pl.multiple_of(j * groups, groups), groups), :] = packed

        @pl.when(i == strips - 1)
        def _():
            owner_ids = lax.broadcasted_iota(jnp.int32, (band_count, tiles), 0)
            sel = jnp.where(owner_ids == own_ref[...], w_ref[...], 0.0)
            for q in range(groups):
                part = pack_ref[pl.ds(q, tiles, stride=groups), :]
                out_ref[:, q, :] = jnp.dot(
                    sel, part, precision=lax.Precision.HIGHEST,
                    preferred_element_type=jnp.float32,
                ).astype(out_ref.dtype)

    full = lambda shape: pl.BlockSpec(shape, lambda i: (0,) * len(shape))
    outgoing = pl.pallas_call(
        match_kernel,
        grid=(strips,),
        in_specs=[pl.BlockSpec(memory_space=pltpu.SMEM), full(picks.shape)]
        + [full(x.shape) for x in pieces]
        + [full(taps.shape), full(owners.shape), full(weights.shape)],
        out_specs=full((band_count, groups, STRIP)),
        out_shape=jax.ShapeDtypeStruct((band_count, groups, STRIP), jnp.bfloat16),
        scratch_shapes=[
            pltpu.VMEM((ROWS, STRIP), jnp.float32),
            pltpu.VMEM((tiles * groups, STRIP), jnp.float32),
            pltpu.VMEM((NBASIS, ROWS, STRIP), jnp.float32),
            pltpu.VMEM((NBASIS, ROWS, STRIP), jnp.float32),
            pltpu.VMEM((span, NBASIS * STRIP), jnp.bfloat16),
            pltpu.VMEM((NBASIS, ROWS, span), jnp.bfloat16),
            pltpu.VMEM((lead_pad, wide_cols), jnp.bfloat16),
        ],
    )(params, picks, *pieces, taps, owners, weights)
    incoming = lax.all_to_all(outgoing, "ccd", split_axis=0, concat_axis=0, tiled=True)
    patch_sum = jnp.sum(incoming.astype(jnp.float32), axis=0, keepdims=True)
    return patch_sum.reshape(1, 1, TILE, TILE)


def solution(mesh):
    in_specs = (
        P("ccd", "section", None, None),
        P("ccd", "section", None),
        P("ccd", "section", None, None),
        P("ccd"),
        P(),
        P("ccd", "section", None, None),
        P("ccd", "section", None),
    )
    out_specs = P("section", "ccd", None, None)
    return jax.shard_map(shards, mesh=mesh, in_specs=in_specs, out_specs=out_specs, check_vma=False)
```

```python
import jax
import jax.numpy as jnp
from jax import lax
from jax.sharding import PartitionSpec as P
from jax.experimental import pallas as pl
from jax.experimental.pallas import tpu as pltpu

ROWS = 128
TILE = 32
STRIP = 128
KW = 21
NBASIS = 13
NPOLY = 6
HALF_K = 10
CH = 1024
REACH = 64


basis_sigma = (0.75, 0.75, 0.75, 0.75, 0.75, 0.75, 1.5, 1.5, 1.5, 1.5, 3.0, 3.0, 3.0)
column_power = (0, 1, 0, 2, 1, 0, 0, 1, 0, 1, 0, 1, 0)
row_power = (0, 0, 1, 0, 1, 2, 0, 0, 1, 1, 0, 0, 1)


def with_halo(array, sides, width):
    for axis, dim in sides:
        devices, length = (lax.axis_size(axis), array.shape[dim])
        up = [(i, (i + 1) % devices) for i in range(devices - 1)]
        down = [(j, i) for i, j in up]
        last = lax.slice_in_dim(array, length - width, length, axis=dim)
        leading = lax.slice_in_dim(array, 0, width, axis=dim)
        before = lax.ppermute(last, axis, up)
        after = lax.ppermute(leading, axis, down)
        array = jnp.concatenate([before, array, after], axis=dim)
    return array


def basis_taps(powers, sigmas=basis_sigma):
    offsets = jnp.arange(KW).astype(jnp.float32) - HALF_K
    sigma_col = jnp.array(sigmas, dtype=jnp.float32)[:, None]
    power_col = jnp.array(powers, dtype=jnp.int32)[:, None]
    spread = offsets[None, :]
    envelope = jnp.exp(-(spread * spread) / (2.0 * sigma_col * sigma_col))
    factor = jnp.where(power_col == 0, 1.0, jnp.where(power_col == 1, spread, spread * spread))
    shaped = envelope * factor
    scale = jnp.sqrt(jnp.sum(shaped * shaped, axis=1, keepdims=True))
    return (shaped / scale).astype(jnp.bfloat16)


def coefficients(terms, row_coord, col_coord):
    return (
        terms[0]
        + terms[1] * row_coord
        + terms[2] * col_coord
        + terms[3] * row_coord * row_coord
        + terms[4] * row_coord * col_coord
        + terms[5] * col_coord * col_coord
    )


def band_matrix(tap_table, inner_len):
    lead_idx = jnp.arange(inner_len + 2 * HALF_K)[:, None]
    trail_idx = jnp.arange(inner_len)[None, :]
    offset = lead_idx - trail_idx
    onehot = (offset[None] == jnp.arange(KW)[:, None, None]).astype(tap_table.dtype)
    band = jnp.einsum("kt,tai->kai", tap_table, onehot, preferred_element_type=jnp.float32)
    return band.astype(tap_table.dtype)


def shards(raw_counts, overscan, response, warp_rows, kernel_poly, tile_owner, tile_weight):
    band_count = lax.axis_size("ccd")
    halves = lax.axis_size("section")
    total_rows = ROWS * band_count
    total_cols = CH * halves
    top_row = lax.axis_index("ccd") * ROWS
    left_col = lax.axis_index("section") * CH
    half = lax.axis_index("section")
    strips = CH // STRIP
    wide_cols = strips * STRIP + STRIP
    rh = raw_counts.shape[2]
    calibrated = ((raw_counts - overscan[..., None]) * response).astype(jnp.bfloat16)[0, 0]
    shifts = (warp_rows - (top_row + jnp.arange(ROWS))).astype(jnp.bfloat16)
    my_shifts = lax.dynamic_slice_in_dim(shifts, half * rh, rh)[:, None]
    wide = jnp.pad(calibrated, ((0, 0), (HALF_K, HALF_K)))
    width = CH + 2 * HALF_K
    filler = jnp.zeros((rh, wide_cols - width - 1), jnp.bfloat16)

    def slab(col_start):
        cols = lax.dynamic_slice_in_dim(wide, col_start, width, 1)
        return jnp.concatenate([cols, my_shifts, filler], axis=1)

    own = slab(half * CH)
    other = slab((1 - half) * CH)
    nb = band_count
    axes = ("section", "ccd")
    swap = [(s * nb + b, (1 - s) * nb + b) for s in range(2) for b in range(nb)]
    got_swap = lax.ppermute(other, axes, swap)
    pick = lambda a, b: jnp.where(half == 0, a, b)
    first_rows = pick(own, got_swap)
    second_rows = pick(got_swap, own)
    rim = 16
    sent_up = jnp.concatenate([first_rows, second_rows[:rim]], axis=0)
    sent_down = jnp.concatenate([first_rows[rh - rim :], second_rows], axis=0)
    upward = [(b, b - 1) for b in range(1, nb)]
    downward = [(b, b + 1) for b in range(nb - 1)]
    mixed = [(x, y) for x, y in upward] + [(nb + x, nb + y) for x, y in downward]
    mirrored = [(x, y) for x, y in downward] + [(nb + x, nb + y) for x, y in upward]
    got_mixed = lax.ppermute(pick(sent_up, sent_down), axes, mixed)
    got_mirrored = lax.ppermute(pick(sent_down, sent_up), axes, mirrored)
    from_below = pick(got_mixed, got_mirrored)
    from_above = pick(got_mirrored, got_mixed)
    lead = ROWS + 2 * HALF_K
    lead_pad = -(-lead // 16) * 16
    above = rh + rim
    steps = jnp.concatenate(
        [
            from_above[above - HALF_K :, width],
            first_rows[:, width],
            second_rows[:, width],
            from_below[:HALF_K, width],
        ]
    ).astype(jnp.int32)
    origin = rim + REACH
    out_rows = top_row - HALF_K + jnp.arange(lead)
    inside = (out_rows >= 0) & (out_rows < total_rows)
    picks = jnp.where(inside, jnp.arange(lead) + origin - HALF_K + steps, -1)
    picks = jnp.pad(picks, (0, lead_pad - lead), constant_values=-1)[None, :]
    pieces = (got_mirrored, own, got_swap, got_mixed)
    bases = ((0, above + 2 * rh), (above, above + rh), (above + rh, above), (above + 2 * rh, 0))
    span = 2 * STRIP
    both_taps = basis_taps(column_power + row_power, basis_sigma + basis_sigma)
    taps = jnp.pad(both_taps.astype(jnp.float32), ((0, 0), (0, span - KW)))
    params = jnp.concatenate(
        [kernel_poly.reshape(-1), jnp.stack([top_row, left_col]).astype(jnp.float32)]
    )
    at = NBASIS * NPOLY
    owners = tile_owner.reshape(1, -1)
    weights = tile_weight.reshape(1, -1)
    groups = TILE * TILE // STRIP
    tiles = owners.shape[1]
    row_tiles = ROWS // TILE
    per_lane = STRIP // TILE

    def match_kernel(kp_ref, picks_ref, p0_ref, p1_ref, p2_ref, p3_ref,
                     tap_ref, own_ref, w_ref,
                     out_ref, acc_ref, pack_ref, a_ref, b_ref, colm_ref, rowm_ref, img_ref):
        i = pl.program_id(0)

        @pl.when(i == 0)
        def _():
            first = kp_ref[at + 1] == 0.0
            gathered = jnp.zeros((lead_pad, wide_cols), jnp.float32)
            piece_refs = (p0_ref, p1_ref, p2_ref, p3_ref)
            for ref, (b0, b1) in zip(piece_refs, bases):
                n = ref.shape[0]
                base = jnp.where(first, b0, b1)
                hit = lax.broadcasted_iota(jnp.int32, (n, lead_pad), 0) + base == picks_ref[...]
                gathered = gathered + lax.dot_general(
                    hit.astype(jnp.bfloat16), ref[...], (((0,), (0,)), ((), ())),
                    preferred_element_type=jnp.float32,
                )
            img_ref[...] = gathered.astype(jnp.bfloat16)
            for k in range(NBASIS):
                spread = jnp.broadcast_to(tap_ref[pl.ds(k, 1), :], (STRIP, span))
                band_t = pltpu.roll(spread, 0, 1, stride=1, stride_axis=0)
                colm_ref[:, k * STRIP : (k + 1) * STRIP] = band_t.T.astype(jnp.bfloat16)
                spread = jnp.broadcast_to(tap_ref[pl.ds(NBASIS + k, 1), :], (ROWS, span))
                band = pltpu.roll(spread, 0, 1, stride=1, stride_axis=0)
                rowm_ref[k] = band.astype(jnp.bfloat16)
            rows = lax.broadcasted_iota(jnp.int32, (ROWS, STRIP), 0).astype(jnp.float32)
            u = 2.0 * (rows + kp_ref[at] + 0.5) / total_rows - 1.0
            for k in range(NBASIS):
                p = lambda m: kp_ref[k * NPOLY + m]
                a_ref[k] = p(0) + p(1) * u + p(3) * u * u
                b_ref[k] = p(2) + p(4) * u

        offset = pl.multiple_of(i * STRIP, STRIP)
        strip = img_ref[:, pl.ds(offset, span)]
        across = jnp.dot(strip, colm_ref[...], preferred_element_type=jnp.float32)
        across = across.astype(jnp.bfloat16)
        cols = lax.broadcasted_iota(jnp.int32, (1, STRIP), 1) + i * STRIP
        v = 2.0 * (cols.astype(jnp.float32) + kp_ref[at + 1] + 0.5) / total_cols - 1.0
        acc = jnp.zeros((ROWS, STRIP), jnp.float32)
        for k in range(NBASIS):
            vert = jnp.dot(
                rowm_ref[k, :, pl.ds(0, lead_pad)], across[:, k * STRIP : (k + 1) * STRIP],
                preferred_element_type=jnp.float32,
            )
            coef = a_ref[k] + v * (b_ref[k] + kp_ref[k * NPOLY + 5] * v)
            acc = acc + coef * vert
        acc_ref[...] = acc
        lane_group = lax.broadcasted_iota(jnp.int32, (groups, STRIP), 1) // TILE
        for rb in range(row_tiles):
            picked = [
                acc_ref[pl.ds(rb * TILE + g, groups, stride=per_lane), :] for g in range(per_lane)
            ]
            for cbl in range(per_lane):
                packed = jnp.zeros((groups, STRIP), jnp.float32)
                for g in range(per_lane):
                    shift = ((g - cbl) % per_lane) * TILE
                    rolled = pltpu.roll(picked[g], shift, 1) if shift else picked[g]
                    packed = jnp.where(lane_group == g, rolled, packed)
                j = (i * per_lane + cbl) * row_tiles + rb
                pack_ref[pl.ds(pl.multiple_of(j * groups, groups), groups), :] = packed

        @pl.when(i == strips - 1)
        def _():
            owner_ids = lax.broadcasted_iota(jnp.int32, (band_count, tiles), 0)
            sel = jnp.where(owner_ids == own_ref[...], w_ref[...], 0.0)
            for q in range(groups):
                part = pack_ref[pl.ds(q, tiles, stride=groups), :]
                out_ref[:, q, :] = jnp.dot(
                    sel, part, precision=lax.Precision.HIGHEST,
                    preferred_element_type=jnp.float32,
                ).astype(out_ref.dtype)

    full = lambda shape: pl.BlockSpec(shape, lambda i: (0,) * len(shape))
    outgoing = pl.pallas_call(
        match_kernel,
        grid=(strips,),
        in_specs=[pl.BlockSpec(memory_space=pltpu.SMEM), full(picks.shape)]
        + [full(x.shape) for x in pieces]
        + [full(taps.shape), full(owners.shape), full(weights.shape)],
        out_specs=full((band_count, groups, STRIP)),
        out_shape=jax.ShapeDtypeStruct((band_count, groups, STRIP), jnp.bfloat16),
        scratch_shapes=[
            pltpu.VMEM((ROWS, STRIP), jnp.float32),
            pltpu.VMEM((tiles * groups, STRIP), jnp.float32),
            pltpu.VMEM((NBASIS, ROWS, STRIP), jnp.float32),
            pltpu.VMEM((NBASIS, ROWS, STRIP), jnp.float32),
            pltpu.VMEM((span, NBASIS * STRIP), jnp.bfloat16),
            pltpu.VMEM((NBASIS, ROWS, span), jnp.bfloat16),
            pltpu.VMEM((lead_pad, wide_cols), jnp.bfloat16),
        ],
    )(params, picks, *pieces, taps, owners, weights)
    incoming = lax.all_to_all(outgoing, "ccd", split_axis=0, concat_axis=0, tiled=True)
    patch_sum = jnp.sum(incoming.astype(jnp.float32), axis=0, keepdims=True)
    return patch_sum.reshape(1, 1, TILE, TILE)


def solution(mesh):
    in_specs = (
        P("ccd", "section", None, None),
        P("ccd", "section", None),
        P("ccd", "section", None, None),
        P("ccd"),
        P(),
        P("ccd", "section", None, None),
        P("ccd", "section", None),
    )
    out_specs = P("section", "ccd", None, None)
    return jax.shard_map(shards, mesh=mesh, in_specs=in_specs, out_specs=out_specs, check_vma=False)
```

```python
import jax
import jax.numpy as jnp
from jax import lax
from jax.sharding import PartitionSpec as P
from jax.experimental import pallas as pl
from jax.experimental.pallas import tpu as pltpu

ROWS = 128
TILE = 32
STRIP = 128
KW = 21
NBASIS = 13
NPOLY = 6
HALF_K = 10
CH = 1024
REACH = 64


basis_sigma = (0.75, 0.75, 0.75, 0.75, 0.75, 0.75, 1.5, 1.5, 1.5, 1.5, 3.0, 3.0, 3.0)
column_power = (0, 1, 0, 2, 1, 0, 0, 1, 0, 1, 0, 1, 0)
row_power = (0, 0, 1, 0, 1, 2, 0, 0, 1, 1, 0, 0, 1)


def with_halo(array, sides, width):
    for axis, dim in sides:
        devices, length = (lax.axis_size(axis), array.shape[dim])
        up = [(i, (i + 1) % devices) for i in range(devices - 1)]
        down = [(j, i) for i, j in up]
        last = lax.slice_in_dim(array, length - width, length, axis=dim)
        leading = lax.slice_in_dim(array, 0, width, axis=dim)
        before = lax.ppermute(last, axis, up)
        after = lax.ppermute(leading, axis, down)
        array = jnp.concatenate([before, array, after], axis=dim)
    return array


def basis_taps(powers, sigmas=basis_sigma):
    offsets = jnp.arange(KW).astype(jnp.float32) - HALF_K
    sigma_col = jnp.array(sigmas, dtype=jnp.float32)[:, None]
    power_col = jnp.array(powers, dtype=jnp.int32)[:, None]
    spread = offsets[None, :]
    envelope = jnp.exp(-(spread * spread) / (2.0 * sigma_col * sigma_col))
    factor = jnp.where(power_col == 0, 1.0, jnp.where(power_col == 1, spread, spread * spread))
    shaped = envelope * factor
    scale = jnp.sqrt(jnp.sum(shaped * shaped, axis=1, keepdims=True))
    return (shaped / scale).astype(jnp.bfloat16)


def coefficients(terms, row_coord, col_coord):
    return (
        terms[0]
        + terms[1] * row_coord
        + terms[2] * col_coord
        + terms[3] * row_coord * row_coord
        + terms[4] * row_coord * col_coord
        + terms[5] * col_coord * col_coord
    )


def band_matrix(tap_table, inner_len):
    lead_idx = jnp.arange(inner_len + 2 * HALF_K)[:, None]
    trail_idx = jnp.arange(inner_len)[None, :]
    offset = lead_idx - trail_idx
    onehot = (offset[None] == jnp.arange(KW)[:, None, None]).astype(tap_table.dtype)
    band = jnp.einsum("kt,tai->kai", tap_table, onehot, preferred_element_type=jnp.float32)
    return band.astype(tap_table.dtype)


def shards(raw_counts, overscan, response, warp_rows, kernel_poly, tile_owner, tile_weight):
    band_count = lax.axis_size("ccd")
    halves = lax.axis_size("section")
    total_rows = ROWS * band_count
    total_cols = CH * halves
    top_row = lax.axis_index("ccd") * ROWS
    left_col = lax.axis_index("section") * CH
    half = lax.axis_index("section")
    strips = CH // STRIP
    wide_cols = strips * STRIP + STRIP
    rh = raw_counts.shape[2]
    calibrated = ((raw_counts - overscan[..., None]) * response).astype(jnp.bfloat16)[0, 0]
    shifts = (warp_rows - (top_row + jnp.arange(ROWS))).astype(jnp.bfloat16)
    my_shifts = lax.dynamic_slice_in_dim(shifts, half * rh, rh)[:, None]
    wide = jnp.pad(calibrated, ((0, 0), (HALF_K, HALF_K)))
    width = CH + 2 * HALF_K
    filler = jnp.zeros((rh, wide_cols - width - 1), jnp.bfloat16)

    def slab(col_start):
        cols = lax.dynamic_slice_in_dim(wide, col_start, width, 1)
        return jnp.concatenate([cols, my_shifts, filler], axis=1)

    own = slab(half * CH)
    other = slab((1 - half) * CH)
    nb = band_count
    axes = ("section", "ccd")
    swap = [(s * nb + b, (1 - s) * nb + b) for s in range(2) for b in range(nb)]
    got_swap = lax.ppermute(other, axes, swap)
    pick = lambda a, b: jnp.where(half == 0, a, b)
    first_rows = pick(own, got_swap)
    second_rows = pick(got_swap, own)
    rim = 16
    sent_up = jnp.concatenate([first_rows, second_rows[:rim]], axis=0)
    sent_down = jnp.concatenate([first_rows[rh - rim :], second_rows], axis=0)
    upward = [(b, b - 1) for b in range(1, nb)]
    downward = [(b, b + 1) for b in range(nb - 1)]
    mixed = [(x, y) for x, y in upward] + [(nb + x, nb + y) for x, y in downward]
    mirrored = [(x, y) for x, y in downward] + [(nb + x, nb + y) for x, y in upward]
    got_mixed = lax.ppermute(pick(sent_up, sent_down), axes, mixed)
    got_mirrored = lax.ppermute(pick(sent_down, sent_up), axes, mirrored)
    from_below = pick(got_mixed, got_mirrored)
    from_above = pick(got_mirrored, got_mixed)
    lead = ROWS + 2 * HALF_K
    lead_pad = -(-lead // 16) * 16
    above = rh + rim
    steps = jnp.concatenate(
        [
            from_above[above - HALF_K :, width],
            first_rows[:, width],
            second_rows[:, width],
            from_below[:HALF_K, width],
        ]
    ).astype(jnp.int32)
    origin = rim + REACH
    out_rows = top_row - HALF_K + jnp.arange(lead)
    inside = (out_rows >= 0) & (out_rows < total_rows)
    picks = jnp.where(inside, jnp.arange(lead) + origin - HALF_K + steps, -1)
    picks = jnp.pad(picks, (0, lead_pad - lead), constant_values=-1)[None, :]
    pieces = (got_mirrored, own, got_swap, got_mixed)
    bases = ((0, above + 2 * rh), (above, above + rh), (above + rh, above), (above + 2 * rh, 0))
    span = 2 * STRIP
    both_taps = basis_taps(column_power + row_power, basis_sigma + basis_sigma)
    taps = jnp.pad(both_taps.astype(jnp.float32), ((0, 0), (0, span - KW)))
    params = jnp.concatenate(
        [kernel_poly.reshape(-1), jnp.stack([top_row, left_col]).astype(jnp.float32)]
    )
    at = NBASIS * NPOLY
    owners = tile_owner.reshape(1, -1)
    weights = tile_weight.reshape(1, -1)
    groups = TILE * TILE // STRIP
    tiles = owners.shape[1]
    row_tiles = ROWS // TILE
    per_lane = STRIP // TILE

    def match_kernel(kp_ref, picks_ref, p0_ref, p1_ref, p2_ref, p3_ref,
                     tap_ref, own_ref, w_ref,
                     out_ref, acc_ref, pack_ref, a_ref, b_ref, colm_ref, rowm_ref, img_ref):
        i = pl.program_id(0)

        @pl.when(i == 0)
        def _():
            first = kp_ref[at + 1] == 0.0
            gathered = jnp.zeros((lead_pad, wide_cols), jnp.float32)
            piece_refs = (p0_ref, p1_ref, p2_ref, p3_ref)
            for ref, (b0, b1) in zip(piece_refs, bases):
                n = ref.shape[0]
                base = jnp.where(first, b0, b1)
                hit = lax.broadcasted_iota(jnp.int32, (n, lead_pad), 0) + base == picks_ref[...]
                gathered = gathered + lax.dot_general(
                    hit.astype(jnp.bfloat16), ref[...], (((0,), (0,)), ((), ())),
                    preferred_element_type=jnp.float32,
                )
            img_ref[...] = gathered.astype(jnp.bfloat16)
            for k in range(NBASIS):
                spread = jnp.broadcast_to(tap_ref[pl.ds(k, 1), :], (STRIP, span))
                band_t = pltpu.roll(spread, 0, 1, stride=1, stride_axis=0)
                colm_ref[:, k * STRIP : (k + 1) * STRIP] = band_t.T.astype(jnp.bfloat16)
                spread = jnp.broadcast_to(tap_ref[pl.ds(NBASIS + k, 1), :], (ROWS, span))
                band = pltpu.roll(spread, 0, 1, stride=1, stride_axis=0)
                rowm_ref[k] = band.astype(jnp.bfloat16)
            rows = lax.broadcasted_iota(jnp.int32, (ROWS, STRIP), 0).astype(jnp.float32)
            u = 2.0 * (rows + kp_ref[at] + 0.5) / total_rows - 1.0
            for k in range(NBASIS):
                p = lambda m: kp_ref[k * NPOLY + m]
                a_ref[k] = p(0) + p(1) * u + p(3) * u * u
                b_ref[k] = p(2) + p(4) * u

        offset = pl.multiple_of(i * STRIP, STRIP)
        strip = img_ref[:, pl.ds(offset, span)]
        across = jnp.dot(strip, colm_ref[...], preferred_element_type=jnp.float32)
        across = across.astype(jnp.bfloat16)
        cols = lax.broadcasted_iota(jnp.int32, (1, STRIP), 1) + i * STRIP
        v = 2.0 * (cols.astype(jnp.float32) + kp_ref[at + 1] + 0.5) / total_cols - 1.0
        acc = jnp.zeros((ROWS, STRIP), jnp.float32)
        for k in range(NBASIS):
            vert = jnp.dot(
                rowm_ref[k, :, pl.ds(0, lead_pad)], across[:, k * STRIP : (k + 1) * STRIP],
                preferred_element_type=jnp.float32,
            )
            coef = a_ref[k] + v * (b_ref[k] + kp_ref[k * NPOLY + 5] * v)
            acc = acc + coef * vert
        acc_ref[...] = acc
        lane_group = lax.broadcasted_iota(jnp.int32, (groups, STRIP), 1) // TILE
        for rb in range(row_tiles):
            picked = [
                acc_ref[pl.ds(rb * TILE + g, groups, stride=per_lane), :] for g in range(per_lane)
            ]
            for cbl in range(per_lane):
                packed = jnp.zeros((groups, STRIP), jnp.float32)
                for g in range(per_lane):
                    shift = ((g - cbl) % per_lane) * TILE
                    rolled = pltpu.roll(picked[g], shift, 1) if shift else picked[g]
                    packed = jnp.where(lane_group == g, rolled, packed)
                j = (i * per_lane + cbl) * row_tiles + rb
                pack_ref[pl.ds(pl.multiple_of(j * groups, groups), groups), :] = packed

        @pl.when(i == strips - 1)
        def _():
            owner_ids = lax.broadcasted_iota(jnp.int32, (band_count, tiles), 0)
            sel = jnp.where(owner_ids == own_ref[...], w_ref[...], 0.0)
            for q in range(groups):
                part = pack_ref[pl.ds(q, tiles, stride=groups), :]
                out_ref[:, q, :] = jnp.dot(
                    sel, part, precision=lax.Precision.HIGHEST,
                    preferred_element_type=jnp.float32,
                ).astype(out_ref.dtype)

    full = lambda shape: pl.BlockSpec(shape, lambda i: (0,) * len(shape))
    outgoing = pl.pallas_call(
        match_kernel,
        grid=(strips,),
        in_specs=[pl.BlockSpec(memory_space=pltpu.SMEM), full(picks.shape)]
        + [full(x.shape) for x in pieces]
        + [full(taps.shape), full(owners.shape), full(weights.shape)],
        out_specs=full((band_count, groups, STRIP)),
        out_shape=jax.ShapeDtypeStruct((band_count, groups, STRIP), jnp.float32),
        scratch_shapes=[
            pltpu.VMEM((ROWS, STRIP), jnp.float32),
            pltpu.VMEM((tiles * groups, STRIP), jnp.float32),
            pltpu.VMEM((NBASIS, ROWS, STRIP), jnp.float32),
            pltpu.VMEM((NBASIS, ROWS, STRIP), jnp.float32),
            pltpu.VMEM((span, NBASIS * STRIP), jnp.bfloat16),
            pltpu.VMEM((NBASIS, ROWS, span), jnp.bfloat16),
            pltpu.VMEM((lead_pad, wide_cols), jnp.bfloat16),
        ],
    )(params, picks, *pieces, taps, owners, weights)
    incoming = lax.all_to_all(outgoing, "ccd", split_axis=0, concat_axis=0, tiled=True)
    patch_sum = jnp.sum(incoming.astype(jnp.float32), axis=0, keepdims=True)
    return patch_sum.reshape(1, 1, TILE, TILE)


def solution(mesh):
    in_specs = (
        P("ccd", "section", None, None),
        P("ccd", "section", None),
        P("ccd", "section", None, None),
        P("ccd"),
        P(),
        P("ccd", "section", None, None),
        P("ccd", "section", None),
    )
    out_specs = P("section", "ccd", None, None)
    return jax.shard_map(shards, mesh=mesh, in_specs=in_specs, out_specs=out_specs, check_vma=False)
```

```python
import jax
import jax.numpy as jnp
from jax import lax
from jax.sharding import PartitionSpec as P
from jax.experimental import pallas as pl
from jax.experimental.pallas import tpu as pltpu

ROWS = 128
TILE = 32
STRIP = 128
KW = 21
NBASIS = 13
NPOLY = 6
HALF_K = 10
CH = 1024
REACH = 64


basis_sigma = (0.75, 0.75, 0.75, 0.75, 0.75, 0.75, 1.5, 1.5, 1.5, 1.5, 3.0, 3.0, 3.0)
column_power = (0, 1, 0, 2, 1, 0, 0, 1, 0, 1, 0, 1, 0)
row_power = (0, 0, 1, 0, 1, 2, 0, 0, 1, 1, 0, 0, 1)


def with_halo(array, sides, width):
    for axis, dim in sides:
        devices, length = (lax.axis_size(axis), array.shape[dim])
        up = [(i, (i + 1) % devices) for i in range(devices - 1)]
        down = [(j, i) for i, j in up]
        last = lax.slice_in_dim(array, length - width, length, axis=dim)
        leading = lax.slice_in_dim(array, 0, width, axis=dim)
        before = lax.ppermute(last, axis, up)
        after = lax.ppermute(leading, axis, down)
        array = jnp.concatenate([before, array, after], axis=dim)
    return array


def basis_taps(powers, sigmas=basis_sigma):
    offsets = jnp.arange(KW).astype(jnp.float32) - HALF_K
    sigma_col = jnp.array(sigmas, dtype=jnp.float32)[:, None]
    power_col = jnp.array(powers, dtype=jnp.int32)[:, None]
    spread = offsets[None, :]
    envelope = jnp.exp(-(spread * spread) / (2.0 * sigma_col * sigma_col))
    factor = jnp.where(power_col == 0, 1.0, jnp.where(power_col == 1, spread, spread * spread))
    shaped = envelope * factor
    scale = jnp.sqrt(jnp.sum(shaped * shaped, axis=1, keepdims=True))
    return (shaped / scale).astype(jnp.bfloat16)


def coefficients(terms, row_coord, col_coord):
    return (
        terms[0]
        + terms[1] * row_coord
        + terms[2] * col_coord
        + terms[3] * row_coord * row_coord
        + terms[4] * row_coord * col_coord
        + terms[5] * col_coord * col_coord
    )


def band_matrix(tap_table, inner_len):
    lead_idx = jnp.arange(inner_len + 2 * HALF_K)[:, None]
    trail_idx = jnp.arange(inner_len)[None, :]
    offset = lead_idx - trail_idx
    onehot = (offset[None] == jnp.arange(KW)[:, None, None]).astype(tap_table.dtype)
    band = jnp.einsum("kt,tai->kai", tap_table, onehot, preferred_element_type=jnp.float32)
    return band.astype(tap_table.dtype)


def shards(raw_counts, overscan, response, warp_rows, kernel_poly, tile_owner, tile_weight):
    band_count = lax.axis_size("ccd")
    halves = lax.axis_size("section")
    total_rows = ROWS * band_count
    total_cols = CH * halves
    top_row = lax.axis_index("ccd") * ROWS
    left_col = lax.axis_index("section") * CH
    half = lax.axis_index("section")
    strips = CH // STRIP
    wide_cols = strips * STRIP + STRIP
    rh = raw_counts.shape[2]
    calibrated = ((raw_counts - overscan[..., None]) * response).astype(jnp.bfloat16)[0, 0]
    shifts = (warp_rows - (top_row + jnp.arange(ROWS))).astype(jnp.bfloat16)
    my_shifts = lax.dynamic_slice_in_dim(shifts, half * rh, rh)[:, None]
    wide = jnp.pad(calibrated, ((0, 0), (HALF_K, HALF_K)))
    width = CH + 2 * HALF_K
    filler = jnp.zeros((rh, wide_cols - width - 1), jnp.bfloat16)

    def slab(col_start):
        cols = lax.dynamic_slice_in_dim(wide, col_start, width, 1)
        return jnp.concatenate([cols, my_shifts, filler], axis=1)

    own = slab(half * CH)
    other = slab((1 - half) * CH)
    nb = band_count
    axes = ("section", "ccd")
    swap = [(s * nb + b, (1 - s) * nb + b) for s in range(2) for b in range(nb)]
    got_swap = lax.ppermute(other, axes, swap)
    pick = lambda a, b: jnp.where(half == 0, a, b)
    first_rows = pick(own, got_swap)
    second_rows = pick(got_swap, own)
    rim = 16
    sent_up = jnp.concatenate([first_rows, second_rows[:rim]], axis=0)
    sent_down = jnp.concatenate([first_rows[rh - rim :], second_rows], axis=0)
    upward = [(b, b - 1) for b in range(1, nb)]
    downward = [(b, b + 1) for b in range(nb - 1)]
    mixed = [(x, y) for x, y in upward] + [(nb + x, nb + y) for x, y in downward]
    mirrored = [(x, y) for x, y in downward] + [(nb + x, nb + y) for x, y in upward]
    got_mixed = lax.ppermute(pick(sent_up, sent_down), axes, mixed)
    got_mirrored = lax.ppermute(pick(sent_down, sent_up), axes, mirrored)
    from_below = pick(got_mixed, got_mirrored)
    from_above = pick(got_mirrored, got_mixed)
    lead = ROWS + 2 * HALF_K
    lead_pad = -(-lead // 16) * 16
    above = rh + rim
    steps = jnp.concatenate(
        [
            from_above[above - HALF_K :, width],
            first_rows[:, width],
            second_rows[:, width],
            from_below[:HALF_K, width],
        ]
    ).astype(jnp.int32)
    origin = rim + REACH
    out_rows = top_row - HALF_K + jnp.arange(lead)
    inside = (out_rows >= 0) & (out_rows < total_rows)
    picks = jnp.where(inside, jnp.arange(lead) + origin - HALF_K + steps, -1)
    picks = jnp.pad(picks, (0, lead_pad - lead), constant_values=-1)[None, :]
    pieces = (got_mirrored, own, got_swap, got_mixed)
    bases = ((0, above + 2 * rh), (above, above + rh), (above + rh, above), (above + 2 * rh, 0))
    span = 2 * STRIP
    both_taps = basis_taps(column_power + row_power, basis_sigma + basis_sigma)
    taps = jnp.pad(both_taps.astype(jnp.float32), ((0, 0), (0, span - KW)))
    params = jnp.concatenate(
        [kernel_poly.reshape(-1), jnp.stack([top_row, left_col]).astype(jnp.float32)]
    )
    at = NBASIS * NPOLY
    owners = tile_owner.reshape(1, -1)
    weights = tile_weight.reshape(1, -1)
    groups = TILE * TILE // STRIP
    tiles = owners.shape[1]
    row_tiles = ROWS // TILE
    per_lane = STRIP // TILE

    def setup_kernel(kp_ref, tap_ref, colm_ref, rowm_ref, a_ref, b_ref):
        for k in range(NBASIS):
            spread = jnp.broadcast_to(tap_ref[pl.ds(k, 1), :], (STRIP, span))
            band_t = pltpu.roll(spread, 0, 1, stride=1, stride_axis=0)
            colm_ref[:, k * STRIP : (k + 1) * STRIP] = band_t.T.astype(jnp.bfloat16)
            spread = jnp.broadcast_to(tap_ref[pl.ds(NBASIS + k, 1), :], (ROWS, span))
            band = pltpu.roll(spread, 0, 1, stride=1, stride_axis=0)
            rowm_ref[k] = band.astype(jnp.bfloat16)
        rows = lax.broadcasted_iota(jnp.int32, (ROWS, STRIP), 0).astype(jnp.float32)
        u = 2.0 * (rows + kp_ref[at] + 0.5) / total_rows - 1.0
        for k in range(NBASIS):
            p = lambda m: kp_ref[k * NPOLY + m]
            a_ref[k] = p(0) + p(1) * u + p(3) * u * u
            b_ref[k] = p(2) + p(4) * u

    colm, rowm, a_tab, b_tab = pl.pallas_call(
        setup_kernel,
        in_specs=[pl.BlockSpec(memory_space=pltpu.SMEM), pl.BlockSpec(memory_space=pltpu.VMEM)],
        out_shape=(
            jax.ShapeDtypeStruct((span, NBASIS * STRIP), jnp.bfloat16),
            jax.ShapeDtypeStruct((NBASIS, ROWS, span), jnp.bfloat16),
            jax.ShapeDtypeStruct((NBASIS, ROWS, STRIP), jnp.float32),
            jax.ShapeDtypeStruct((NBASIS, ROWS, STRIP), jnp.float32),
        ),
    )(params, taps)

    def match_kernel(kp_ref, picks_ref, p0_ref, p1_ref, p2_ref, p3_ref,
                     colm_ref, rowm_ref, a_ref, b_ref, own_ref, w_ref,
                     out_ref, acc_ref, pack_ref, img_ref):
        i = pl.program_id(0)

        @pl.when(i == 0)
        def _():
            first = kp_ref[at + 1] == 0.0
            gathered = jnp.zeros((lead_pad, wide_cols), jnp.float32)
            piece_refs = (p0_ref, p1_ref, p2_ref, p3_ref)
            for ref, (b0, b1) in zip(piece_refs, bases):
                n = ref.shape[0]
                base = jnp.where(first, b0, b1)
                hit = lax.broadcasted_iota(jnp.int32, (n, lead_pad), 0) + base == picks_ref[...]
                gathered = gathered + lax.dot_general(
                    hit.astype(jnp.bfloat16), ref[...], (((0,), (0,)), ((), ())),
                    preferred_element_type=jnp.float32,
                )
            img_ref[...] = gathered.astype(jnp.bfloat16)

        offset = pl.multiple_of(i * STRIP, STRIP)
        strip = img_ref[:, pl.ds(offset, span)]
        across = jnp.dot(strip, colm_ref[...], preferred_element_type=jnp.float32)
        across = across.astype(jnp.bfloat16)
        cols = lax.broadcasted_iota(jnp.int32, (1, STRIP), 1) + i * STRIP
        v = 2.0 * (cols.astype(jnp.float32) + kp_ref[at + 1] + 0.5) / total_cols - 1.0
        acc = jnp.zeros((ROWS, STRIP), jnp.float32)
        for k in range(NBASIS):
            vert = jnp.dot(
                rowm_ref[k, :, pl.ds(0, lead_pad)], across[:, k * STRIP : (k + 1) * STRIP],
                preferred_element_type=jnp.float32,
            )
            coef = a_ref[k] + v * (b_ref[k] + kp_ref[k * NPOLY + 5] * v)
            acc = acc + coef * vert
        acc_ref[...] = acc
        lane_group = lax.broadcasted_iota(jnp.int32, (groups, STRIP), 1) // TILE
        for rb in range(row_tiles):
            picked = [
                acc_ref[pl.ds(rb * TILE + g, groups, stride=per_lane), :] for g in range(per_lane)
            ]
            for cbl in range(per_lane):
                packed = jnp.zeros((groups, STRIP), jnp.float32)
                for g in range(per_lane):
                    shift = ((g - cbl) % per_lane) * TILE
                    rolled = pltpu.roll(picked[g], shift, 1) if shift else picked[g]
                    packed = jnp.where(lane_group == g, rolled, packed)
                j = (i * per_lane + cbl) * row_tiles + rb
                pack_ref[pl.ds(pl.multiple_of(j * groups, groups), groups), :] = packed

        @pl.when(i == strips - 1)
        def _():
            owner_ids = lax.broadcasted_iota(jnp.int32, (band_count, tiles), 0)
            sel = jnp.where(owner_ids == own_ref[...], w_ref[...], 0.0)
            for q in range(groups):
                part = pack_ref[pl.ds(q, tiles, stride=groups), :]
                out_ref[:, q, :] = jnp.dot(
                    sel, part, precision=lax.Precision.HIGHEST,
                    preferred_element_type=jnp.float32,
                ).astype(out_ref.dtype)

    full = lambda shape: pl.BlockSpec(shape, lambda i: (0,) * len(shape))
    outgoing = pl.pallas_call(
        match_kernel,
        grid=(strips,),
        in_specs=[pl.BlockSpec(memory_space=pltpu.SMEM), full(picks.shape)]
        + [full(x.shape) for x in pieces]
        + [full(colm.shape), full(rowm.shape), full(a_tab.shape), full(b_tab.shape)]
        + [full(owners.shape), full(weights.shape)],
        out_specs=full((band_count, groups, STRIP)),
        out_shape=jax.ShapeDtypeStruct((band_count, groups, STRIP), jnp.bfloat16),
        scratch_shapes=[
            pltpu.VMEM((ROWS, STRIP), jnp.float32),
            pltpu.VMEM((tiles * groups, STRIP), jnp.float32),
            pltpu.VMEM((lead_pad, wide_cols), jnp.bfloat16),
        ],
    )(params, picks, *pieces, colm, rowm, a_tab, b_tab, owners, weights)
    incoming = lax.all_to_all(outgoing, "ccd", split_axis=0, concat_axis=0, tiled=True)
    patch_sum = jnp.sum(incoming.astype(jnp.float32), axis=0, keepdims=True)
    return patch_sum.reshape(1, 1, TILE, TILE)


def solution(mesh):
    in_specs = (
        P("ccd", "section", None, None),
        P("ccd", "section", None),
        P("ccd", "section", None, None),
        P("ccd"),
        P(),
        P("ccd", "section", None, None),
        P("ccd", "section", None),
    )
    out_specs = P("section", "ccd", None, None)
    return jax.shard_map(shards, mesh=mesh, in_specs=in_specs, out_specs=out_specs, check_vma=False)
```

```python
import jax
import jax.numpy as jnp
from jax import lax
from jax.sharding import PartitionSpec as P
from jax.experimental import pallas as pl
from jax.experimental.pallas import tpu as pltpu

ROWS = 128
TILE = 32
STRIP = 128
KW = 21
NBASIS = 13
NPOLY = 6
HALF_K = 10
CH = 1024
REACH = 64


basis_sigma = (0.75, 0.75, 0.75, 0.75, 0.75, 0.75, 1.5, 1.5, 1.5, 1.5, 3.0, 3.0, 3.0)
column_power = (0, 1, 0, 2, 1, 0, 0, 1, 0, 1, 0, 1, 0)
row_power = (0, 0, 1, 0, 1, 2, 0, 0, 1, 1, 0, 0, 1)


def with_halo(array, sides, width):
    for axis, dim in sides:
        devices, length = (lax.axis_size(axis), array.shape[dim])
        up = [(i, (i + 1) % devices) for i in range(devices - 1)]
        down = [(j, i) for i, j in up]
        last = lax.slice_in_dim(array, length - width, length, axis=dim)
        leading = lax.slice_in_dim(array, 0, width, axis=dim)
        before = lax.ppermute(last, axis, up)
        after = lax.ppermute(leading, axis, down)
        array = jnp.concatenate([before, array, after], axis=dim)
    return array


def basis_taps(powers, sigmas=basis_sigma):
    offsets = jnp.arange(KW).astype(jnp.float32) - HALF_K
    sigma_col = jnp.array(sigmas, dtype=jnp.float32)[:, None]
    power_col = jnp.array(powers, dtype=jnp.int32)[:, None]
    spread = offsets[None, :]
    envelope = jnp.exp(-(spread * spread) / (2.0 * sigma_col * sigma_col))
    factor = jnp.where(power_col == 0, 1.0, jnp.where(power_col == 1, spread, spread * spread))
    shaped = envelope * factor
    scale = jnp.sqrt(jnp.sum(shaped * shaped, axis=1, keepdims=True))
    return (shaped / scale).astype(jnp.bfloat16)


def coefficients(terms, row_coord, col_coord):
    return (
        terms[0]
        + terms[1] * row_coord
        + terms[2] * col_coord
        + terms[3] * row_coord * row_coord
        + terms[4] * row_coord * col_coord
        + terms[5] * col_coord * col_coord
    )


def band_matrix(tap_table, inner_len):
    lead_idx = jnp.arange(inner_len + 2 * HALF_K)[:, None]
    trail_idx = jnp.arange(inner_len)[None, :]
    offset = lead_idx - trail_idx
    onehot = (offset[None] == jnp.arange(KW)[:, None, None]).astype(tap_table.dtype)
    band = jnp.einsum("kt,tai->kai", tap_table, onehot, preferred_element_type=jnp.float32)
    return band.astype(tap_table.dtype)


def shards(raw_counts, overscan, response, warp_rows, kernel_poly, tile_owner, tile_weight):
    band_count = lax.axis_size("ccd")
    halves = lax.axis_size("section")
    total_rows = ROWS * band_count
    total_cols = CH * halves
    top_row = lax.axis_index("ccd") * ROWS
    left_col = lax.axis_index("section") * CH
    half = lax.axis_index("section")
    strips = CH // STRIP
    wide_cols = strips * STRIP + STRIP
    rh = raw_counts.shape[2]
    calibrated = ((raw_counts - overscan[..., None]) * response).astype(jnp.bfloat16)[0, 0]
    shifts = (warp_rows - (top_row + jnp.arange(ROWS))).astype(jnp.bfloat16)
    my_shifts = lax.dynamic_slice_in_dim(shifts, half * rh, rh)[:, None]
    wide = jnp.pad(calibrated, ((0, 0), (HALF_K, HALF_K)))
    width = CH + 2 * HALF_K
    filler = jnp.zeros((rh, wide_cols - width - 1), jnp.bfloat16)

    def slab(col_start):
        cols = lax.dynamic_slice_in_dim(wide, col_start, width, 1)
        return jnp.concatenate([cols, my_shifts, filler], axis=1)

    own = slab(half * CH)
    other = slab((1 - half) * CH)
    nb = band_count
    axes = ("section", "ccd")
    swap = [(s * nb + b, (1 - s) * nb + b) for s in range(2) for b in range(nb)]
    got_swap = lax.ppermute(other, axes, swap)
    pick = lambda a, b: jnp.where(half == 0, a, b)
    first_rows = pick(own, got_swap)
    second_rows = pick(got_swap, own)
    rim = HALF_K
    sent_up = jnp.concatenate([first_rows, second_rows[:rim]], axis=0)
    sent_down = jnp.concatenate([first_rows[rh - rim :], second_rows], axis=0)
    upward = [(b, b - 1) for b in range(1, nb)]
    downward = [(b, b + 1) for b in range(nb - 1)]
    mixed = [(x, y) for x, y in upward] + [(nb + x, nb + y) for x, y in downward]
    mirrored = [(x, y) for x, y in downward] + [(nb + x, nb + y) for x, y in upward]
    got_mixed = lax.ppermute(pick(sent_up, sent_down), axes, mixed)
    got_mirrored = lax.ppermute(pick(sent_down, sent_up), axes, mirrored)
    from_below = pick(got_mixed, got_mirrored)
    from_above = pick(got_mirrored, got_mixed)
    lead = ROWS + 2 * HALF_K
    lead_pad = -(-lead // 16) * 16
    above = rh + rim
    steps = jnp.concatenate(
        [
            from_above[above - HALF_K :, width],
            first_rows[:, width],
            second_rows[:, width],
            from_below[:HALF_K, width],
        ]
    ).astype(jnp.int32)
    origin = rim + REACH
    out_rows = top_row - HALF_K + jnp.arange(lead)
    inside = (out_rows >= 0) & (out_rows < total_rows)
    picks = jnp.where(inside, jnp.arange(lead) + origin - HALF_K + steps, -1)
    picks = jnp.pad(picks, (0, lead_pad - lead), constant_values=-1)[None, :]
    pieces = (got_mirrored, own, got_swap, got_mixed)
    bases = ((0, above + 2 * rh), (above, above + rh), (above + rh, above), (above + 2 * rh, 0))
    span = 2 * STRIP
    both_taps = basis_taps(column_power + row_power, basis_sigma + basis_sigma)
    taps = jnp.pad(both_taps.astype(jnp.float32), ((0, 0), (0, span - KW)))
    params = jnp.concatenate(
        [kernel_poly.reshape(-1), jnp.stack([top_row, left_col]).astype(jnp.float32)]
    )
    at = NBASIS * NPOLY
    owners = tile_owner.reshape(1, -1)
    weights = tile_weight.reshape(1, -1)
    groups = TILE * TILE // STRIP
    tiles = owners.shape[1]
    row_tiles = ROWS // TILE
    per_lane = STRIP // TILE

    def match_kernel(kp_ref, picks_ref, p0_ref, p1_ref, p2_ref, p3_ref,
                     tap_ref, own_ref, w_ref,
                     out_ref, acc_ref, pack_ref, a_ref, b_ref, colm_ref, rowm_ref, img_ref):
        i = pl.program_id(0)

        @pl.when(i == 0)
        def _():
            first = kp_ref[at + 1] == 0.0
            gathered = jnp.zeros((lead_pad, wide_cols), jnp.float32)
            piece_refs = (p0_ref, p1_ref, p2_ref, p3_ref)
            for ref, (b0, b1) in zip(piece_refs, bases):
                n = ref.shape[0]
                base = jnp.where(first, b0, b1)
                hit = lax.broadcasted_iota(jnp.int32, (n, lead_pad), 0) + base == picks_ref[...]
                gathered = gathered + lax.dot_general(
                    hit.astype(jnp.bfloat16), ref[...], (((0,), (0,)), ((), ())),
                    preferred_element_type=jnp.float32,
                )
            img_ref[...] = gathered.astype(jnp.bfloat16)
            for k in range(NBASIS):
                spread = jnp.broadcast_to(tap_ref[pl.ds(k, 1), :], (STRIP, span))
                band_t = pltpu.roll(spread, 0, 1, stride=1, stride_axis=0)
                colm_ref[:, k * STRIP : (k + 1) * STRIP] = band_t.T.astype(jnp.bfloat16)
                spread = jnp.broadcast_to(tap_ref[pl.ds(NBASIS + k, 1), :], (ROWS, span))
                band = pltpu.roll(spread, 0, 1, stride=1, stride_axis=0)
                rowm_ref[k] = band.astype(jnp.bfloat16)
            rows = lax.broadcasted_iota(jnp.int32, (ROWS, STRIP), 0).astype(jnp.float32)
            u = 2.0 * (rows + kp_ref[at] + 0.5) / total_rows - 1.0
            for k in range(NBASIS):
                p = lambda m: kp_ref[k * NPOLY + m]
                a_ref[k] = p(0) + p(1) * u + p(3) * u * u
                b_ref[k] = p(2) + p(4) * u

        offset = pl.multiple_of(i * STRIP, STRIP)
        strip = img_ref[:, pl.ds(offset, span)]
        across = jnp.dot(strip, colm_ref[...], preferred_element_type=jnp.float32)
        across = across.astype(jnp.bfloat16)
        cols = lax.broadcasted_iota(jnp.int32, (1, STRIP), 1) + i * STRIP
        v = 2.0 * (cols.astype(jnp.float32) + kp_ref[at + 1] + 0.5) / total_cols - 1.0
        acc = jnp.zeros((ROWS, STRIP), jnp.float32)
        for k in range(NBASIS):
            vert = jnp.dot(
                rowm_ref[k, :, pl.ds(0, lead_pad)], across[:, k * STRIP : (k + 1) * STRIP],
                preferred_element_type=jnp.float32,
            )
            coef = a_ref[k] + v * (b_ref[k] + kp_ref[k * NPOLY + 5] * v)
            acc = acc + coef * vert
        acc_ref[...] = acc
        lane_group = lax.broadcasted_iota(jnp.int32, (groups, STRIP), 1) // TILE
        for rb in range(row_tiles):
            picked = [
                acc_ref[pl.ds(rb * TILE + g, groups, stride=per_lane), :] for g in range(per_lane)
            ]
            for cbl in range(per_lane):
                packed = jnp.zeros((groups, STRIP), jnp.float32)
                for g in range(per_lane):
                    shift = ((g - cbl) % per_lane) * TILE
                    rolled = pltpu.roll(picked[g], shift, 1) if shift else picked[g]
                    packed = jnp.where(lane_group == g, rolled, packed)
                j = (i * per_lane + cbl) * row_tiles + rb
                pack_ref[pl.ds(pl.multiple_of(j * groups, groups), groups), :] = packed

        @pl.when(i == strips - 1)
        def _():
            owner_ids = lax.broadcasted_iota(jnp.int32, (band_count, tiles), 0)
            sel = jnp.where(owner_ids == own_ref[...], w_ref[...], 0.0)
            for q in range(groups):
                part = pack_ref[pl.ds(q, tiles, stride=groups), :]
                out_ref[:, q, :] = jnp.dot(
                    sel, part, precision=lax.Precision.HIGHEST,
                    preferred_element_type=jnp.float32,
                ).astype(out_ref.dtype)

    full = lambda shape: pl.BlockSpec(shape, lambda i: (0,) * len(shape))
    outgoing = pl.pallas_call(
        match_kernel,
        grid=(strips,),
        in_specs=[pl.BlockSpec(memory_space=pltpu.SMEM), full(picks.shape)]
        + [full(x.shape) for x in pieces]
        + [full(taps.shape), full(owners.shape), full(weights.shape)],
        out_specs=full((band_count, groups, STRIP)),
        out_shape=jax.ShapeDtypeStruct((band_count, groups, STRIP), jnp.bfloat16),
        scratch_shapes=[
            pltpu.VMEM((ROWS, STRIP), jnp.float32),
            pltpu.VMEM((tiles * groups, STRIP), jnp.float32),
            pltpu.VMEM((NBASIS, ROWS, STRIP), jnp.float32),
            pltpu.VMEM((NBASIS, ROWS, STRIP), jnp.float32),
            pltpu.VMEM((span, NBASIS * STRIP), jnp.bfloat16),
            pltpu.VMEM((NBASIS, ROWS, span), jnp.bfloat16),
            pltpu.VMEM((lead_pad, wide_cols), jnp.bfloat16),
        ],
    )(params, picks, *pieces, taps, owners, weights)
    incoming = lax.all_to_all(outgoing, "ccd", split_axis=0, concat_axis=0, tiled=True)
    patch_sum = jnp.sum(incoming.astype(jnp.float32), axis=0, keepdims=True)
    return patch_sum.reshape(1, 1, TILE, TILE)


def solution(mesh):
    in_specs = (
        P("ccd", "section", None, None),
        P("ccd", "section", None),
        P("ccd", "section", None, None),
        P("ccd"),
        P(),
        P("ccd", "section", None, None),
        P("ccd", "section", None),
    )
    out_specs = P("section", "ccd", None, None)
    return jax.shard_map(shards, mesh=mesh, in_specs=in_specs, out_specs=out_specs, check_vma=False)
```

```python
import jax
import jax.numpy as jnp
from jax import lax
from jax.sharding import PartitionSpec as P
from jax.experimental import pallas as pl
from jax.experimental.pallas import tpu as pltpu

ROWS = 128
TILE = 32
STRIP = 128
KW = 21
NBASIS = 13
NPOLY = 6
HALF_K = 10
CH = 1024
REACH = 64


basis_sigma = (0.75, 0.75, 0.75, 0.75, 0.75, 0.75, 1.5, 1.5, 1.5, 1.5, 3.0, 3.0, 3.0)
column_power = (0, 1, 0, 2, 1, 0, 0, 1, 0, 1, 0, 1, 0)
row_power = (0, 0, 1, 0, 1, 2, 0, 0, 1, 1, 0, 0, 1)


def with_halo(array, sides, width):
    for axis, dim in sides:
        devices, length = (lax.axis_size(axis), array.shape[dim])
        up = [(i, (i + 1) % devices) for i in range(devices - 1)]
        down = [(j, i) for i, j in up]
        last = lax.slice_in_dim(array, length - width, length, axis=dim)
        leading = lax.slice_in_dim(array, 0, width, axis=dim)
        before = lax.ppermute(last, axis, up)
        after = lax.ppermute(leading, axis, down)
        array = jnp.concatenate([before, array, after], axis=dim)
    return array


def basis_taps(powers, sigmas=basis_sigma):
    offsets = jnp.arange(KW).astype(jnp.float32) - HALF_K
    sigma_col = jnp.array(sigmas, dtype=jnp.float32)[:, None]
    power_col = jnp.array(powers, dtype=jnp.int32)[:, None]
    spread = offsets[None, :]
    envelope = jnp.exp(-(spread * spread) / (2.0 * sigma_col * sigma_col))
    factor = jnp.where(power_col == 0, 1.0, jnp.where(power_col == 1, spread, spread * spread))
    shaped = envelope * factor
    scale = jnp.sqrt(jnp.sum(shaped * shaped, axis=1, keepdims=True))
    return (shaped / scale).astype(jnp.bfloat16)


def coefficients(terms, row_coord, col_coord):
    return (
        terms[0]
        + terms[1] * row_coord
        + terms[2] * col_coord
        + terms[3] * row_coord * row_coord
        + terms[4] * row_coord * col_coord
        + terms[5] * col_coord * col_coord
    )


def band_matrix(tap_table, inner_len):
    lead_idx = jnp.arange(inner_len + 2 * HALF_K)[:, None]
    trail_idx = jnp.arange(inner_len)[None, :]
    offset = lead_idx - trail_idx
    onehot = (offset[None] == jnp.arange(KW)[:, None, None]).astype(tap_table.dtype)
    band = jnp.einsum("kt,tai->kai", tap_table, onehot, preferred_element_type=jnp.float32)
    return band.astype(tap_table.dtype)


def shards(raw_counts, overscan, response, warp_rows, kernel_poly, tile_owner, tile_weight):
    band_count = lax.axis_size("ccd")
    halves = lax.axis_size("section")
    total_rows = ROWS * band_count
    total_cols = CH * halves
    top_row = lax.axis_index("ccd") * ROWS
    left_col = lax.axis_index("section") * CH
    half = lax.axis_index("section")
    strips = CH // STRIP
    wide_cols = strips * STRIP + STRIP
    rh = raw_counts.shape[2]
    calibrated = ((raw_counts - overscan[..., None]) * response).astype(jnp.bfloat16)[0, 0]
    shifts = (warp_rows - (top_row + jnp.arange(ROWS))).astype(jnp.bfloat16)
    my_shifts = lax.dynamic_slice_in_dim(shifts, half * rh, rh)[:, None]
    wide = jnp.pad(calibrated, ((0, 0), (HALF_K, HALF_K)))
    width = CH + 2 * HALF_K
    filler = jnp.zeros((rh, wide_cols - width - 1), jnp.bfloat16)

    def slab(col_start):
        cols = lax.dynamic_slice_in_dim(wide, col_start, width, 1)
        return jnp.concatenate([cols, my_shifts, filler], axis=1)

    own = slab(half * CH)
    other = slab((1 - half) * CH)
    nb = band_count
    axes = ("section", "ccd")
    swap = [(s * nb + b, (1 - s) * nb + b) for s in range(2) for b in range(nb)]
    got_swap = lax.ppermute(other, axes, swap)
    pick = lambda a, b: jnp.where(half == 0, a, b)
    first_rows = pick(own, got_swap)
    second_rows = pick(got_swap, own)
    rim = HALF_K
    sent_up = jnp.concatenate([first_rows, second_rows[:rim]], axis=0)
    sent_down = jnp.concatenate([first_rows[rh - rim :], second_rows], axis=0)
    upward = [(b, b - 1) for b in range(1, nb)]
    downward = [(b, b + 1) for b in range(nb - 1)]
    mixed = [(x, y) for x, y in upward] + [(nb + x, nb + y) for x, y in downward]
    mirrored = [(x, y) for x, y in downward] + [(nb + x, nb + y) for x, y in upward]
    got_mixed = lax.ppermute(pick(sent_up, sent_down), axes, mixed)
    got_mirrored = lax.ppermute(pick(sent_down, sent_up), axes, mirrored)
    from_below = pick(got_mixed, got_mirrored)
    from_above = pick(got_mirrored, got_mixed)
    lead = ROWS + 2 * HALF_K
    lead_pad = -(-lead // 16) * 16
    above = rh + rim
    steps = jnp.concatenate(
        [
            from_above[above - HALF_K :, width],
            first_rows[:, width],
            second_rows[:, width],
            from_below[:HALF_K, width],
        ]
    ).astype(jnp.int32)
    origin = rim + REACH
    out_rows = top_row - HALF_K + jnp.arange(lead)
    inside = (out_rows >= 0) & (out_rows < total_rows)
    picks = jnp.where(inside, jnp.arange(lead) + origin - HALF_K + steps, -1)
    picks = jnp.pad(picks, (0, lead_pad - lead), constant_values=-1)[None, :]
    pieces = (got_mirrored, own, got_swap, got_mixed)
    bases = ((0, above + 2 * rh), (above, above + rh), (above + rh, above), (above + 2 * rh, 0))
    span = 2 * STRIP
    both_taps = basis_taps(column_power + row_power, basis_sigma + basis_sigma)
    taps = jnp.pad(both_taps.astype(jnp.float32), ((0, 0), (0, span - KW)))
    params = jnp.concatenate(
        [kernel_poly.reshape(-1), jnp.stack([top_row, left_col]).astype(jnp.float32)]
    )
    at = NBASIS * NPOLY
    owners = tile_owner.reshape(1, -1)
    weights = tile_weight.reshape(1, -1)
    groups = TILE * TILE // STRIP
    tiles = owners.shape[1]
    row_tiles = ROWS // TILE
    per_lane = STRIP // TILE

    def match_kernel(kp_ref, picks_ref, p0_ref, p1_ref, p2_ref, p3_ref,
                     tap_ref, own_ref, w_ref,
                     out_ref, acc_ref, pack_ref, a_ref, b_ref, colm_ref, rowm_ref, img_ref):
        i = pl.program_id(0)

        @pl.when(i == 0)
        def _():
            first = kp_ref[at + 1] == 0.0
            gathered = jnp.zeros((lead_pad, wide_cols), jnp.float32)
            piece_refs = (p0_ref, p1_ref, p2_ref, p3_ref)
            for ref, (b0, b1) in zip(piece_refs, bases):
                n = ref.shape[0]
                base = jnp.where(first, b0, b1)
                hit = lax.broadcasted_iota(jnp.int32, (n, lead_pad), 0) + base == picks_ref[...]
                gathered = gathered + lax.dot_general(
                    hit.astype(jnp.bfloat16), ref[...], (((0,), (0,)), ((), ())),
                    preferred_element_type=jnp.float32,
                )
            img_ref[...] = gathered.astype(jnp.bfloat16)
            for k in range(NBASIS):
                spread = jnp.broadcast_to(tap_ref[pl.ds(k, 1), :], (STRIP, span))
                band_t = pltpu.roll(spread, 0, 1, stride=1, stride_axis=0)
                colm_ref[:, k * STRIP : (k + 1) * STRIP] = band_t.T.astype(jnp.bfloat16)
                spread = jnp.broadcast_to(tap_ref[pl.ds(NBASIS + k, 1), :], (ROWS, span))
                band = pltpu.roll(spread, 0, 1, stride=1, stride_axis=0)
                rowm_ref[k] = band.astype(jnp.bfloat16)
            rows = lax.broadcasted_iota(jnp.int32, (ROWS, STRIP), 0).astype(jnp.float32)
            u = 2.0 * (rows + kp_ref[at] + 0.5) / total_rows - 1.0
            for k in range(NBASIS):
                p = lambda m: kp_ref[k * NPOLY + m]
                a_ref[k] = p(0) + p(1) * u + p(3) * u * u
                b_ref[k] = p(2) + p(4) * u

        offset = pl.multiple_of(i * STRIP, STRIP)
        strip = img_ref[:, pl.ds(offset, span)]
        across = jnp.dot(strip, colm_ref[...], preferred_element_type=jnp.float32)
        across = across.astype(jnp.bfloat16)
        cols = lax.broadcasted_iota(jnp.int32, (1, STRIP), 1) + i * STRIP
        v = 2.0 * (cols.astype(jnp.float32) + kp_ref[at + 1] + 0.5) / total_cols - 1.0
        acc = jnp.zeros((ROWS, STRIP), jnp.float32)
        for k in range(NBASIS):
            vert = jnp.dot(
                rowm_ref[k, :, pl.ds(0, lead_pad)], across[:, k * STRIP : (k + 1) * STRIP],
                preferred_element_type=jnp.float32,
            )
            coef = a_ref[k] + v * (b_ref[k] + kp_ref[k * NPOLY + 5] * v)
            acc = acc + coef * vert
        acc_ref[...] = acc
        lane_group = lax.broadcasted_iota(jnp.int32, (groups, STRIP), 1) // TILE
        for rb in range(row_tiles):
            picked = [
                acc_ref[pl.ds(rb * TILE + g, groups, stride=per_lane), :] for g in range(per_lane)
            ]
            for cbl in range(per_lane):
                packed = jnp.zeros((groups, STRIP), jnp.float32)
                for g in range(per_lane):
                    shift = ((g - cbl) % per_lane) * TILE
                    rolled = pltpu.roll(picked[g], shift, 1) if shift else picked[g]
                    packed = jnp.where(lane_group == g, rolled, packed)
                j = (i * per_lane + cbl) * row_tiles + rb
                pack_ref[pl.ds(pl.multiple_of(j * groups, groups), groups), :] = packed

        @pl.when(i == strips - 1)
        def _():
            owner_ids = lax.broadcasted_iota(jnp.int32, (band_count, tiles), 0)
            sel = jnp.where(owner_ids == own_ref[...], w_ref[...], 0.0)
            for q in range(groups):
                part = pack_ref[pl.ds(q, tiles, stride=groups), :]
                out_ref[:, q, :] = jnp.dot(
                    sel, part, precision=lax.Precision.HIGH,
                    preferred_element_type=jnp.float32,
                ).astype(out_ref.dtype)

    full = lambda shape: pl.BlockSpec(shape, lambda i: (0,) * len(shape))
    outgoing = pl.pallas_call(
        match_kernel,
        grid=(strips,),
        in_specs=[pl.BlockSpec(memory_space=pltpu.SMEM), full(picks.shape)]
        + [full(x.shape) for x in pieces]
        + [full(taps.shape), full(owners.shape), full(weights.shape)],
        out_specs=full((band_count, groups, STRIP)),
        out_shape=jax.ShapeDtypeStruct((band_count, groups, STRIP), jnp.bfloat16),
        scratch_shapes=[
            pltpu.VMEM((ROWS, STRIP), jnp.float32),
            pltpu.VMEM((tiles * groups, STRIP), jnp.float32),
            pltpu.VMEM((NBASIS, ROWS, STRIP), jnp.float32),
            pltpu.VMEM((NBASIS, ROWS, STRIP), jnp.float32),
            pltpu.VMEM((span, NBASIS * STRIP), jnp.bfloat16),
            pltpu.VMEM((NBASIS, ROWS, span), jnp.bfloat16),
            pltpu.VMEM((lead_pad, wide_cols), jnp.bfloat16),
        ],
    )(params, picks, *pieces, taps, owners, weights)
    incoming = lax.all_to_all(outgoing, "ccd", split_axis=0, concat_axis=0, tiled=True)
    patch_sum = jnp.sum(incoming.astype(jnp.float32), axis=0, keepdims=True)
    return patch_sum.reshape(1, 1, TILE, TILE)


def solution(mesh):
    in_specs = (
        P("ccd", "section", None, None),
        P("ccd", "section", None),
        P("ccd", "section", None, None),
        P("ccd"),
        P(),
        P("ccd", "section", None, None),
        P("ccd", "section", None),
    )
    out_specs = P("section", "ccd", None, None)
    return jax.shard_map(shards, mesh=mesh, in_specs=in_specs, out_specs=out_specs, check_vma=False)
```
